32 devices in a mesh: groups: 2 (over y), seq: 4 (over z), queue: 4 (over x, core).
Axes of the slice: x: 2, y: 2, z: 4, core: 2. Of those that a mesh axis runs over, the one named last changes fastest.
Arguments:
- query_rows: bfloat16 [8, 512, 4096], P(('groups', 'queue'), 'seq'), parts along dimension 0, may hold values from -8 to 8
- key_rows: bfloat16 [8, 512, 4096], P(('groups', 'queue'), 'seq'), parts along dimension 0, may hold values from -8 to 8
- value_rows: bfloat16 [8, 512, 4096], P(('groups', 'queue'), 'seq'), parts along dimension 0, may hold values from -6 to 6
- hidden_state: bfloat16 [8, 512, 5120], P(('groups', 'queue'), 'seq'), parts along dimension 0, may hold values from -6 to 6
- modulation: float32 [8, 2, 5120], P(('groups', 'queue')), parts along dimension 0, may hold values from -4 to 4
- head_weight: bfloat16 [5120, 64], replicated, may hold values from -0.078125 to 0.078125
- latents: float32 [8, 512, 64], P(('groups', 'queue'), 'seq'), parts along dimension 0, may hold values from -6 to 6
- time_index: int32 [8], P(('groups', 'queue')), parts along dimension 0, may hold values from 1 to 8, as said below
- live_counts: int32 [32, 4], replicated, may hold values from 1 to 4, as said below
- block_lists: int32 [32, 4, 4], replicated, may hold values from 0 to 3, as said below
Outputs:
- attention_out: bfloat16 [8, 512, 4096], P(('groups', 'queue'), 'seq'), parts along dimension 0
- queue_next: float32 [8, 512, 64], P(('groups', 'queue'), 'seq'), parts along dimension 0
The draws below stay inside these ranges and needn't reach their ends.
There are 2 independent parts, one for each index of `groups`. The reference program is written for one: setup_inputs(seed, part) draws one part's arguments, and reference() takes and returns one part's arrays. A program takes and returns all parts, laid end to end along the dimension named above; an argument that names none is the same for every part. Nothing has to cross between parts.
Inputs may be any that keep to these rules, and one draw needn't show every extreme that they name: live_counts[h, b] leading entries of block_lists[h, b] are attended; 4 is reached in every draw. `block_lists`: for each head and query block the 4 entries are distinct block numbers, the first being the query block itself. `time_index`: strictly rising along the queue; the first position is at 1 and the last at 8.
All inputs are finite; a program needn't handle non-finite values.
Results may differ from the reference program's by a relative error of at most 0.0055.
Values may be sent and summed in bfloat16 or wider, within the bound.
No kernel may reach another device: no remote copies, remote signals or barrier semaphores. Data moves between devices by JAX's collectives and lax.ppermute only.
A program may use at most 64 MiB of HBM per device.

```python
import jax
import jax.numpy as jnp
from jax import lax

D = 5120
HEADS = 32
HDIM = 128
LATENT = 64
BLK = 128
STEPS = 8
TOKENS = 512
QBLOCKS = 4
KMAX = 4
QUEUE = 4


def paired_fields(key):
    shape = (QUEUE, TOKENS, HEADS * HDIM)
    query_field = jnp.clip(jax.random.normal(jax.random.fold_in(key, 11), shape, jnp.float32), -6.0, 6.0)
    key_field = jnp.clip(jax.random.normal(jax.random.fold_in(key, 12), shape, jnp.float32), -6.0, 6.0)
    return (query_field, key_field)


def draw_query_rows(key, part):
    return paired_fields(key)[0].astype(jnp.bfloat16)


def draw_key_rows(key, part):
    return paired_fields(key)[1].astype(jnp.bfloat16)


def draw_time_index(key, part):
    middle = jnp.sort(jax.random.permutation(key, STEPS - 2)[:QUEUE - 2]) + 2
    values = jnp.concatenate([jnp.array([1], jnp.int32), middle.astype(jnp.int32), jnp.array([STEPS], jnp.int32)])
    return values.astype(jnp.int32)


def draw_live_counts(key, part):
    lowest = max(KMAX // 4, 1)
    upper = max(KMAX // 2, lowest)
    heavy = jax.random.randint(jax.random.fold_in(key, 1), (HEADS, 1), 0, 4) == 0
    lighter = jax.random.randint(jax.random.fold_in(key, 2), (HEADS, 1), lowest, upper + 1)
    level = jnp.where(heavy, KMAX, lighter)
    jitter = jax.random.randint(jax.random.fold_in(key, 3), (HEADS, QBLOCKS), -1, 2)
    live = jnp.clip(level + jitter, 1, KMAX)
    chosen_head = jax.random.randint(jax.random.fold_in(key, 4), (), 0, HEADS)
    marked = (jnp.arange(HEADS)[:, None] == chosen_head) & (jnp.arange(QBLOCKS)[None, :] == 0)
    return jnp.where(marked, KMAX, live).astype(jnp.int32)


def draw_block_lists(key, part):
    noise = jax.random.randint(key, (HEADS, QBLOCKS, QBLOCKS), 0, 1 << 20)
    column = jnp.arange(QBLOCKS, dtype=jnp.int32)
    scores = noise * QBLOCKS + column[None, None, :]
    itself = column[None, :, None] == column[None, None, :]
    scores = jnp.where(itself, -1, scores)
    ranked = jnp.argsort(scores, axis=2)
    return ranked[:, :, :KMAX].astype(jnp.int32)


def steps_of(stream_key, shape, shards, least, top_value):
    loudness = 1.0
    for dim, blocks in shards:
        draws = jax.random.uniform(jax.random.fold_in(jax.random.fold_in(stream_key, 6), dim), (blocks,), jnp.float32, least / len(shards), top_value / len(shards))
        loudness = loudness * jnp.repeat(jnp.exp(draws), shape[dim] // blocks).reshape((-1,) + (1,) * (len(shape) - 1 - dim))
    return loudness


def gaussian(own_key, shape, scale, most, cuts=(), held_as=jnp.bfloat16):
    values = scale * jax.random.normal(own_key, shape, jnp.float32)
    if cuts:
        values = values * steps_of(own_key, shape, cuts, -0.22, 0.18)
    return jnp.clip(values, -most, most).astype(held_as)


def setup_inputs(seed: int = 0, part: int = 0) -> dict:
    key_list = jax.random.split(jax.random.key(seed), 11)
    own_keys = jax.random.split(jax.random.fold_in(key_list[10], part), 11)
    query_rows = draw_query_rows(jax.random.fold_in(jax.random.fold_in(key_list[10], part), 71), part)
    key_rows = draw_key_rows(jax.random.fold_in(jax.random.fold_in(key_list[10], part), 71), part)
    value_rows = gaussian(own_keys[2], (QUEUE, TOKENS, HEADS * HDIM), 1.0, 6.0, ((0, 4), (1, 4)))
    hidden_state = gaussian(own_keys[3], (QUEUE, TOKENS, D), 1.0, 6.0, ((0, 4), (1, 4)))
    modulation = gaussian(own_keys[4], (QUEUE, 2, D), 1.0, 4.0, ((0, 4),), jnp.float32)
    head_weight = gaussian(key_list[5], (D, LATENT), D ** -0.5, 0.078125)
    latents = gaussian(own_keys[6], (QUEUE, TOKENS, LATENT), 1.0, 6.0, ((0, 4), (1, 4)), jnp.float32)
    time_index = draw_time_index(jax.random.fold_in(jax.random.fold_in(key_list[10], part), 71), part)
    live_counts = draw_live_counts(jax.random.fold_in(key_list[10], 71), part)
    block_lists = draw_block_lists(jax.random.fold_in(key_list[10], 71), part)
    return dict(query_rows=query_rows, key_rows=key_rows, value_rows=value_rows, hidden_state=hidden_state, modulation=modulation, head_weight=head_weight, latents=latents, time_index=time_index, live_counts=live_counts, block_lists=block_lists)


epsilon = 1e-06
plan_shift = 5.0

def noise_level(step_value):
    fraction = step_value.astype(jnp.float32) / STEPS
    return plan_shift * fraction / (1.0 + (plan_shift - 1.0) * fraction)

def head_attention(query_head, key_head, value_head, live, blocks):
    query_blocks = query_head.astype(jnp.float32).reshape(QBLOCKS, BLK, HDIM)
    key_blocks = key_head.astype(jnp.float32).reshape(QBLOCKS, BLK, HDIM)
    value_blocks = value_head.astype(jnp.float32).reshape(QBLOCKS, BLK, HDIM)
    key_chosen = key_blocks[blocks]
    value_chosen = value_blocks[blocks]
    scores = jnp.einsum('qid,qkjd->qikj', query_blocks, key_chosen) * HDIM ** (-0.5)
    active = (jnp.arange(KMAX, dtype=jnp.int32)[None, :] < live[:, None])[:, None, :, None]
    scores = jnp.where(active, scores, -jnp.inf)
    highest = lax.optimization_barrier(jnp.max(scores, axis=(2, 3), keepdims=True))
    weights = jnp.exp(scores - highest)
    totals = lax.optimization_barrier(jnp.sum(weights, axis=(2, 3)))
    rounded = lax.optimization_barrier(weights.astype(jnp.bfloat16)).astype(jnp.float32)
    mixed = jnp.einsum('qikj,qkjd->qid', rounded, value_chosen)
    return (mixed / totals[:, :, None]).astype(jnp.bfloat16).reshape(TOKENS, HDIM)

def reference(query_rows, key_rows, value_rows, hidden_state, modulation, head_weight, latents, time_index, live_counts, block_lists):
    attended_all = []
    moved_all = []
    for position in range(QUEUE):
        query_here = query_rows[position]
        key_here = key_rows[position]
        value_here = value_rows[position]

        def per_head(head_number):
            column = (head_number * HDIM).astype(jnp.int32)
            query_head = lax.dynamic_slice_in_dim(query_here, column, HDIM, 1)
            key_head = lax.dynamic_slice_in_dim(key_here, column, HDIM, 1)
            value_head = lax.dynamic_slice_in_dim(value_here, column, HDIM, 1)
            return head_attention(query_head, key_head, value_head, live_counts[head_number], block_lists[head_number])
        stacked = lax.map(per_head, jnp.arange(HEADS, dtype=jnp.int32))
        attended_all.append(jnp.transpose(stacked, (1, 0, 2)).reshape(TOKENS, HEADS * HDIM))
        source = hidden_state[position].astype(jnp.float32)
        mean_row = lax.optimization_barrier(jnp.mean(source, axis=1, keepdims=True))
        centred = source - mean_row
        spread = lax.optimization_barrier(jnp.mean(centred * centred, axis=1, keepdims=True))
        normed = centred * lax.rsqrt(spread + epsilon)
        shaped = (normed * (1.0 + modulation[position, 1]) + modulation[position, 0]).astype(jnp.bfloat16)
        velocity = jnp.dot(shaped, head_weight, preferred_element_type=jnp.float32)
        change = noise_level(time_index[position] - 1) - noise_level(time_index[position])
        moved_all.append(latents[position] + change * velocity)
    return (jnp.stack(attended_all), jnp.roll(jnp.stack(moved_all), -1, axis=0))
```

```python
import functools

import jax
import jax.numpy as jnp
from jax import lax
from jax.experimental import pallas as pl
from jax.experimental.pallas import tpu as pltpu
from jax.sharding import PartitionSpec as P

STEPS = 8
CHUNKS = 2


epsilon = 1e-06
plan_shift = 5.0


def passed_along(value, axis, steps):
    count = lax.axis_size(axis)
    pairs = [(source, (source + steps) % count) for source in range(count)]
    return lax.ppermute(value, axis, pairs)


def noise_level(step_value):
    fraction = step_value.astype(jnp.float32) / STEPS
    return plan_shift * fraction / (1.0 + (plan_shift - 1.0) * fraction)


def attend_kernel(lists_ref, live_ref, q_ref, k_ref, v_ref, o_ref, *, block, slots, qblocks):
    head = pl.program_id(0)
    qblock = pl.program_id(1)
    total = k_ref.shape[0]
    scale = q_ref.shape[1] ** (-0.5)
    scores = (
        lax.dot_general(
            q_ref[...],
            k_ref[...],
            (((1,), (1,)), ((), ())),
            preferred_element_type=jnp.float32,
        )
        * scale
    )
    column = lax.broadcasted_iota(jnp.int32, (1, total), 1)
    live = live_ref[head * qblocks + qblock]
    active = column < 0
    for slot in range(slots):
        chosen = lists_ref[(head * qblocks + qblock) * slots + slot]
        low = chosen * block
        hit = (column >= low) & (column < low + block) & (slot < live)
        active = active | hit
    scores = jnp.where(active, scores, -jnp.inf)
    highest = jnp.max(scores, axis=1, keepdims=True)
    weights = jnp.exp(scores - highest)
    totals = jnp.sum(weights, axis=1, keepdims=True)
    mixed = jnp.dot(
        weights.astype(jnp.bfloat16), v_ref[...], preferred_element_type=jnp.float32
    )
    o_ref[...] = (mixed / totals).astype(o_ref.dtype)


def attend_heads(query_cols, key_cols, value_cols, lists, live):
    total, width = query_cols.shape
    head_total, qblocks = live.shape
    slots = lists.shape[2]
    depth = width // head_total
    block = total // qblocks
    kernel = functools.partial(attend_kernel, block=block, slots=slots, qblocks=qblocks)
    grid_spec = pltpu.PrefetchScalarGridSpec(
        num_scalar_prefetch=2,
        grid=(head_total, qblocks),
        in_specs=[
            pl.BlockSpec((block, depth), lambda h, b, *_: (b, h)),
            pl.BlockSpec((total, depth), lambda h, b, *_: (0, h)),
            pl.BlockSpec((total, depth), lambda h, b, *_: (0, h)),
        ],
        out_specs=pl.BlockSpec((block, depth), lambda h, b, *_: (b, h)),
    )
    return pl.pallas_call(
        kernel,
        grid_spec=grid_spec,
        out_shape=jax.ShapeDtypeStruct((total, width), jnp.bfloat16),
    )(lists.reshape(-1), live.reshape(-1), query_cols, key_cols, value_cols)


def local(
    query_rows,
    key_rows,
    value_rows,
    hidden_state,
    modulation,
    head_weight,
    latents,
    time_index,
    live_counts,
    block_lists,
):
    seq_count = lax.axis_size("seq")
    own_index = lax.axis_index("seq")
    head_count = live_counts.shape[0]
    per_device = head_count // seq_count
    chunks = CHUNKS if per_device % CHUNKS == 0 else 1
    per_chunk = per_device // chunks
    tokens = query_rows.shape[1]
    width = query_rows.shape[2]
    depth = width // head_count
    chunk_width = per_chunk * depth

    def split(rows):
        return rows[0].reshape(tokens, seq_count, chunks, chunk_width)

    query_split, key_split, value_split = split(query_rows), split(key_rows), split(value_rows)

    def gathered(parts, c):
        send = jnp.transpose(parts[:, :, c, :], (1, 0, 2))
        recv = lax.all_to_all(send, "seq", 0, 0, tiled=True)
        return recv.reshape(seq_count * tokens, chunk_width)

    backs = []
    for c in range(chunks):
        query_cols = gathered(query_split, c)
        key_cols = gathered(key_split, c)
        value_cols = gathered(value_split, c)
        first = own_index * per_device + c * per_chunk
        lists = lax.dynamic_slice_in_dim(block_lists, first, per_chunk, 0)
        live = lax.dynamic_slice_in_dim(live_counts, first, per_chunk, 0)
        attended = attend_heads(query_cols, key_cols, value_cols, lists, live)
        back = lax.all_to_all(
            attended.reshape(seq_count, tokens, chunk_width), "seq", 0, 0, tiled=True
        )
        backs.append(back)
    stacked = jnp.stack(backs)
    mixed_back = jnp.transpose(stacked, (2, 1, 0, 3)).reshape(1, tokens, width)

    source = hidden_state[0].astype(jnp.float32)
    mean_row = jnp.mean(source, axis=1, keepdims=True)
    centred = source - mean_row
    spread = jnp.mean(centred * centred, axis=1, keepdims=True)
    normed = centred * lax.rsqrt(spread + epsilon)
    shaped = (normed * (1.0 + modulation[0, 1]) + modulation[0, 0]).astype(jnp.bfloat16)
    velocity = jnp.dot(shaped, head_weight, preferred_element_type=jnp.float32)
    change = noise_level(time_index[0] - 1) - noise_level(time_index[0])
    moved = latents[0] + change * velocity
    queue_next = passed_along(moved[None], "queue", -1)
    return (mixed_back, queue_next)


def solution(mesh):
    placed = (
        P(("groups", "queue"), "seq", None),
        P(("groups", "queue"), "seq", None),
        P(("groups", "queue"), "seq", None),
        P(("groups", "queue"), "seq", None),
        P(("groups", "queue"), None, None),
        P(),
        P(("groups", "queue"), "seq", None),
        P(("groups", "queue")),
        P(),
        P(),
    )
    return jax.shard_map(
        local,
        mesh=mesh,
        in_specs=placed,
        out_specs=(P(("groups", "queue"), "seq", None), P(("groups", "queue"), "seq", None)),
        check_vma=False,
    )
```

```python
import functools

import jax
import jax.numpy as jnp
from jax import lax
from jax.experimental import pallas as pl
from jax.experimental.pallas import tpu as pltpu
from jax.sharding import PartitionSpec as P

STEPS = 8
CHUNKS = 2


epsilon = 1e-06
plan_shift = 5.0


def passed_along(value, axis, steps):
    count = lax.axis_size(axis)
    pairs = [(source, (source + steps) % count) for source in range(count)]
    return lax.ppermute(value, axis, pairs)


def noise_level(step_value):
    fraction = step_value.astype(jnp.float32) / STEPS
    return plan_shift * fraction / (1.0 + (plan_shift - 1.0) * fraction)


def attend_kernel(lists_ref, live_ref, x_ref, o_ref, *, block, slots, qblocks, heads, depth):
    sources, _, tokens, _ = x_ref.shape
    total = sources * tokens
    scale = depth ** (-0.5)
    column = lax.broadcasted_iota(jnp.int32, (1, total), 1)
    per_source = tokens // block
    for head in range(heads):
        cols = slice(head * depth, (head + 1) * depth)
        keys = x_ref[:, 1, :, cols].reshape(total, depth)
        values = x_ref[:, 2, :, cols].reshape(total, depth)

        def body(qblock, carry):
            source = qblock // per_source
            first = pl.multiple_of((qblock % per_source) * block, block)
            query = x_ref[source, 0, pl.ds(first, block), cols]
            scores = (
                lax.dot_general(
                    query, keys, (((1,), (1,)), ((), ())), preferred_element_type=jnp.float32
                )
                * scale
            )
            live = live_ref[head * qblocks + qblock]
            active = column < 0
            for slot in range(slots):
                low = lists_ref[(head * qblocks + qblock) * slots + slot] * block
                active = active | ((column >= low) & (column < low + block) & (slot < live))
            scores = jnp.where(active, scores, -jnp.inf)
            highest = jnp.max(scores, axis=1, keepdims=True)
            weights = jnp.exp(scores - highest)
            totals = jnp.sum(weights, axis=1, keepdims=True)
            mixed = jnp.dot(
                weights.astype(jnp.bfloat16), values, preferred_element_type=jnp.float32
            )
            o_ref[source, pl.ds(first, block), cols] = (mixed / totals).astype(o_ref.dtype)
            return carry

        lax.fori_loop(0, qblocks, body, 0)


def attend_heads(packed, lists, live):
    sources, _, tokens, width = packed.shape
    head_total, qblocks = live.shape
    slots = lists.shape[2]
    depth = width // head_total
    block = sources * tokens // qblocks
    kernel = functools.partial(
        attend_kernel, block=block, slots=slots, qblocks=qblocks, heads=head_total, depth=depth
    )
    smem = pltpu.SMEM
    return pl.pallas_call(
        kernel,
        in_specs=[
            pl.BlockSpec(memory_space=smem),
            pl.BlockSpec(memory_space=smem),
            pl.BlockSpec(memory_space=pltpu.VMEM),
        ],
        out_specs=pl.BlockSpec(memory_space=pltpu.VMEM),
        out_shape=jax.ShapeDtypeStruct((sources, tokens, width), jnp.bfloat16),
    )(lists.reshape(-1), live.reshape(-1), packed)


def pack_kernel(query_hbm, key_hbm, value_hbm, out_hbm, sems, *, seq, stride, offset, width):
    copies = []
    for group in range(seq):
        for kind, source in enumerate((query_hbm, key_hbm, value_hbm)):
            copy = pltpu.make_async_copy(
                source.at[0, :, pl.ds(group * stride + offset, width)],
                out_hbm.at[group, kind],
                sems.at[group * 3 + kind],
            )
            copy.start()
            copies.append(copy)
    for copy in copies:
        copy.wait()


def packed_chunk(query_rows, key_rows, value_rows, seq, stride, offset, width):
    tokens = query_rows.shape[1]
    kernel = functools.partial(pack_kernel, seq=seq, stride=stride, offset=offset, width=width)
    return pl.pallas_call(
        kernel,
        in_specs=[pl.BlockSpec(memory_space=pl.ANY)] * 3,
        out_specs=pl.BlockSpec(memory_space=pl.ANY),
        out_shape=jax.ShapeDtypeStruct((seq, 3, tokens, width), query_rows.dtype),
        scratch_shapes=[pltpu.SemaphoreType.DMA((seq * 3,))],
    )(query_rows, key_rows, value_rows)


def unpack_kernel(*refs, seq, stride, width):
    chunks = len(refs) - 2
    out_hbm, sems = refs[chunks], refs[chunks + 1]
    copies = []
    for c in range(chunks):
        for group in range(seq):
            copy = pltpu.make_async_copy(
                refs[c].at[group],
                out_hbm.at[0, :, pl.ds(group * stride + c * width, width)],
                sems.at[c * seq + group],
            )
            copy.start()
            copies.append(copy)
    for copy in copies:
        copy.wait()


def unpacked(backs, seq, stride, width):
    tokens = backs[0].shape[1]
    kernel = functools.partial(unpack_kernel, seq=seq, stride=stride, width=width)
    return pl.pallas_call(
        kernel,
        in_specs=[pl.BlockSpec(memory_space=pl.ANY)] * len(backs),
        out_specs=pl.BlockSpec(memory_space=pl.ANY),
        out_shape=jax.ShapeDtypeStruct((1, tokens, seq * stride), backs[0].dtype),
        scratch_shapes=[pltpu.SemaphoreType.DMA((seq * len(backs),))],
    )(*backs)


def local(
    query_rows,
    key_rows,
    value_rows,
    hidden_state,
    modulation,
    head_weight,
    latents,
    time_index,
    live_counts,
    block_lists,
):
    seq_count = lax.axis_size("seq")
    own_index = lax.axis_index("seq")
    head_count = live_counts.shape[0]
    per_device = head_count // seq_count
    chunks = CHUNKS if per_device % CHUNKS == 0 else 1
    per_chunk = per_device // chunks
    tokens = query_rows.shape[1]
    width = query_rows.shape[2]
    depth = width // head_count
    chunk_width = per_chunk * depth

    backs = []
    for c in range(chunks):
        send = packed_chunk(
            query_rows, key_rows, value_rows, seq_count, per_device * depth, c * chunk_width, chunk_width
        )
        packed = lax.all_to_all(send, "seq", 0, 0, tiled=True)
        first = own_index * per_device + c * per_chunk
        lists = lax.dynamic_slice_in_dim(block_lists, first, per_chunk, 0)
        live = lax.dynamic_slice_in_dim(live_counts, first, per_chunk, 0)
        attended = attend_heads(packed, lists, live)
        back = lax.all_to_all(attended, "seq", 0, 0, tiled=True)
        backs.append(back)
    mixed_back = unpacked(backs, seq_count, per_device * depth, chunk_width)

    source = hidden_state[0].astype(jnp.float32)
    mean_row = jnp.mean(source, axis=1, keepdims=True)
    centred = source - mean_row
    spread = jnp.mean(centred * centred, axis=1, keepdims=True)
    normed = centred * lax.rsqrt(spread + epsilon)
    shaped = (normed * (1.0 + modulation[0, 1]) + modulation[0, 0]).astype(jnp.bfloat16)
    velocity = jnp.dot(shaped, head_weight, preferred_element_type=jnp.float32)
    change = noise_level(time_index[0] - 1) - noise_level(time_index[0])
    moved = latents[0] + change * velocity
    queue_next = passed_along(moved[None], "queue", -1)
    return (mixed_back, queue_next)


def solution(mesh):
    placed = (
        P(("groups", "queue"), "seq", None),
        P(("groups", "queue"), "seq", None),
        P(("groups", "queue"), "seq", None),
        P(("groups", "queue"), "seq", None),
        P(("groups", "queue"), None, None),
        P(),
        P(("groups", "queue"), "seq", None),
        P(("groups", "queue")),
        P(),
        P(),
    )
    return jax.shard_map(
        local,
        mesh=mesh,
        in_specs=placed,
        out_specs=(P(("groups", "queue"), "seq", None), P(("groups", "queue"), "seq", None)),
        check_vma=False,
    )
```

```python
import functools

import jax
import jax.numpy as jnp
from jax import lax
from jax.experimental import pallas as pl
from jax.experimental.pallas import tpu as pltpu
from jax.sharding import PartitionSpec as P

STEPS = 8
CHUNKS = 2


epsilon = 1e-06
plan_shift = 5.0


def passed_along(value, axis, steps):
    count = lax.axis_size(axis)
    pairs = [(source, (source + steps) % count) for source in range(count)]
    return lax.ppermute(value, axis, pairs)


def noise_level(step_value):
    fraction = step_value.astype(jnp.float32) / STEPS
    return plan_shift * fraction / (1.0 + (plan_shift - 1.0) * fraction)


def attend_kernel(lists_ref, live_ref, x_ref, o_ref, *, block, slots, qblocks, heads, depth):
    sources, _, tokens, _ = x_ref.shape
    total = sources * tokens
    scale = depth ** (-0.5)
    column = lax.broadcasted_iota(jnp.int32, (1, total), 1)
    per_source = tokens // block
    for head in range(heads):
        cols = slice(head * depth, (head + 1) * depth)
        keys = x_ref[:, 1, :, cols].reshape(total, depth)
        values = x_ref[:, 2, :, cols].reshape(total, depth)

        def body(qblock, carry):
            source = qblock // per_source
            first = pl.multiple_of((qblock % per_source) * block, block)
            query = x_ref[source, 0, pl.ds(first, block), cols]
            scores = (
                lax.dot_general(
                    query, keys, (((1,), (1,)), ((), ())), preferred_element_type=jnp.float32
                )
                * scale
            )
            live = live_ref[head * qblocks + qblock]
            active = column < 0
            for slot in range(slots):
                low = lists_ref[(head * qblocks + qblock) * slots + slot] * block
                active = active | ((column >= low) & (column < low + block) & (slot < live))
            scores = jnp.where(active, scores, -jnp.inf)
            highest = jnp.max(scores, axis=1, keepdims=True)
            weights = jnp.exp(scores - highest)
            totals = jnp.sum(weights, axis=1, keepdims=True)
            mixed = jnp.dot(
                weights.astype(jnp.bfloat16), values, preferred_element_type=jnp.float32
            )
            o_ref[source, pl.ds(first, block), cols] = (mixed / totals).astype(o_ref.dtype)
            return carry

        lax.fori_loop(0, qblocks, body, 0)


def attend_heads(packed, lists, live):
    sources, _, tokens, width = packed.shape
    head_total, qblocks = live.shape
    slots = lists.shape[2]
    depth = width // head_total
    block = sources * tokens // qblocks
    kernel = functools.partial(
        attend_kernel, block=block, slots=slots, qblocks=qblocks, heads=head_total, depth=depth
    )
    smem = pltpu.SMEM
    return pl.pallas_call(
        kernel,
        in_specs=[
            pl.BlockSpec(memory_space=smem),
            pl.BlockSpec(memory_space=smem),
            pl.BlockSpec(memory_space=pltpu.VMEM),
        ],
        out_specs=pl.BlockSpec(memory_space=pltpu.VMEM),
        out_shape=jax.ShapeDtypeStruct((sources, tokens, width), jnp.bfloat16),
    )(lists.reshape(-1), live.reshape(-1), packed)


def pack_kernel(query_ref, key_ref, value_ref, out_ref, *, seq, stride, offset, width):
    for group in range(seq):
        cols = slice(group * stride + offset, group * stride + offset + width)
        for kind, source in enumerate((query_ref, key_ref, value_ref)):
            out_ref[group, kind] = source[0, :, cols]


def packed_chunk(query_rows, key_rows, value_rows, seq, stride, offset, width):
    tokens = query_rows.shape[1]
    kernel = functools.partial(pack_kernel, seq=seq, stride=stride, offset=offset, width=width)
    return pl.pallas_call(
        kernel,
        in_specs=[pl.BlockSpec(memory_space=pltpu.VMEM)] * 3,
        out_specs=pl.BlockSpec(memory_space=pltpu.VMEM),
        out_shape=jax.ShapeDtypeStruct((seq, 3, tokens, width), query_rows.dtype),
    )(query_rows, key_rows, value_rows)


def unpack_kernel(*refs, seq, stride, width):
    chunks = len(refs) - 1
    out_ref = refs[chunks]
    for c in range(chunks):
        for group in range(seq):
            low = group * stride + c * width
            out_ref[0, :, low:low + width] = refs[c][group]


def unpacked(backs, seq, stride, width):
    tokens = backs[0].shape[1]
    kernel = functools.partial(unpack_kernel, seq=seq, stride=stride, width=width)
    return pl.pallas_call(
        kernel,
        in_specs=[pl.BlockSpec(memory_space=pltpu.VMEM)] * len(backs),
        out_specs=pl.BlockSpec(memory_space=pltpu.VMEM),
        out_shape=jax.ShapeDtypeStruct((1, tokens, seq * stride), backs[0].dtype),
    )(*backs)


def local(
    query_rows,
    key_rows,
    value_rows,
    hidden_state,
    modulation,
    head_weight,
    latents,
    time_index,
    live_counts,
    block_lists,
):
    seq_count = lax.axis_size("seq")
    own_index = lax.axis_index("seq")
    head_count = live_counts.shape[0]
    per_device = head_count // seq_count
    chunks = CHUNKS if per_device % CHUNKS == 0 else 1
    per_chunk = per_device // chunks
    tokens = query_rows.shape[1]
    width = query_rows.shape[2]
    depth = width // head_count
    chunk_width = per_chunk * depth

    backs = []
    for c in range(chunks):
        send = packed_chunk(
            query_rows, key_rows, value_rows, seq_count, per_device * depth, c * chunk_width, chunk_width
        )
        packed = lax.all_to_all(send, "seq", 0, 0, tiled=True)
        first = own_index * per_device + c * per_chunk
        lists = lax.dynamic_slice_in_dim(block_lists, first, per_chunk, 0)
        live = lax.dynamic_slice_in_dim(live_counts, first, per_chunk, 0)
        attended = attend_heads(packed, lists, live)
        back = lax.all_to_all(attended, "seq", 0, 0, tiled=True)
        backs.append(back)
    mixed_back = unpacked(backs, seq_count, per_device * depth, chunk_width)

    source = hidden_state[0].astype(jnp.float32)
    mean_row = jnp.mean(source, axis=1, keepdims=True)
    centred = source - mean_row
    spread = jnp.mean(centred * centred, axis=1, keepdims=True)
    normed = centred * lax.rsqrt(spread + epsilon)
    shaped = (normed * (1.0 + modulation[0, 1]) + modulation[0, 0]).astype(jnp.bfloat16)
    velocity = jnp.dot(shaped, head_weight, preferred_element_type=jnp.float32)
    change = noise_level(time_index[0] - 1) - noise_level(time_index[0])
    moved = latents[0] + change * velocity
    queue_next = passed_along(moved[None], "queue", -1)
    return (mixed_back, queue_next)


def solution(mesh):
    placed = (
        P(("groups", "queue"), "seq", None),
        P(("groups", "queue"), "seq", None),
        P(("groups", "queue"), "seq", None),
        P(("groups", "queue"), "seq", None),
        P(("groups", "queue"), None, None),
        P(),
        P(("groups", "queue"), "seq", None),
        P(("groups", "queue")),
        P(),
        P(),
    )
    return jax.shard_map(
        local,
        mesh=mesh,
        in_specs=placed,
        out_specs=(P(("groups", "queue"), "seq", None), P(("groups", "queue"), "seq", None)),
        check_vma=False,
    )
```

```python
import functools

import jax
import jax.numpy as jnp
from jax import lax
from jax.experimental import pallas as pl
from jax.experimental.pallas import tpu as pltpu
from jax.sharding import PartitionSpec as P

STEPS = 8
CHUNKS = 2


epsilon = 1e-06
plan_shift = 5.0


def passed_along(value, axis, steps):
    count = lax.axis_size(axis)
    pairs = [(source, (source + steps) % count) for source in range(count)]
    return lax.ppermute(value, axis, pairs)


def noise_level(step_value):
    fraction = step_value.astype(jnp.float32) / STEPS
    return plan_shift * fraction / (1.0 + (plan_shift - 1.0) * fraction)


def attend_kernel(
    lists_ref, live_ref, me_ref, x_ref, o_ref, *, block, slots, qblocks, heads, depth, shifted
):
    sources, _, tokens, _ = x_ref.shape
    me = me_ref[0]

    def slot_of(device):
        if shifted:
            return (me - device + sources) % sources
        return device

    total = sources * tokens
    scale = depth ** (-0.5)
    column = lax.broadcasted_iota(jnp.int32, (1, total), 1)
    per_source = tokens // block
    for head in range(heads):
        cols = slice(head * depth, (head + 1) * depth)
        keys = x_ref[:, 1, :, cols].reshape(total, depth)
        values = x_ref[:, 2, :, cols].reshape(total, depth)

        def body(qblock, carry):
            source = slot_of(qblock // per_source)
            first = pl.multiple_of((qblock % per_source) * block, block)
            query = x_ref[source, 0, pl.ds(first, block), cols]
            scores = (
                lax.dot_general(
                    query, keys, (((1,), (1,)), ((), ())), preferred_element_type=jnp.float32
                )
                * scale
            )
            live = live_ref[head * qblocks + qblock]
            active = column < 0
            for slot in range(slots):
                chosen = lists_ref[(head * qblocks + qblock) * slots + slot]
                place = slot_of(chosen // per_source)
                low = place * tokens + (chosen % per_source) * block
                active = active | ((column >= low) & (column < low + block) & (slot < live))
            scores = jnp.where(active, scores, -jnp.inf)
            highest = jnp.max(scores, axis=1, keepdims=True)
            weights = jnp.exp(scores - highest)
            totals = jnp.sum(weights, axis=1, keepdims=True)
            mixed = jnp.dot(
                weights.astype(jnp.bfloat16), values, preferred_element_type=jnp.float32
            )
            o_ref[source, pl.ds(first, block), cols] = (mixed / totals).astype(o_ref.dtype)
            return carry

        lax.fori_loop(0, qblocks, body, 0)


def attend_heads(packed, lists, live, me, shifted):
    sources, _, tokens, width = packed.shape
    head_total, qblocks = live.shape
    slots = lists.shape[2]
    depth = width // head_total
    block = sources * tokens // qblocks
    kernel = functools.partial(
        attend_kernel,
        block=block,
        slots=slots,
        qblocks=qblocks,
        heads=head_total,
        depth=depth,
        shifted=shifted,
    )
    smem = pltpu.SMEM
    return pl.pallas_call(
        kernel,
        in_specs=[
            pl.BlockSpec(memory_space=smem),
            pl.BlockSpec(memory_space=smem),
            pl.BlockSpec(memory_space=smem),
            pl.BlockSpec(memory_space=pltpu.VMEM),
        ],
        out_specs=pl.BlockSpec(memory_space=pltpu.VMEM),
        out_shape=jax.ShapeDtypeStruct((sources, tokens, width), jnp.bfloat16),
    )(lists.reshape(-1), live.reshape(-1), me.reshape(1), packed)


def pack_kernel(query_ref, key_ref, value_ref, out_ref, *, seq, stride, offset, width):
    for group in range(seq):
        cols = slice(group * stride + offset, group * stride + offset + width)
        for kind, source in enumerate((query_ref, key_ref, value_ref)):
            out_ref[group, kind] = source[0, :, cols]


def packed_chunk(query_rows, key_rows, value_rows, seq, stride, offset, width):
    tokens = query_rows.shape[1]
    kernel = functools.partial(pack_kernel, seq=seq, stride=stride, offset=offset, width=width)
    return pl.pallas_call(
        kernel,
        in_specs=[pl.BlockSpec(memory_space=pltpu.VMEM)] * 3,
        out_specs=pl.BlockSpec(memory_space=pltpu.VMEM),
        out_shape=jax.ShapeDtypeStruct((seq, 3, tokens, width), query_rows.dtype),
    )(query_rows, key_rows, value_rows)


def unpack_kernel(*refs, seq, stride, width):
    chunks = len(refs) - 1
    out_ref = refs[chunks]
    for c in range(chunks):
        for group in range(seq):
            low = group * stride + c * width
            out_ref[0, :, low:low + width] = refs[c][group]


def unpacked(backs, seq, stride, width):
    tokens = backs[0].shape[1]
    kernel = functools.partial(unpack_kernel, seq=seq, stride=stride, width=width)
    return pl.pallas_call(
        kernel,
        in_specs=[pl.BlockSpec(memory_space=pltpu.VMEM)] * len(backs),
        out_specs=pl.BlockSpec(memory_space=pltpu.VMEM),
        out_shape=jax.ShapeDtypeStruct((1, tokens, seq * stride), backs[0].dtype),
    )(*backs)


def local(
    query_rows,
    key_rows,
    value_rows,
    hidden_state,
    modulation,
    head_weight,
    latents,
    time_index,
    live_counts,
    block_lists,
):
    seq_count = lax.axis_size("seq")
    own_index = lax.axis_index("seq")
    head_count = live_counts.shape[0]
    per_device = head_count // seq_count
    chunks = CHUNKS if per_device % CHUNKS == 0 else 1
    per_chunk = per_device // chunks
    tokens = query_rows.shape[1]
    width = query_rows.shape[2]
    depth = width // head_count
    chunk_width = per_chunk * depth
    permuted = seq_count <= 8

    backs = []
    for c in range(chunks):
        send = packed_chunk(
            query_rows, key_rows, value_rows, seq_count, per_device * depth, c * chunk_width, chunk_width
        )
        if permuted:
            pieces = [lax.dynamic_index_in_dim(send, own_index, 0, keepdims=False)]
            for step in range(1, seq_count):
                target = (own_index + step) % seq_count
                piece = lax.dynamic_index_in_dim(send, target, 0, keepdims=False)
                pieces.append(passed_along(piece, "seq", step))
            packed = jnp.stack(pieces)
            place = own_index
        else:
            packed = lax.all_to_all(send, "seq", 0, 0, tiled=True)
            place = jnp.zeros((), jnp.int32)
        first = own_index * per_device + c * per_chunk
        lists = lax.dynamic_slice_in_dim(block_lists, first, per_chunk, 0)
        live = lax.dynamic_slice_in_dim(live_counts, first, per_chunk, 0)
        attended = attend_heads(packed, lists, live, place.astype(jnp.int32), permuted)
        if permuted:
            outs = [attended[0]]
            for step in range(1, seq_count):
                outs.append(passed_along(attended[step], "seq", -step))
            back = jnp.roll(jnp.stack(outs), own_index, axis=0)
        else:
            back = lax.all_to_all(attended, "seq", 0, 0, tiled=True)
        backs.append(back)
    mixed_back = unpacked(backs, seq_count, per_device * depth, chunk_width)

    source = hidden_state[0].astype(jnp.float32)
    mean_row = jnp.mean(source, axis=1, keepdims=True)
    centred = source - mean_row
    spread = jnp.mean(centred * centred, axis=1, keepdims=True)
    normed = centred * lax.rsqrt(spread + epsilon)
    shaped = (normed * (1.0 + modulation[0, 1]) + modulation[0, 0]).astype(jnp.bfloat16)
    velocity = jnp.dot(shaped, head_weight, preferred_element_type=jnp.float32)
    change = noise_level(time_index[0] - 1) - noise_level(time_index[0])
    moved = latents[0] + change * velocity
    queue_next = passed_along(moved[None], "queue", -1)
    return (mixed_back, queue_next)


def solution(mesh):
    placed = (
        P(("groups", "queue"), "seq", None),
        P(("groups", "queue"), "seq", None),
        P(("groups", "queue"), "seq", None),
        P(("groups", "queue"), "seq", None),
        P(("groups", "queue"), None, None),
        P(),
        P(("groups", "queue"), "seq", None),
        P(("groups", "queue")),
        P(),
        P(),
    )
    return jax.shard_map(
        local,
        mesh=mesh,
        in_specs=placed,
        out_specs=(P(("groups", "queue"), "seq", None), P(("groups", "queue"), "seq", None)),
        check_vma=False,
    )
```

```python
import functools

import jax
import jax.numpy as jnp
from jax import lax
from jax.experimental import pallas as pl
from jax.experimental.pallas import tpu as pltpu
from jax.sharding import PartitionSpec as P

STEPS = 8
CHUNKS = 4


epsilon = 1e-06
plan_shift = 5.0


def passed_along(value, axis, steps):
    count = lax.axis_size(axis)
    pairs = [(source, (source + steps) % count) for source in range(count)]
    return lax.ppermute(value, axis, pairs)


def noise_level(step_value):
    fraction = step_value.astype(jnp.float32) / STEPS
    return plan_shift * fraction / (1.0 + (plan_shift - 1.0) * fraction)


def attend_kernel(
    lists_ref, live_ref, me_ref, x_ref, o_ref, *, block, slots, qblocks, heads, depth, shifted
):
    sources, _, tokens, _ = x_ref.shape
    me = me_ref[0]

    def slot_of(device):
        if shifted:
            return (me - device + sources) % sources
        return device

    total = sources * tokens
    scale = depth ** (-0.5)
    column = lax.broadcasted_iota(jnp.int32, (1, total), 1)
    per_source = tokens // block
    for head in range(heads):
        cols = slice(head * depth, (head + 1) * depth)
        keys = x_ref[:, 1, :, cols].reshape(total, depth)
        values = x_ref[:, 2, :, cols].reshape(total, depth)

        def body(qblock, carry):
            source = slot_of(qblock // per_source)
            first = pl.multiple_of((qblock % per_source) * block, block)
            query = x_ref[source, 0, pl.ds(first, block), cols]
            scores = (
                lax.dot_general(
                    query, keys, (((1,), (1,)), ((), ())), preferred_element_type=jnp.float32
                )
                * scale
            )
            live = live_ref[head * qblocks + qblock]
            active = column < 0
            for slot in range(slots):
                chosen = lists_ref[(head * qblocks + qblock) * slots + slot]
                place = slot_of(chosen // per_source)
                low = place * tokens + (chosen % per_source) * block
                active = active | ((column >= low) & (column < low + block) & (slot < live))
            scores = jnp.where(active, scores, -jnp.inf)
            highest = jnp.max(scores, axis=1, keepdims=True)
            weights = jnp.exp(scores - highest)
            totals = jnp.sum(weights, axis=1, keepdims=True)
            mixed = jnp.dot(
                weights.astype(jnp.bfloat16), values, preferred_element_type=jnp.float32
            )
            o_ref[source, pl.ds(first, block), cols] = (mixed / totals).astype(o_ref.dtype)
            return carry

        lax.fori_loop(0, qblocks, body, 0)


def attend_heads(packed, lists, live, me, shifted):
    sources, _, tokens, width = packed.shape
    head_total, qblocks = live.shape
    slots = lists.shape[2]
    depth = width // head_total
    block = sources * tokens // qblocks
    kernel = functools.partial(
        attend_kernel,
        block=block,
        slots=slots,
        qblocks=qblocks,
        heads=head_total,
        depth=depth,
        shifted=shifted,
    )
    smem = pltpu.SMEM
    return pl.pallas_call(
        kernel,
        in_specs=[
            pl.BlockSpec(memory_space=smem),
            pl.BlockSpec(memory_space=smem),
            pl.BlockSpec(memory_space=smem),
            pl.BlockSpec(memory_space=pltpu.VMEM),
        ],
        out_specs=pl.BlockSpec(memory_space=pltpu.VMEM),
        out_shape=jax.ShapeDtypeStruct((sources, tokens, width), jnp.bfloat16),
    )(lists.reshape(-1), live.reshape(-1), me.reshape(1), packed)


def pack_kernel(query_ref, key_ref, value_ref, out_ref, *, seq, stride, offset, width):
    for group in range(seq):
        cols = slice(group * stride + offset, group * stride + offset + width)
        for kind, source in enumerate((query_ref, key_ref, value_ref)):
            out_ref[group, kind] = source[0, :, cols]


def packed_chunk(query_rows, key_rows, value_rows, seq, stride, offset, width):
    tokens = query_rows.shape[1]
    kernel = functools.partial(pack_kernel, seq=seq, stride=stride, offset=offset, width=width)
    return pl.pallas_call(
        kernel,
        in_specs=[pl.BlockSpec(memory_space=pltpu.VMEM)] * 3,
        out_specs=pl.BlockSpec(memory_space=pltpu.VMEM),
        out_shape=jax.ShapeDtypeStruct((seq, 3, tokens, width), query_rows.dtype),
    )(query_rows, key_rows, value_rows)


def unpack_kernel(*refs, seq, stride, width):
    chunks = len(refs) - 1
    out_ref = refs[chunks]
    for c in range(chunks):
        for group in range(seq):
            low = group * stride + c * width
            out_ref[0, :, low:low + width] = refs[c][group]


def unpacked(backs, seq, stride, width):
    tokens = backs[0].shape[1]
    kernel = functools.partial(unpack_kernel, seq=seq, stride=stride, width=width)
    return pl.pallas_call(
        kernel,
        in_specs=[pl.BlockSpec(memory_space=pltpu.VMEM)] * len(backs),
        out_specs=pl.BlockSpec(memory_space=pltpu.VMEM),
        out_shape=jax.ShapeDtypeStruct((1, tokens, seq * stride), backs[0].dtype),
    )(*backs)


def local(
    query_rows,
    key_rows,
    value_rows,
    hidden_state,
    modulation,
    head_weight,
    latents,
    time_index,
    live_counts,
    block_lists,
):
    seq_count = lax.axis_size("seq")
    own_index = lax.axis_index("seq")
    head_count = live_counts.shape[0]
    per_device = head_count // seq_count
    chunks = CHUNKS if per_device % CHUNKS == 0 else 1
    per_chunk = per_device // chunks
    tokens = query_rows.shape[1]
    width = query_rows.shape[2]
    depth = width // head_count
    chunk_width = per_chunk * depth
    permuted = seq_count <= 8

    backs = []
    for c in range(chunks):
        send = packed_chunk(
            query_rows, key_rows, value_rows, seq_count, per_device * depth, c * chunk_width, chunk_width
        )
        if permuted:
            pieces = [lax.dynamic_index_in_dim(send, own_index, 0, keepdims=False)]
            for step in range(1, seq_count):
                target = (own_index + step) % seq_count
                piece = lax.dynamic_index_in_dim(send, target, 0, keepdims=False)
                pieces.append(passed_along(piece, "seq", step))
            packed = jnp.stack(pieces)
            place = own_index
        else:
            packed = lax.all_to_all(send, "seq", 0, 0, tiled=True)
            place = jnp.zeros((), jnp.int32)
        first = own_index * per_device + c * per_chunk
        lists = lax.dynamic_slice_in_dim(block_lists, first, per_chunk, 0)
        live = lax.dynamic_slice_in_dim(live_counts, first, per_chunk, 0)
        attended = attend_heads(packed, lists, live, place.astype(jnp.int32), permuted)
        if permuted:
            outs = [attended[0]]
            for step in range(1, seq_count):
                outs.append(passed_along(attended[step], "seq", -step))
            back = jnp.roll(jnp.stack(outs), own_index, axis=0)
        else:
            back = lax.all_to_all(attended, "seq", 0, 0, tiled=True)
        backs.append(back)
    mixed_back = unpacked(backs, seq_count, per_device * depth, chunk_width)

    source = hidden_state[0].astype(jnp.float32)
    mean_row = jnp.mean(source, axis=1, keepdims=True)
    centred = source - mean_row
    spread = jnp.mean(centred * centred, axis=1, keepdims=True)
    normed = centred * lax.rsqrt(spread + epsilon)
    shaped = (normed * (1.0 + modulation[0, 1]) + modulation[0, 0]).astype(jnp.bfloat16)
    velocity = jnp.dot(shaped, head_weight, preferred_element_type=jnp.float32)
    change = noise_level(time_index[0] - 1) - noise_level(time_index[0])
    moved = latents[0] + change * velocity
    queue_next = passed_along(moved[None], "queue", -1)
    return (mixed_back, queue_next)


def solution(mesh):
    placed = (
        P(("groups", "queue"), "seq", None),
        P(("groups", "queue"), "seq", None),
        P(("groups", "queue"), "seq", None),
        P(("groups", "queue"), "seq", None),
        P(("groups", "queue"), None, None),
        P(),
        P(("groups", "queue"), "seq", None),
        P(("groups", "queue")),
        P(),
        P(),
    )
    return jax.shard_map(
        local,
        mesh=mesh,
        in_specs=placed,
        out_specs=(P(("groups", "queue"), "seq", None), P(("groups", "queue"), "seq", None)),
        check_vma=False,
    )
```

```python
import functools

import jax
import jax.numpy as jnp
from jax import lax
from jax.experimental import pallas as pl
from jax.experimental.pallas import tpu as pltpu
from jax.sharding import PartitionSpec as P

STEPS = 8
CHUNKS = 2


epsilon = 1e-06
plan_shift = 5.0


def passed_along(value, axis, steps):
    count = lax.axis_size(axis)
    pairs = [(source, (source + steps) % count) for source in range(count)]
    return lax.ppermute(value, axis, pairs)


def noise_level(step_value):
    fraction = step_value.astype(jnp.float32) / STEPS
    return plan_shift * fraction / (1.0 + (plan_shift - 1.0) * fraction)


def attend_kernel(
    lists_ref,
    live_ref,
    me_ref,
    x_ref,
    o_ref,
    scores_ref,
    highest_ref,
    totals_ref,
    mixed_ref,
    *,
    block,
    slots,
    qblocks,
    heads,
    depth,
    shifted,
):
    sources, _, tokens, _ = x_ref.shape
    me = me_ref[0]
    scale = depth ** (-0.5)
    per_source = tokens // block

    def slot_of(device):
        if shifted:
            return (me - device + sources) % sources
        return device

    for head in range(heads):
        cols = slice(head * depth, (head + 1) * depth)

        def body(qblock, carry):
            source = slot_of(qblock // per_source)
            first = pl.multiple_of((qblock % per_source) * block, block)
            query = x_ref[source, 0, pl.ds(first, block), cols]
            entry = head * qblocks + qblock
            live = live_ref[entry]

            def rows_of(slot):
                chosen = lists_ref[entry * slots + slot]
                low = pl.multiple_of((chosen % per_source) * block, block)
                return slot_of(chosen // per_source), low

            def score(slot):
                place, low = rows_of(slot)
                keys = x_ref[place, 1, pl.ds(low, block), cols]
                scores = (
                    lax.dot_general(
                        query, keys, (((1,), (1,)), ((), ())), preferred_element_type=jnp.float32
                    )
                    * scale
                )
                scores_ref[slot] = scores
                return jnp.max(scores, axis=1, keepdims=True)

            highest_ref[...] = score(0)
            for slot in range(1, slots):

                @pl.when(slot < live)
                def _():
                    highest_ref[...] = jnp.maximum(highest_ref[...], score(slot))

            def mix(slot):
                place, low = rows_of(slot)
                weights = jnp.exp(scores_ref[slot] - highest_ref[...])
                values = x_ref[place, 2, pl.ds(low, block), cols]
                mixed = jnp.dot(
                    weights.astype(jnp.bfloat16), values, preferred_element_type=jnp.float32
                )
                return jnp.sum(weights, axis=1, keepdims=True), mixed

            totals_ref[...], mixed_ref[...] = mix(0)
            for slot in range(1, slots):

                @pl.when(slot < live)
                def _():
                    totals, mixed = mix(slot)
                    totals_ref[...] += totals
                    mixed_ref[...] += mixed

            o_ref[source, pl.ds(first, block), cols] = (
                mixed_ref[...] / totals_ref[...]
            ).astype(o_ref.dtype)
            return carry

        lax.fori_loop(0, qblocks, body, 0)


def attend_heads(packed, lists, live, me, shifted):
    sources, _, tokens, width = packed.shape
    head_total, qblocks = live.shape
    slots = lists.shape[2]
    depth = width // head_total
    block = sources * tokens // qblocks
    kernel = functools.partial(
        attend_kernel,
        block=block,
        slots=slots,
        qblocks=qblocks,
        heads=head_total,
        depth=depth,
        shifted=shifted,
    )
    smem = pltpu.SMEM
    return pl.pallas_call(
        kernel,
        in_specs=[
            pl.BlockSpec(memory_space=smem),
            pl.BlockSpec(memory_space=smem),
            pl.BlockSpec(memory_space=smem),
            pl.BlockSpec(memory_space=pltpu.VMEM),
        ],
        out_specs=pl.BlockSpec(memory_space=pltpu.VMEM),
        out_shape=jax.ShapeDtypeStruct((sources, tokens, width), jnp.bfloat16),
        scratch_shapes=[
            pltpu.VMEM((slots, block, block), jnp.float32),
            pltpu.VMEM((block, 1), jnp.float32),
            pltpu.VMEM((block, 1), jnp.float32),
            pltpu.VMEM((block, depth), jnp.float32),
        ],
    )(lists.reshape(-1), live.reshape(-1), me.reshape(1), packed)


def pack_kernel(query_ref, key_ref, value_ref, out_ref, *, seq, stride, offset, width):
    for group in range(seq):
        cols = slice(group * stride + offset, group * stride + offset + width)
        for kind, source in enumerate((query_ref, key_ref, value_ref)):
            out_ref[group, kind] = source[0, :, cols]


def packed_chunk(query_rows, key_rows, value_rows, seq, stride, offset, width):
    tokens = query_rows.shape[1]
    kernel = functools.partial(pack_kernel, seq=seq, stride=stride, offset=offset, width=width)
    return pl.pallas_call(
        kernel,
        in_specs=[pl.BlockSpec(memory_space=pltpu.VMEM)] * 3,
        out_specs=pl.BlockSpec(memory_space=pltpu.VMEM),
        out_shape=jax.ShapeDtypeStruct((seq, 3, tokens, width), query_rows.dtype),
    )(query_rows, key_rows, value_rows)


def unpack_kernel(*refs, seq, stride, width):
    chunks = len(refs) - 1
    out_ref = refs[chunks]
    for c in range(chunks):
        for group in range(seq):
            low = group * stride + c * width
            out_ref[0, :, low:low + width] = refs[c][group]


def unpacked(backs, seq, stride, width):
    tokens = backs[0].shape[1]
    kernel = functools.partial(unpack_kernel, seq=seq, stride=stride, width=width)
    return pl.pallas_call(
        kernel,
        in_specs=[pl.BlockSpec(memory_space=pltpu.VMEM)] * len(backs),
        out_specs=pl.BlockSpec(memory_space=pltpu.VMEM),
        out_shape=jax.ShapeDtypeStruct((1, tokens, seq * stride), backs[0].dtype),
    )(*backs)


def local(
    query_rows,
    key_rows,
    value_rows,
    hidden_state,
    modulation,
    head_weight,
    latents,
    time_index,
    live_counts,
    block_lists,
):
    seq_count = lax.axis_size("seq")
    own_index = lax.axis_index("seq")
    head_count = live_counts.shape[0]
    per_device = head_count // seq_count
    chunks = CHUNKS if per_device % CHUNKS == 0 else 1
    per_chunk = per_device // chunks
    tokens = query_rows.shape[1]
    width = query_rows.shape[2]
    depth = width // head_count
    chunk_width = per_chunk * depth
    permuted = seq_count <= 8

    backs = []
    for c in range(chunks):
        send = packed_chunk(
            query_rows, key_rows, value_rows, seq_count, per_device * depth, c * chunk_width, chunk_width
        )
        if permuted:
            pieces = [lax.dynamic_index_in_dim(send, own_index, 0, keepdims=False)]
            for step in range(1, seq_count):
                target = (own_index + step) % seq_count
                piece = lax.dynamic_index_in_dim(send, target, 0, keepdims=False)
                pieces.append(passed_along(piece, "seq", step))
            packed = jnp.stack(pieces)
            place = own_index
        else:
            packed = lax.all_to_all(send, "seq", 0, 0, tiled=True)
            place = jnp.zeros((), jnp.int32)
        first = own_index * per_device + c * per_chunk
        lists = lax.dynamic_slice_in_dim(block_lists, first, per_chunk, 0)
        live = lax.dynamic_slice_in_dim(live_counts, first, per_chunk, 0)
        attended = attend_heads(packed, lists, live, place.astype(jnp.int32), permuted)
        if permuted:
            outs = [attended[0]]
            for step in range(1, seq_count):
                outs.append(passed_along(attended[step], "seq", -step))
            back = jnp.roll(jnp.stack(outs), own_index, axis=0)
        else:
            back = lax.all_to_all(attended, "seq", 0, 0, tiled=True)
        backs.append(back)
    mixed_back = unpacked(backs, seq_count, per_device * depth, chunk_width)

    source = hidden_state[0].astype(jnp.float32)
    mean_row = jnp.mean(source, axis=1, keepdims=True)
    centred = source - mean_row
    spread = jnp.mean(centred * centred, axis=1, keepdims=True)
    normed = centred * lax.rsqrt(spread + epsilon)
    shaped = (normed * (1.0 + modulation[0, 1]) + modulation[0, 0]).astype(jnp.bfloat16)
    velocity = jnp.dot(shaped, head_weight, preferred_element_type=jnp.float32)
    change = noise_level(time_index[0] - 1) - noise_level(time_index[0])
    moved = latents[0] + change * velocity
    queue_next = passed_along(moved[None], "queue", -1)
    return (mixed_back, queue_next)


def solution(mesh):
    placed = (
        P(("groups", "queue"), "seq", None),
        P(("groups", "queue"), "seq", None),
        P(("groups", "queue"), "seq", None),
        P(("groups", "queue"), "seq", None),
        P(("groups", "queue"), None, None),
        P(),
        P(("groups", "queue"), "seq", None),
        P(("groups", "queue")),
        P(),
        P(),
    )
    return jax.shard_map(
        local,
        mesh=mesh,
        in_specs=placed,
        out_specs=(P(("groups", "queue"), "seq", None), P(("groups", "queue"), "seq", None)),
        check_vma=False,
    )
```

```python
import functools

import jax
import jax.numpy as jnp
from jax import lax
from jax.experimental import pallas as pl
from jax.experimental.pallas import tpu as pltpu
from jax.sharding import PartitionSpec as P

STEPS = 8


epsilon = 1e-06
plan_shift = 5.0


def passed_along(value, axis, steps):
    count = lax.axis_size(axis)
    pairs = [(source, (source + steps) % count) for source in range(count)]
    return lax.ppermute(value, axis, pairs)


def noise_level(step_value):
    fraction = step_value.astype(jnp.float32) / STEPS
    return plan_shift * fraction / (1.0 + (plan_shift - 1.0) * fraction)


def attend_kernel(
    lists_ref, live_ref, me_ref, x_ref, o_ref, *, block, slots, qblocks, heads, depth, shifted
):
    sources, _, tokens, _ = x_ref.shape
    me = me_ref[0]

    def slot_of(device):
        if shifted:
            return (me - device + sources) % sources
        return device

    total = sources * tokens
    scale = depth ** (-0.5)
    column = lax.broadcasted_iota(jnp.int32, (1, total), 1)
    per_source = tokens // block
    for head in range(heads):
        cols = slice(head * depth, (head + 1) * depth)
        keys = x_ref[:, 1, :, cols].reshape(total, depth)
        values = x_ref[:, 2, :, cols].reshape(total, depth)

        def body(qblock, carry):
            source = slot_of(qblock // per_source)
            first = pl.multiple_of((qblock % per_source) * block, block)
            query = x_ref[source, 0, pl.ds(first, block), cols]
            scores = (
                lax.dot_general(
                    query, keys, (((1,), (1,)), ((), ())), preferred_element_type=jnp.float32
                )
                * scale
            )
            live = live_ref[head * qblocks + qblock]
            active = column < 0
            for slot in range(slots):
                chosen = lists_ref[(head * qblocks + qblock) * slots + slot]
                place = slot_of(chosen // per_source)
                low = place * tokens + (chosen % per_source) * block
                active = active | ((column >= low) & (column < low + block) & (slot < live))
            scores = jnp.where(active, scores, -jnp.inf)
            highest = jnp.max(scores, axis=1, keepdims=True)
            weights = jnp.exp(scores - highest)
            totals = jnp.sum(weights, axis=1, keepdims=True)
            mixed = jnp.dot(
                weights.astype(jnp.bfloat16), values, preferred_element_type=jnp.float32
            )
            o_ref[source, pl.ds(first, block), cols] = (mixed / totals).astype(o_ref.dtype)
            return carry

        lax.fori_loop(0, qblocks, body, 0)


def attend_heads(packed, lists, live, me, shifted):
    sources, _, tokens, width = packed.shape
    head_total, qblocks = live.shape
    slots = lists.shape[2]
    depth = width // head_total
    block = sources * tokens // qblocks
    kernel = functools.partial(
        attend_kernel,
        block=block,
        slots=slots,
        qblocks=qblocks,
        heads=head_total,
        depth=depth,
        shifted=shifted,
    )
    smem = pltpu.SMEM
    return pl.pallas_call(
        kernel,
        in_specs=[
            pl.BlockSpec(memory_space=smem),
            pl.BlockSpec(memory_space=smem),
            pl.BlockSpec(memory_space=smem),
            pl.BlockSpec(memory_space=pltpu.VMEM),
        ],
        out_specs=pl.BlockSpec(memory_space=pltpu.VMEM),
        out_shape=jax.ShapeDtypeStruct((sources, tokens, width), jnp.bfloat16),
    )(lists.reshape(-1), live.reshape(-1), me.reshape(1), packed)


def pack_kernel(query_ref, key_ref, value_ref, out_ref, *, seq, stride, offset, width):
    for group in range(seq):
        cols = slice(group * stride + offset, group * stride + offset + width)
        for kind, source in enumerate((query_ref, key_ref, value_ref)):
            out_ref[group, kind] = source[0, :, cols]


def packed_chunk(query_rows, key_rows, value_rows, seq, stride, offset, width):
    tokens = query_rows.shape[1]
    kernel = functools.partial(pack_kernel, seq=seq, stride=stride, offset=offset, width=width)
    return pl.pallas_call(
        kernel,
        in_specs=[pl.BlockSpec(memory_space=pltpu.VMEM)] * 3,
        out_specs=pl.BlockSpec(memory_space=pltpu.VMEM),
        out_shape=jax.ShapeDtypeStruct((seq, 3, tokens, width), query_rows.dtype),
    )(query_rows, key_rows, value_rows)


def unpack_kernel(*refs, seq, stride, offsets):
    chunks = len(refs) - 1
    out_ref = refs[chunks]
    for c in range(chunks):
        width = refs[c].shape[2]
        for group in range(seq):
            low = group * stride + offsets[c]
            out_ref[0, :, low:low + width] = refs[c][group]


def unpacked(backs, seq, stride, offsets):
    tokens = backs[0].shape[1]
    kernel = functools.partial(unpack_kernel, seq=seq, stride=stride, offsets=tuple(offsets))
    return pl.pallas_call(
        kernel,
        in_specs=[pl.BlockSpec(memory_space=pltpu.VMEM)] * len(backs),
        out_specs=pl.BlockSpec(memory_space=pltpu.VMEM),
        out_shape=jax.ShapeDtypeStruct((1, tokens, seq * stride), backs[0].dtype),
    )(*backs)


def local(
    query_rows,
    key_rows,
    value_rows,
    hidden_state,
    modulation,
    head_weight,
    latents,
    time_index,
    live_counts,
    block_lists,
):
    seq_count = lax.axis_size("seq")
    own_index = lax.axis_index("seq")
    head_count = live_counts.shape[0]
    per_device = head_count // seq_count
    if per_device % 4 == 0:
        sizes = [per_device * 3 // 4, per_device // 4]
    else:
        sizes = [per_device]
    starts = [sum(sizes[:c]) for c in range(len(sizes))]
    tokens = query_rows.shape[1]
    width = query_rows.shape[2]
    depth = width // head_count
    permuted = seq_count <= 8

    backs = []
    previous = None
    for per_chunk, start in zip(sizes, starts):
        chunk_width = per_chunk * depth
        send = packed_chunk(
            query_rows, key_rows, value_rows, seq_count, per_device * depth, start * depth, chunk_width
        )
        if previous is not None:
            send, _ = lax.optimization_barrier((send, previous))
        if permuted:
            pieces = [lax.dynamic_index_in_dim(send, own_index, 0, keepdims=False)]
            for step in range(1, seq_count):
                target = (own_index + step) % seq_count
                piece = lax.dynamic_index_in_dim(send, target, 0, keepdims=False)
                pieces.append(passed_along(piece, "seq", step))
            packed = jnp.stack(pieces)
            place = own_index
        else:
            packed = lax.all_to_all(send, "seq", 0, 0, tiled=True)
            place = jnp.zeros((), jnp.int32)
        first = own_index * per_device + start
        lists = lax.dynamic_slice_in_dim(block_lists, first, per_chunk, 0)
        live = lax.dynamic_slice_in_dim(live_counts, first, per_chunk, 0)
        previous = packed
        attended = attend_heads(packed, lists, live, place.astype(jnp.int32), permuted)
        if permuted:
            outs = [attended[0]]
            for step in range(1, seq_count):
                outs.append(passed_along(attended[step], "seq", -step))
            back = jnp.roll(jnp.stack(outs), own_index, axis=0)
        else:
            back = lax.all_to_all(attended, "seq", 0, 0, tiled=True)
        backs.append(back)
    mixed_back = unpacked(backs, seq_count, per_device * depth, [s * depth for s in starts])

    source = hidden_state[0].astype(jnp.float32)
    mean_row = jnp.mean(source, axis=1, keepdims=True)
    centred = source - mean_row
    spread = jnp.mean(centred * centred, axis=1, keepdims=True)
    normed = centred * lax.rsqrt(spread + epsilon)
    shaped = (normed * (1.0 + modulation[0, 1]) + modulation[0, 0]).astype(jnp.bfloat16)
    velocity = jnp.dot(shaped, head_weight, preferred_element_type=jnp.float32)
    change = noise_level(time_index[0] - 1) - noise_level(time_index[0])
    moved = latents[0] + change * velocity
    queue_next = passed_along(moved[None], "queue", -1)
    return (mixed_back, queue_next)


def solution(mesh):
    placed = (
        P(("groups", "queue"), "seq", None),
        P(("groups", "queue"), "seq", None),
        P(("groups", "queue"), "seq", None),
        P(("groups", "queue"), "seq", None),
        P(("groups", "queue"), None, None),
        P(),
        P(("groups", "queue"), "seq", None),
        P(("groups", "queue")),
        P(),
        P(),
    )
    return jax.shard_map(
        local,
        mesh=mesh,
        in_specs=placed,
        out_specs=(P(("groups", "queue"), "seq", None), P(("groups", "queue"), "seq", None)),
        check_vma=False,
    )
```

```python
import functools

import jax
import jax.numpy as jnp
from jax import lax
from jax.experimental import pallas as pl
from jax.experimental.pallas import tpu as pltpu
from jax.sharding import PartitionSpec as P

STEPS = 8


epsilon = 1e-06
plan_shift = 5.0


def passed_along(value, axis, steps):
    count = lax.axis_size(axis)
    pairs = [(source, (source + steps) % count) for source in range(count)]
    return lax.ppermute(value, axis, pairs)


def noise_level(step_value):
    fraction = step_value.astype(jnp.float32) / STEPS
    return plan_shift * fraction / (1.0 + (plan_shift - 1.0) * fraction)


def attend_kernel(
    lists_ref, live_ref, me_ref, x_ref, o_ref, *, block, slots, qblocks, heads, depth, shifted
):
    sources, _, tokens, _ = x_ref.shape
    me = me_ref[0]

    def slot_of(device):
        if shifted:
            return (me - device + sources) % sources
        return device

    total = sources * tokens
    scale = depth ** (-0.5)
    column = lax.broadcasted_iota(jnp.int32, (1, total), 1)
    per_source = tokens // block
    for head in range(heads):
        cols = slice(head * depth, (head + 1) * depth)
        keys = x_ref[:, 1, :, cols].reshape(total, depth)
        values = x_ref[:, 2, :, cols].reshape(total, depth)

        def body(qblock, carry):
            source = slot_of(qblock // per_source)
            first = pl.multiple_of((qblock % per_source) * block, block)
            query = x_ref[source, 0, pl.ds(first, block), cols]
            scores = (
                lax.dot_general(
                    query, keys, (((1,), (1,)), ((), ())), preferred_element_type=jnp.float32
                )
                * scale
            )
            live = live_ref[head * qblocks + qblock]
            active = column < 0
            for slot in range(slots):
                chosen = lists_ref[(head * qblocks + qblock) * slots + slot]
                place = slot_of(chosen // per_source)
                low = place * tokens + (chosen % per_source) * block
                active = active | ((column >= low) & (column < low + block) & (slot < live))
            scores = jnp.where(active, scores, -jnp.inf)
            highest = jnp.max(scores, axis=1, keepdims=True)
            weights = jnp.exp(scores - highest)
            totals = jnp.sum(weights, axis=1, keepdims=True)
            mixed = jnp.dot(
                weights.astype(jnp.bfloat16), values, preferred_element_type=jnp.float32
            )
            o_ref[source, pl.ds(first, block), cols] = (mixed / totals).astype(o_ref.dtype)
            return carry

        lax.fori_loop(0, qblocks, body, 0)


def attend_heads(packed, lists, live, me, shifted):
    sources, _, tokens, width = packed.shape
    head_total, qblocks = live.shape
    slots = lists.shape[2]
    depth = width // head_total
    block = sources * tokens // qblocks
    kernel = functools.partial(
        attend_kernel,
        block=block,
        slots=slots,
        qblocks=qblocks,
        heads=head_total,
        depth=depth,
        shifted=shifted,
    )
    smem = pltpu.SMEM
    return pl.pallas_call(
        kernel,
        in_specs=[
            pl.BlockSpec(memory_space=smem),
            pl.BlockSpec(memory_space=smem),
            pl.BlockSpec(memory_space=smem),
            pl.BlockSpec(memory_space=pltpu.VMEM),
        ],
        out_specs=pl.BlockSpec(memory_space=pltpu.VMEM),
        out_shape=jax.ShapeDtypeStruct((sources, tokens, width), jnp.bfloat16),
    )(lists.reshape(-1), live.reshape(-1), me.reshape(1), packed)


def pack_kernel(query_ref, key_ref, value_ref, out_ref, *, seq, stride, offset, width):
    for group in range(seq):
        cols = slice(group * stride + offset, group * stride + offset + width)
        for kind, source in enumerate((query_ref, key_ref, value_ref)):
            out_ref[group, kind] = source[0, :, cols]


def packed_chunk(query_rows, key_rows, value_rows, seq, stride, offset, width):
    tokens = query_rows.shape[1]
    kernel = functools.partial(pack_kernel, seq=seq, stride=stride, offset=offset, width=width)
    return pl.pallas_call(
        kernel,
        in_specs=[pl.BlockSpec(memory_space=pltpu.VMEM)] * 3,
        out_specs=pl.BlockSpec(memory_space=pltpu.VMEM),
        out_shape=jax.ShapeDtypeStruct((seq, 3, tokens, width), query_rows.dtype),
    )(query_rows, key_rows, value_rows)


def unpack_kernel(*refs, seq, stride, offsets):
    chunks = len(refs) - 1
    out_ref = refs[chunks]
    for c in range(chunks):
        width = refs[c].shape[2]
        for group in range(seq):
            low = group * stride + offsets[c]
            out_ref[0, :, low:low + width] = refs[c][group]


def unpacked(backs, seq, stride, offsets):
    tokens = backs[0].shape[1]
    kernel = functools.partial(unpack_kernel, seq=seq, stride=stride, offsets=tuple(offsets))
    return pl.pallas_call(
        kernel,
        in_specs=[pl.BlockSpec(memory_space=pltpu.VMEM)] * len(backs),
        out_specs=pl.BlockSpec(memory_space=pltpu.VMEM),
        out_shape=jax.ShapeDtypeStruct((1, tokens, seq * stride), backs[0].dtype),
    )(*backs)


def pieces_kernel(*refs, seq, stride, offset, width, me):
    sources, outs = refs[:3], refs[3:]
    for step in range(seq):
        low = ((me + step) % seq) * stride + offset
        for kind, source in enumerate(sources):
            outs[step][kind] = source[0, :, low:low + width]


def pieces_of(query_rows, key_rows, value_rows, own_index, seq, stride, offset, width):
    tokens = query_rows.shape[1]

    def branch(me, *rows):
        kernel = functools.partial(
            pieces_kernel, seq=seq, stride=stride, offset=offset, width=width, me=me
        )
        return tuple(
            pl.pallas_call(
                kernel,
                in_specs=[pl.BlockSpec(memory_space=pltpu.VMEM)] * 3,
                out_specs=[pl.BlockSpec(memory_space=pltpu.VMEM)] * seq,
                out_shape=[jax.ShapeDtypeStruct((3, tokens, width), query_rows.dtype)] * seq,
            )(*rows)
        )

    branches = [functools.partial(branch, me) for me in range(seq)]
    return lax.switch(own_index, branches, query_rows, key_rows, value_rows)


def attend_pieces_kernel(lists_ref, live_ref, me_ref, *refs, block, slots, qblocks, heads, depth):
    sources = len(refs) // 2
    x_refs, o_refs = refs[:sources], refs[sources:]
    tokens = x_refs[0].shape[1]
    total = sources * tokens
    me = me_ref[0]
    scale = depth ** (-0.5)
    per_source = tokens // block
    column = lax.broadcasted_iota(jnp.int32, (1, total), 1)
    for head in range(heads):
        cols = slice(head * depth, (head + 1) * depth)
        keys = jnp.concatenate([ref[1, :, cols] for ref in x_refs], axis=0)
        values = jnp.concatenate([ref[2, :, cols] for ref in x_refs], axis=0)
        for step in range(sources):
            device = (me - step + sources) % sources
            for sub in range(per_source):
                rows = slice(sub * block, (sub + 1) * block)
                query = x_refs[step][0, rows, cols]
                entry = head * qblocks + device * per_source + sub
                live = live_ref[entry]
                active = column < 0
                for slot in range(slots):
                    chosen = lists_ref[entry * slots + slot]
                    place = (me - chosen // per_source + sources) % sources
                    low = place * tokens + (chosen % per_source) * block
                    active = active | ((column >= low) & (column < low + block) & (slot < live))
                scores = (
                    lax.dot_general(
                        query, keys, (((1,), (1,)), ((), ())), preferred_element_type=jnp.float32
                    )
                    * scale
                )
                scores = jnp.where(active, scores, -jnp.inf)
                highest = jnp.max(scores, axis=1, keepdims=True)
                weights = jnp.exp(scores - highest)
                totals = jnp.sum(weights, axis=1, keepdims=True)
                mixed = jnp.dot(
                    weights.astype(jnp.bfloat16), values, preferred_element_type=jnp.float32
                )
                o_refs[step][rows, cols] = (mixed / totals).astype(o_refs[step].dtype)


def attend_pieces(pieces, lists, live, me):
    _, tokens, width = pieces[0].shape
    head_total, qblocks = live.shape
    slots = lists.shape[2]
    depth = width // head_total
    block = len(pieces) * tokens // qblocks
    kernel = functools.partial(
        attend_pieces_kernel,
        block=block,
        slots=slots,
        qblocks=qblocks,
        heads=head_total,
        depth=depth,
    )
    smem = pltpu.SMEM
    return pl.pallas_call(
        kernel,
        in_specs=[pl.BlockSpec(memory_space=smem)] * 3
        + [pl.BlockSpec(memory_space=pltpu.VMEM)] * len(pieces),
        out_specs=[pl.BlockSpec(memory_space=pltpu.VMEM)] * len(pieces),
        out_shape=[jax.ShapeDtypeStruct((tokens, width), jnp.bfloat16)] * len(pieces),
    )(lists.reshape(-1), live.reshape(-1), me.reshape(1), *pieces)


def place_kernel(*refs, seq, stride, offsets, me):
    out_ref = refs[-1]
    for c, offset in enumerate(offsets):
        for step in range(seq):
            piece = refs[c * seq + step]
            width = piece.shape[1]
            low = ((me + step) % seq) * stride + offset
            out_ref[0, :, low:low + width] = piece[...]


def placed_back(backs, own_index, seq, stride, offsets):
    tokens = backs[0].shape[0]

    def branch(me, *pieces):
        kernel = functools.partial(
            place_kernel, seq=seq, stride=stride, offsets=tuple(offsets), me=me
        )
        return pl.pallas_call(
            kernel,
            in_specs=[pl.BlockSpec(memory_space=pltpu.VMEM)] * len(pieces),
            out_specs=pl.BlockSpec(memory_space=pltpu.VMEM),
            out_shape=jax.ShapeDtypeStruct((1, tokens, seq * stride), pieces[0].dtype),
        )(*pieces)

    branches = [functools.partial(branch, me) for me in range(seq)]
    return lax.switch(own_index, branches, *backs)


def local(
    query_rows,
    key_rows,
    value_rows,
    hidden_state,
    modulation,
    head_weight,
    latents,
    time_index,
    live_counts,
    block_lists,
):
    seq_count = lax.axis_size("seq")
    own_index = lax.axis_index("seq")
    head_count = live_counts.shape[0]
    per_device = head_count // seq_count
    if per_device % 4 == 0:
        sizes = [per_device * 3 // 4, per_device // 4]
    else:
        sizes = [per_device]
    starts = [sum(sizes[:c]) for c in range(len(sizes))]
    tokens = query_rows.shape[1]
    width = query_rows.shape[2]
    depth = width // head_count
    permuted = seq_count <= 8

    backs = []
    previous = None
    for per_chunk, start in zip(sizes, starts):
        chunk_width = per_chunk * depth
        first = own_index * per_device + start
        lists = lax.dynamic_slice_in_dim(block_lists, first, per_chunk, 0)
        live = lax.dynamic_slice_in_dim(live_counts, first, per_chunk, 0)
        if permuted:
            pieces = pieces_of(
                query_rows,
                key_rows,
                value_rows,
                own_index,
                seq_count,
                per_device * depth,
                start * depth,
                chunk_width,
            )
            if previous is not None:
                pieces, _ = lax.optimization_barrier((pieces, previous))
            received = [pieces[0]]
            for step in range(1, seq_count):
                received.append(passed_along(pieces[step], "seq", step))
            previous = received
            outs = attend_pieces(received, lists, live, own_index.astype(jnp.int32))
            backs.append(outs[0])
            for step in range(1, seq_count):
                backs.append(passed_along(outs[step], "seq", -step))
            continue
        send = packed_chunk(
            query_rows, key_rows, value_rows, seq_count, per_device * depth, start * depth, chunk_width
        )
        if previous is not None:
            send, _ = lax.optimization_barrier((send, previous))
        packed = lax.all_to_all(send, "seq", 0, 0, tiled=True)
        previous = packed
        attended = attend_heads(packed, lists, live, jnp.zeros((), jnp.int32), False)
        backs.append(lax.all_to_all(attended, "seq", 0, 0, tiled=True))
    offsets = [s * depth for s in starts]
    if permuted:
        mixed_back = placed_back(backs, own_index, seq_count, per_device * depth, offsets)
    else:
        mixed_back = unpacked(backs, seq_count, per_device * depth, offsets)

    source = hidden_state[0].astype(jnp.float32)
    mean_row = jnp.mean(source, axis=1, keepdims=True)
    centred = source - mean_row
    spread = jnp.mean(centred * centred, axis=1, keepdims=True)
    normed = centred * lax.rsqrt(spread + epsilon)
    shaped = (normed * (1.0 + modulation[0, 1]) + modulation[0, 0]).astype(jnp.bfloat16)
    velocity = jnp.dot(shaped, head_weight, preferred_element_type=jnp.float32)
    change = noise_level(time_index[0] - 1) - noise_level(time_index[0])
    moved = latents[0] + change * velocity
    queue_next = passed_along(moved[None], "queue", -1)
    return (mixed_back, queue_next)


def solution(mesh):
    placed = (
        P(("groups", "queue"), "seq", None),
        P(("groups", "queue"), "seq", None),
        P(("groups", "queue"), "seq", None),
        P(("groups", "queue"), "seq", None),
        P(("groups", "queue"), None, None),
        P(),
        P(("groups", "queue"), "seq", None),
        P(("groups", "queue")),
        P(),
        P(),
    )
    return jax.shard_map(
        local,
        mesh=mesh,
        in_specs=placed,
        out_specs=(P(("groups", "queue"), "seq", None), P(("groups", "queue"), "seq", None)),
        check_vma=False,
    )
```

```python
import functools

import jax
import jax.numpy as jnp
from jax import lax
from jax.experimental import pallas as pl
from jax.experimental.pallas import tpu as pltpu
from jax.sharding import PartitionSpec as P

STEPS = 8


epsilon = 1e-06
plan_shift = 5.0


def passed_along(value, axis, steps):
    count = lax.axis_size(axis)
    pairs = [(source, (source + steps) % count) for source in range(count)]
    return lax.ppermute(value, axis, pairs)


def noise_level(step_value):
    fraction = step_value.astype(jnp.float32) / STEPS
    return plan_shift * fraction / (1.0 + (plan_shift - 1.0) * fraction)


def attend_kernel(
    lists_ref, live_ref, me_ref, x_ref, o_ref, *, block, slots, qblocks, heads, depth, shifted
):
    sources, _, tokens, _ = x_ref.shape
    me = me_ref[0]

    def slot_of(device):
        if shifted:
            return (me - device + sources) % sources
        return device

    total = sources * tokens
    scale = depth ** (-0.5)
    column = lax.broadcasted_iota(jnp.int32, (1, total), 1)
    per_source = tokens // block
    for head in range(heads):
        cols = slice(head * depth, (head + 1) * depth)
        keys = x_ref[:, 1, :, cols].reshape(total, depth)
        values = x_ref[:, 2, :, cols].reshape(total, depth)

        def body(qblock, carry):
            source = slot_of(qblock // per_source)
            first = pl.multiple_of((qblock % per_source) * block, block)
            query = x_ref[source, 0, pl.ds(first, block), cols]
            scores = (
                lax.dot_general(
                    query, keys, (((1,), (1,)), ((), ())), preferred_element_type=jnp.float32
                )
                * scale
            )
            live = live_ref[head * qblocks + qblock]
            active = column < 0
            for slot in range(slots):
                chosen = lists_ref[(head * qblocks + qblock) * slots + slot]
                place = slot_of(chosen // per_source)
                low = place * tokens + (chosen % per_source) * block
                active = active | ((column >= low) & (column < low + block) & (slot < live))
            scores = jnp.where(active, scores, -jnp.inf)
            highest = jnp.max(scores, axis=1, keepdims=True)
            weights = jnp.exp(scores - highest)
            totals = jnp.sum(weights, axis=1, keepdims=True)
            mixed = jnp.dot(
                weights.astype(jnp.bfloat16), values, preferred_element_type=jnp.float32
            )
            o_ref[source, pl.ds(first, block), cols] = (mixed / totals).astype(o_ref.dtype)
            return carry

        lax.fori_loop(0, qblocks, body, 0)


def attend_heads(packed, lists, live, me, shifted):
    sources, _, tokens, width = packed.shape
    head_total, qblocks = live.shape
    slots = lists.shape[2]
    depth = width // head_total
    block = sources * tokens // qblocks
    kernel = functools.partial(
        attend_kernel,
        block=block,
        slots=slots,
        qblocks=qblocks,
        heads=head_total,
        depth=depth,
        shifted=shifted,
    )
    smem = pltpu.SMEM
    return pl.pallas_call(
        kernel,
        in_specs=[
            pl.BlockSpec(memory_space=smem),
            pl.BlockSpec(memory_space=smem),
            pl.BlockSpec(memory_space=smem),
            pl.BlockSpec(memory_space=pltpu.VMEM),
        ],
        out_specs=pl.BlockSpec(memory_space=pltpu.VMEM),
        out_shape=jax.ShapeDtypeStruct((sources, tokens, width), jnp.bfloat16),
    )(lists.reshape(-1), live.reshape(-1), me.reshape(1), packed)


def pack_kernel(query_ref, key_ref, value_ref, out_ref, *, seq, stride, offset, width):
    for group in range(seq):
        cols = slice(group * stride + offset, group * stride + offset + width)
        for kind, source in enumerate((query_ref, key_ref, value_ref)):
            out_ref[group, kind] = source[0, :, cols]


def packed_chunk(query_rows, key_rows, value_rows, seq, stride, offset, width):
    tokens = query_rows.shape[1]
    kernel = functools.partial(pack_kernel, seq=seq, stride=stride, offset=offset, width=width)
    return pl.pallas_call(
        kernel,
        in_specs=[pl.BlockSpec(memory_space=pltpu.VMEM)] * 3,
        out_specs=pl.BlockSpec(memory_space=pltpu.VMEM),
        out_shape=jax.ShapeDtypeStruct((seq, 3, tokens, width), query_rows.dtype),
    )(query_rows, key_rows, value_rows)


def unpack_kernel(*refs, seq, stride, offsets):
    chunks = len(refs) - 1
    out_ref = refs[chunks]
    for c in range(chunks):
        width = refs[c].shape[2]
        for group in range(seq):
            low = group * stride + offsets[c]
            out_ref[0, :, low:low + width] = refs[c][group]


def unpacked(backs, seq, stride, offsets):
    tokens = backs[0].shape[1]
    kernel = functools.partial(unpack_kernel, seq=seq, stride=stride, offsets=tuple(offsets))
    return pl.pallas_call(
        kernel,
        in_specs=[pl.BlockSpec(memory_space=pltpu.VMEM)] * len(backs),
        out_specs=pl.BlockSpec(memory_space=pltpu.VMEM),
        out_shape=jax.ShapeDtypeStruct((1, tokens, seq * stride), backs[0].dtype),
    )(*backs)


def piece_kernel(query_ref, key_ref, value_ref, out_ref, *, low, width):
    for kind, source in enumerate((query_ref, key_ref, value_ref)):
        out_ref[kind] = source[0, :, low:low + width]


def pieces_of(query_rows, key_rows, value_rows, own_index, seq, stride, offset, width):
    tokens = query_rows.shape[1]

    def branch(me, step, *rows):
        low = ((me + step) % seq) * stride + offset
        return pl.pallas_call(
            functools.partial(piece_kernel, low=low, width=width),
            in_specs=[pl.BlockSpec(memory_space=pltpu.VMEM)] * 3,
            out_specs=pl.BlockSpec(memory_space=pltpu.VMEM),
            out_shape=jax.ShapeDtypeStruct((3, tokens, width), query_rows.dtype),
        )(*rows)

    pieces = []
    for step in range(seq):
        branches = [functools.partial(branch, me, step) for me in range(seq)]
        pieces.append(lax.switch(own_index, branches, query_rows, key_rows, value_rows))
    return tuple(pieces)


def attend_pieces_kernel(lists_ref, live_ref, me_ref, *refs, block, slots, qblocks, heads, depth):
    sources = len(refs) // 2
    x_refs, o_refs = refs[:sources], refs[sources:]
    tokens = x_refs[0].shape[1]
    total = sources * tokens
    me = me_ref[0]
    scale = depth ** (-0.5)
    per_source = tokens // block
    column = lax.broadcasted_iota(jnp.int32, (1, total), 1)
    for head in range(heads):
        cols = slice(head * depth, (head + 1) * depth)
        keys = jnp.concatenate([ref[1, :, cols] for ref in x_refs], axis=0)
        values = jnp.concatenate([ref[2, :, cols] for ref in x_refs], axis=0)
        for step in range(sources):
            device = (me - step + sources) % sources
            for sub in range(per_source):
                rows = slice(sub * block, (sub + 1) * block)
                query = x_refs[step][0, rows, cols]
                entry = head * qblocks + device * per_source + sub
                live = live_ref[entry]
                active = column < 0
                for slot in range(slots):
                    chosen = lists_ref[entry * slots + slot]
                    place = (me - chosen // per_source + sources) % sources
                    low = place * tokens + (chosen % per_source) * block
                    active = active | ((column >= low) & (column < low + block) & (slot < live))
                scores = (
                    lax.dot_general(
                        query, keys, (((1,), (1,)), ((), ())), preferred_element_type=jnp.float32
                    )
                    * scale
                )
                scores = jnp.where(active, scores, -jnp.inf)
                highest = jnp.max(scores, axis=1, keepdims=True)
                weights = jnp.exp(scores - highest)
                totals = jnp.sum(weights, axis=1, keepdims=True)
                mixed = jnp.dot(
                    weights.astype(jnp.bfloat16), values, preferred_element_type=jnp.float32
                )
                o_refs[step][rows, cols] = (mixed / totals).astype(o_refs[step].dtype)


def attend_pieces(pieces, lists, live, me):
    _, tokens, width = pieces[0].shape
    head_total, qblocks = live.shape
    slots = lists.shape[2]
    depth = width // head_total
    block = len(pieces) * tokens // qblocks
    kernel = functools.partial(
        attend_pieces_kernel,
        block=block,
        slots=slots,
        qblocks=qblocks,
        heads=head_total,
        depth=depth,
    )
    smem = pltpu.SMEM
    return pl.pallas_call(
        kernel,
        in_specs=[pl.BlockSpec(memory_space=smem)] * 3
        + [pl.BlockSpec(memory_space=pltpu.VMEM)] * len(pieces),
        out_specs=[pl.BlockSpec(memory_space=pltpu.VMEM)] * len(pieces),
        out_shape=[jax.ShapeDtypeStruct((tokens, width), jnp.bfloat16)] * len(pieces),
    )(lists.reshape(-1), live.reshape(-1), me.reshape(1), *pieces)


def place_kernel(*refs, seq, stride, offsets, me):
    out_ref = refs[-1]
    for c, offset in enumerate(offsets):
        for step in range(seq):
            piece = refs[c * seq + step]
            width = piece.shape[1]
            low = ((me + step) % seq) * stride + offset
            out_ref[0, :, low:low + width] = piece[...]


def placed_back(backs, own_index, seq, stride, offsets):
    tokens = backs[0].shape[0]

    def branch(me, *pieces):
        kernel = functools.partial(
            place_kernel, seq=seq, stride=stride, offsets=tuple(offsets), me=me
        )
        return pl.pallas_call(
            kernel,
            in_specs=[pl.BlockSpec(memory_space=pltpu.VMEM)] * len(pieces),
            out_specs=pl.BlockSpec(memory_space=pltpu.VMEM),
            out_shape=jax.ShapeDtypeStruct((1, tokens, seq * stride), pieces[0].dtype),
        )(*pieces)

    branches = [functools.partial(branch, me) for me in range(seq)]
    return lax.switch(own_index, branches, *backs)


def local(
    query_rows,
    key_rows,
    value_rows,
    hidden_state,
    modulation,
    head_weight,
    latents,
    time_index,
    live_counts,
    block_lists,
):
    seq_count = lax.axis_size("seq")
    own_index = lax.axis_index("seq")
    head_count = live_counts.shape[0]
    per_device = head_count // seq_count
    if per_device % 4 == 0:
        sizes = [per_device * 3 // 4, per_device // 4]
    else:
        sizes = [per_device]
    starts = [sum(sizes[:c]) for c in range(len(sizes))]
    tokens = query_rows.shape[1]
    width = query_rows.shape[2]
    depth = width // head_count
    permuted = seq_count <= 8

    backs = []
    previous = None
    for per_chunk, start in zip(sizes, starts):
        chunk_width = per_chunk * depth
        first = own_index * per_device + start
        lists = lax.dynamic_slice_in_dim(block_lists, first, per_chunk, 0)
        live = lax.dynamic_slice_in_dim(live_counts, first, per_chunk, 0)
        if permuted:
            pieces = pieces_of(
                query_rows,
                key_rows,
                value_rows,
                own_index,
                seq_count,
                per_device * depth,
                start * depth,
                chunk_width,
            )
            if previous is not None:
                pieces, _ = lax.optimization_barrier((pieces, previous))
            received = [pieces[0]]
            for step in range(1, seq_count):
                received.append(passed_along(pieces[step], "seq", step))
            previous = received
            outs = attend_pieces(received, lists, live, own_index.astype(jnp.int32))
            backs.append(outs[0])
            for step in range(1, seq_count):
                backs.append(passed_along(outs[step], "seq", -step))
            continue
        send = packed_chunk(
            query_rows, key_rows, value_rows, seq_count, per_device * depth, start * depth, chunk_width
        )
        if previous is not None:
            send, _ = lax.optimization_barrier((send, previous))
        packed = lax.all_to_all(send, "seq", 0, 0, tiled=True)
        previous = packed
        attended = attend_heads(packed, lists, live, jnp.zeros((), jnp.int32), False)
        backs.append(lax.all_to_all(attended, "seq", 0, 0, tiled=True))
    offsets = [s * depth for s in starts]
    if permuted:
        mixed_back = placed_back(backs, own_index, seq_count, per_device * depth, offsets)
    else:
        mixed_back = unpacked(backs, seq_count, per_device * depth, offsets)

    source = hidden_state[0].astype(jnp.float32)
    mean_row = jnp.mean(source, axis=1, keepdims=True)
    centred = source - mean_row
    spread = jnp.mean(centred * centred, axis=1, keepdims=True)
    normed = centred * lax.rsqrt(spread + epsilon)
    shaped = (normed * (1.0 + modulation[0, 1]) + modulation[0, 0]).astype(jnp.bfloat16)
    velocity = jnp.dot(shaped, head_weight, preferred_element_type=jnp.float32)
    change = noise_level(time_index[0] - 1) - noise_level(time_index[0])
    moved = latents[0] + change * velocity
    queue_next = passed_along(moved[None], "queue", -1)
    return (mixed_back, queue_next)


def solution(mesh):
    placed = (
        P(("groups", "queue"), "seq", None),
        P(("groups", "queue"), "seq", None),
        P(("groups", "queue"), "seq", None),
        P(("groups", "queue"), "seq", None),
        P(("groups", "queue"), None, None),
        P(),
        P(("groups", "queue"), "seq", None),
        P(("groups", "queue")),
        P(),
        P(),
    )
    return jax.shard_map(
        local,
        mesh=mesh,
        in_specs=placed,
        out_specs=(P(("groups", "queue"), "seq", None), P(("groups", "queue"), "seq", None)),
        check_vma=False,
    )
```

```python
import functools

import jax
import jax.numpy as jnp
from jax import lax
from jax.experimental import pallas as pl
from jax.experimental.pallas import tpu as pltpu
from jax.sharding import PartitionSpec as P

STEPS = 8


epsilon = 1e-06
plan_shift = 5.0


def passed_along(value, axis, steps):
    count = lax.axis_size(axis)
    pairs = [(source, (source + steps) % count) for source in range(count)]
    return lax.ppermute(value, axis, pairs)


def noise_level(step_value):
    fraction = step_value.astype(jnp.float32) / STEPS
    return plan_shift * fraction / (1.0 + (plan_shift - 1.0) * fraction)


def attend_kernel(
    lists_ref, live_ref, me_ref, x_ref, o_ref, *, block, slots, qblocks, heads, depth, shifted
):
    sources, _, tokens, _ = x_ref.shape
    me = me_ref[0]

    def slot_of(device):
        if shifted:
            return (me - device + sources) % sources
        return device

    total = sources * tokens
    scale = depth ** (-0.5)
    column = lax.broadcasted_iota(jnp.int32, (1, total), 1)
    per_source = tokens // block
    for head in range(heads):
        cols = slice(head * depth, (head + 1) * depth)
        keys = x_ref[:, 1, :, cols].reshape(total, depth)
        values = x_ref[:, 2, :, cols].reshape(total, depth)

        def body(qblock, carry):
            source = slot_of(qblock // per_source)
            first = pl.multiple_of((qblock % per_source) * block, block)
            query = x_ref[source, 0, pl.ds(first, block), cols]
            scores = (
                lax.dot_general(
                    query, keys, (((1,), (1,)), ((), ())), preferred_element_type=jnp.float32
                )
                * scale
            )
            live = live_ref[head * qblocks + qblock]
            active = column < 0
            for slot in range(slots):
                chosen = lists_ref[(head * qblocks + qblock) * slots + slot]
                place = slot_of(chosen // per_source)
                low = place * tokens + (chosen % per_source) * block
                active = active | ((column >= low) & (column < low + block) & (slot < live))
            scores = jnp.where(active, scores, -jnp.inf)
            highest = jnp.max(scores, axis=1, keepdims=True)
            weights = jnp.exp(scores - highest)
            totals = jnp.sum(weights, axis=1, keepdims=True)
            mixed = jnp.dot(
                weights.astype(jnp.bfloat16), values, preferred_element_type=jnp.float32
            )
            o_ref[source, pl.ds(first, block), cols] = (mixed / totals).astype(o_ref.dtype)
            return carry

        lax.fori_loop(0, qblocks, body, 0)


def attend_heads(packed, lists, live, me, shifted):
    sources, _, tokens, width = packed.shape
    head_total, qblocks = live.shape
    slots = lists.shape[2]
    depth = width // head_total
    block = sources * tokens // qblocks
    kernel = functools.partial(
        attend_kernel,
        block=block,
        slots=slots,
        qblocks=qblocks,
        heads=head_total,
        depth=depth,
        shifted=shifted,
    )
    smem = pltpu.SMEM
    return pl.pallas_call(
        kernel,
        in_specs=[
            pl.BlockSpec(memory_space=smem),
            pl.BlockSpec(memory_space=smem),
            pl.BlockSpec(memory_space=smem),
            pl.BlockSpec(memory_space=pltpu.VMEM),
        ],
        out_specs=pl.BlockSpec(memory_space=pltpu.VMEM),
        out_shape=jax.ShapeDtypeStruct((sources, tokens, width), jnp.bfloat16),
    )(lists.reshape(-1), live.reshape(-1), me.reshape(1), packed)


def pack_kernel(query_ref, key_ref, value_ref, out_ref, *, seq, stride, offset, width):
    for group in range(seq):
        cols = slice(group * stride + offset, group * stride + offset + width)
        for kind, source in enumerate((query_ref, key_ref, value_ref)):
            out_ref[group, kind] = source[0, :, cols]


def packed_chunk(query_rows, key_rows, value_rows, seq, stride, offset, width):
    tokens = query_rows.shape[1]
    kernel = functools.partial(pack_kernel, seq=seq, stride=stride, offset=offset, width=width)
    return pl.pallas_call(
        kernel,
        in_specs=[pl.BlockSpec(memory_space=pltpu.VMEM)] * 3,
        out_specs=pl.BlockSpec(memory_space=pltpu.VMEM),
        out_shape=jax.ShapeDtypeStruct((seq, 3, tokens, width), query_rows.dtype),
    )(query_rows, key_rows, value_rows)


def unpack_kernel(*refs, seq, stride, offsets):
    chunks = len(refs) - 1
    out_ref = refs[chunks]
    for c in range(chunks):
        width = refs[c].shape[2]
        for group in range(seq):
            low = group * stride + offsets[c]
            out_ref[0, :, low:low + width] = refs[c][group]


def unpacked(backs, seq, stride, offsets):
    tokens = backs[0].shape[1]
    kernel = functools.partial(unpack_kernel, seq=seq, stride=stride, offsets=tuple(offsets))
    return pl.pallas_call(
        kernel,
        in_specs=[pl.BlockSpec(memory_space=pltpu.VMEM)] * len(backs),
        out_specs=pl.BlockSpec(memory_space=pltpu.VMEM),
        out_shape=jax.ShapeDtypeStruct((1, tokens, seq * stride), backs[0].dtype),
    )(*backs)


def pieces_kernel(*refs, seq, stride, offset, width, me):
    sources, outs = refs[:3], refs[3:]
    for step in range(seq):
        low = ((me + step) % seq) * stride + offset
        for kind, source in enumerate(sources):
            outs[step][kind] = source[0, :, low:low + width]


def pieces_of(query_rows, key_rows, value_rows, own_index, seq, stride, offset, width):
    tokens = query_rows.shape[1]

    def branch(me, *rows):
        kernel = functools.partial(
            pieces_kernel, seq=seq, stride=stride, offset=offset, width=width, me=me
        )
        return tuple(
            pl.pallas_call(
                kernel,
                in_specs=[pl.BlockSpec(memory_space=pltpu.VMEM)] * 3,
                out_specs=[pl.BlockSpec(memory_space=pltpu.VMEM)] * seq,
                out_shape=[jax.ShapeDtypeStruct((3, tokens, width), query_rows.dtype)] * seq,
            )(*rows)
        )

    branches = [functools.partial(branch, me) for me in range(seq)]
    return lax.switch(own_index, branches, query_rows, key_rows, value_rows)


def attend_pieces_kernel(lists_ref, live_ref, me_ref, *refs, block, slots, qblocks, heads, depth):
    sources = len(refs) // 2
    x_refs, o_refs = refs[:sources], refs[sources:]
    tokens = x_refs[0].shape[1]
    total = sources * tokens
    me = me_ref[0]
    scale = depth ** (-0.5)
    per_source = tokens // block
    column = lax.broadcasted_iota(jnp.int32, (1, total), 1)
    for head in range(heads):
        cols = slice(head * depth, (head + 1) * depth)
        keys = jnp.concatenate([ref[1, :, cols] for ref in x_refs], axis=0)
        values = jnp.concatenate([ref[2, :, cols] for ref in x_refs], axis=0)
        for step in range(sources):
            device = (me - step + sources) % sources
            for sub in range(per_source):
                rows = slice(sub * block, (sub + 1) * block)
                query = x_refs[step][0, rows, cols]
                entry = head * qblocks + device * per_source + sub
                live = live_ref[entry]
                active = column < 0
                for slot in range(slots):
                    chosen = lists_ref[entry * slots + slot]
                    place = (me - chosen // per_source + sources) % sources
                    low = place * tokens + (chosen % per_source) * block
                    active = active | ((column >= low) & (column < low + block) & (slot < live))
                scores = (
                    lax.dot_general(
                        query, keys, (((1,), (1,)), ((), ())), preferred_element_type=jnp.float32
                    )
                    * scale
                )
                scores = jnp.where(active, scores, -jnp.inf)
                highest = jnp.max(scores, axis=1, keepdims=True)
                weights = jnp.exp(scores - highest)
                totals = jnp.sum(weights, axis=1, keepdims=True)
                mixed = jnp.dot(
                    weights.astype(jnp.bfloat16), values, preferred_element_type=jnp.float32
                )
                o_refs[step][rows, cols] = (mixed / totals).astype(o_refs[step].dtype)


def attend_pieces(pieces, lists, live, me):
    _, tokens, width = pieces[0].shape
    head_total, qblocks = live.shape
    slots = lists.shape[2]
    depth = width // head_total
    block = len(pieces) * tokens // qblocks
    kernel = functools.partial(
        attend_pieces_kernel,
        block=block,
        slots=slots,
        qblocks=qblocks,
        heads=head_total,
        depth=depth,
    )
    smem = pltpu.SMEM
    return pl.pallas_call(
        kernel,
        in_specs=[pl.BlockSpec(memory_space=smem)] * 3
        + [pl.BlockSpec(memory_space=pltpu.VMEM)] * len(pieces),
        out_specs=[pl.BlockSpec(memory_space=pltpu.VMEM)] * len(pieces),
        out_shape=[jax.ShapeDtypeStruct((tokens, width), jnp.bfloat16)] * len(pieces),
    )(lists.reshape(-1), live.reshape(-1), me.reshape(1), *pieces)


def place_kernel(*refs, seq, stride, offsets, me):
    out_ref = refs[-1]
    for c, offset in enumerate(offsets):
        for step in range(seq):
            piece = refs[c * seq + step]
            width = piece.shape[1]
            low = ((me + step) % seq) * stride + offset
            out_ref[0, :, low:low + width] = piece[...]


def placed_back(backs, own_index, seq, stride, offsets):
    tokens = backs[0].shape[0]

    def branch(me, *pieces):
        kernel = functools.partial(
            place_kernel, seq=seq, stride=stride, offsets=tuple(offsets), me=me
        )
        return pl.pallas_call(
            kernel,
            in_specs=[pl.BlockSpec(memory_space=pltpu.VMEM)] * len(pieces),
            out_specs=pl.BlockSpec(memory_space=pltpu.VMEM),
            out_shape=jax.ShapeDtypeStruct((1, tokens, seq * stride), pieces[0].dtype),
        )(*pieces)

    branches = [functools.partial(branch, me) for me in range(seq)]
    return lax.switch(own_index, branches, *backs)


def local(
    query_rows,
    key_rows,
    value_rows,
    hidden_state,
    modulation,
    head_weight,
    latents,
    time_index,
    live_counts,
    block_lists,
):
    seq_count = lax.axis_size("seq")
    own_index = lax.axis_index("seq")
    head_count = live_counts.shape[0]
    per_device = head_count // seq_count
    if per_device % 8 == 0:
        sizes = [per_device * 5 // 8, per_device * 2 // 8, per_device // 8]
    elif per_device % 4 == 0:
        sizes = [per_device * 3 // 4, per_device // 4]
    else:
        sizes = [per_device]
    starts = [sum(sizes[:c]) for c in range(len(sizes))]
    tokens = query_rows.shape[1]
    width = query_rows.shape[2]
    depth = width // head_count
    permuted = seq_count <= 8

    backs = []
    previous = None
    for per_chunk, start in zip(sizes, starts):
        chunk_width = per_chunk * depth
        first = own_index * per_device + start
        lists = lax.dynamic_slice_in_dim(block_lists, first, per_chunk, 0)
        live = lax.dynamic_slice_in_dim(live_counts, first, per_chunk, 0)
        if permuted:
            pieces = pieces_of(
                query_rows,
                key_rows,
                value_rows,
                own_index,
                seq_count,
                per_device * depth,
                start * depth,
                chunk_width,
            )
            if previous is not None:
                pieces, _ = lax.optimization_barrier((pieces, previous))
            received = [pieces[0]]
            for step in range(1, seq_count):
                received.append(passed_along(pieces[step], "seq", step))
            previous = received
            outs = attend_pieces(received, lists, live, own_index.astype(jnp.int32))
            backs.append(outs[0])
            for step in range(1, seq_count):
                backs.append(passed_along(outs[step], "seq", -step))
            continue
        send = packed_chunk(
            query_rows, key_rows, value_rows, seq_count, per_device * depth, start * depth, chunk_width
        )
        if previous is not None:
            send, _ = lax.optimization_barrier((send, previous))
        packed = lax.all_to_all(send, "seq", 0, 0, tiled=True)
        previous = packed
        attended = attend_heads(packed, lists, live, jnp.zeros((), jnp.int32), False)
        backs.append(lax.all_to_all(attended, "seq", 0, 0, tiled=True))
    offsets = [s * depth for s in starts]
    if permuted:
        mixed_back = placed_back(backs, own_index, seq_count, per_device * depth, offsets)
    else:
        mixed_back = unpacked(backs, seq_count, per_device * depth, offsets)

    source = hidden_state[0].astype(jnp.float32)
    mean_row = jnp.mean(source, axis=1, keepdims=True)
    centred = source - mean_row
    spread = jnp.mean(centred * centred, axis=1, keepdims=True)
    normed = centred * lax.rsqrt(spread + epsilon)
    shaped = (normed * (1.0 + modulation[0, 1]) + modulation[0, 0]).astype(jnp.bfloat16)
    velocity = jnp.dot(shaped, head_weight, preferred_element_type=jnp.float32)
    change = noise_level(time_index[0] - 1) - noise_level(time_index[0])
    moved = latents[0] + change * velocity
    queue_next = passed_along(moved[None], "queue", -1)
    return (mixed_back, queue_next)


def solution(mesh):
    placed = (
        P(("groups", "queue"), "seq", None),
        P(("groups", "queue"), "seq", None),
        P(("groups", "queue"), "seq", None),
        P(("groups", "queue"), "seq", None),
        P(("groups", "queue"), None, None),
        P(),
        P(("groups", "queue"), "seq", None),
        P(("groups", "queue")),
        P(),
        P(),
    )
    return jax.shard_map(
        local,
        mesh=mesh,
        in_specs=placed,
        out_specs=(P(("groups", "queue"), "seq", None), P(("groups", "queue"), "seq", None)),
        check_vma=False,
    )
```

```python
import functools

import jax
import jax.numpy as jnp
from jax import lax
from jax.experimental import pallas as pl
from jax.experimental.pallas import tpu as pltpu
from jax.sharding import PartitionSpec as P

STEPS = 8


epsilon = 1e-06
plan_shift = 5.0


def passed_along(value, axis, steps):
    count = lax.axis_size(axis)
    pairs = [(source, (source + steps) % count) for source in range(count)]
    return lax.ppermute(value, axis, pairs)


def noise_level(step_value):
    fraction = step_value.astype(jnp.float32) / STEPS
    return plan_shift * fraction / (1.0 + (plan_shift - 1.0) * fraction)


def attend_kernel(
    lists_ref, live_ref, me_ref, x_ref, o_ref, *, block, slots, qblocks, heads, depth, shifted
):
    sources, _, tokens, _ = x_ref.shape
    me = me_ref[0]

    def slot_of(device):
        if shifted:
            return (me - device + sources) % sources
        return device

    total = sources * tokens
    scale = depth ** (-0.5)
    column = lax.broadcasted_iota(jnp.int32, (1, total), 1)
    per_source = tokens // block
    for head in range(heads):
        cols = slice(head * depth, (head + 1) * depth)
        keys = x_ref[:, 1, :, cols].reshape(total, depth)
        values = x_ref[:, 2, :, cols].reshape(total, depth)

        def body(qblock, carry):
            source = slot_of(qblock // per_source)
            first = pl.multiple_of((qblock % per_source) * block, block)
            query = x_ref[source, 0, pl.ds(first, block), cols]
            scores = (
                lax.dot_general(
                    query, keys, (((1,), (1,)), ((), ())), preferred_element_type=jnp.float32
                )
                * scale
            )
            live = live_ref[head * qblocks + qblock]
            active = column < 0
            for slot in range(slots):
                chosen = lists_ref[(head * qblocks + qblock) * slots + slot]
                place = slot_of(chosen // per_source)
                low = place * tokens + (chosen % per_source) * block
                active = active | ((column >= low) & (column < low + block) & (slot < live))
            scores = jnp.where(active, scores, -jnp.inf)
            highest = jnp.max(scores, axis=1, keepdims=True)
            weights = jnp.exp(scores - highest)
            totals = jnp.sum(weights, axis=1, keepdims=True)
            mixed = jnp.dot(
                weights.astype(jnp.bfloat16), values, preferred_element_type=jnp.float32
            )
            o_ref[source, pl.ds(first, block), cols] = (mixed / totals).astype(o_ref.dtype)
            return carry

        lax.fori_loop(0, qblocks, body, 0)


def attend_heads(packed, lists, live, me, shifted):
    sources, _, tokens, width = packed.shape
    head_total, qblocks = live.shape
    slots = lists.shape[2]
    depth = width // head_total
    block = sources * tokens // qblocks
    kernel = functools.partial(
        attend_kernel,
        block=block,
        slots=slots,
        qblocks=qblocks,
        heads=head_total,
        depth=depth,
        shifted=shifted,
    )
    smem = pltpu.SMEM
    return pl.pallas_call(
        kernel,
        in_specs=[
            pl.BlockSpec(memory_space=smem),
            pl.BlockSpec(memory_space=smem),
            pl.BlockSpec(memory_space=smem),
            pl.BlockSpec(memory_space=pltpu.VMEM),
        ],
        out_specs=pl.BlockSpec(memory_space=pltpu.VMEM),
        out_shape=jax.ShapeDtypeStruct((sources, tokens, width), jnp.bfloat16),
    )(lists.reshape(-1), live.reshape(-1), me.reshape(1), packed)


def pack_kernel(query_ref, key_ref, value_ref, out_ref, *, seq, stride, offset, width):
    for group in range(seq):
        cols = slice(group * stride + offset, group * stride + offset + width)
        for kind, source in enumerate((query_ref, key_ref, value_ref)):
            out_ref[group, kind] = source[0, :, cols]


def packed_chunk(query_rows, key_rows, value_rows, seq, stride, offset, width):
    tokens = query_rows.shape[1]
    kernel = functools.partial(pack_kernel, seq=seq, stride=stride, offset=offset, width=width)
    return pl.pallas_call(
        kernel,
        in_specs=[pl.BlockSpec(memory_space=pltpu.VMEM)] * 3,
        out_specs=pl.BlockSpec(memory_space=pltpu.VMEM),
        out_shape=jax.ShapeDtypeStruct((seq, 3, tokens, width), query_rows.dtype),
    )(query_rows, key_rows, value_rows)


def unpack_kernel(*refs, seq, stride, offsets):
    chunks = len(refs) - 1
    out_ref = refs[chunks]
    for c in range(chunks):
        width = refs[c].shape[2]
        for group in range(seq):
            low = group * stride + offsets[c]
            out_ref[0, :, low:low + width] = refs[c][group]


def unpacked(backs, seq, stride, offsets):
    tokens = backs[0].shape[1]
    kernel = functools.partial(unpack_kernel, seq=seq, stride=stride, offsets=tuple(offsets))
    return pl.pallas_call(
        kernel,
        in_specs=[pl.BlockSpec(memory_space=pltpu.VMEM)] * len(backs),
        out_specs=pl.BlockSpec(memory_space=pltpu.VMEM),
        out_shape=jax.ShapeDtypeStruct((1, tokens, seq * stride), backs[0].dtype),
    )(*backs)


def pieces_kernel(*refs, seq, stride, offset, width, me):
    sources, outs = refs[:3], refs[3:]
    for step in range(seq):
        low = ((me + step) % seq) * stride + offset
        for kind, source in enumerate(sources):
            outs[step][kind] = source[0, :, low:low + width]


def pieces_of(query_rows, key_rows, value_rows, own_index, seq, stride, offset, width):
    tokens = query_rows.shape[1]

    def branch(me, *rows):
        kernel = functools.partial(
            pieces_kernel, seq=seq, stride=stride, offset=offset, width=width, me=me
        )
        return tuple(
            pl.pallas_call(
                kernel,
                in_specs=[pl.BlockSpec(memory_space=pltpu.VMEM)] * 3,
                out_specs=[pl.BlockSpec(memory_space=pltpu.VMEM)] * seq,
                out_shape=[jax.ShapeDtypeStruct((3, tokens, width), query_rows.dtype)] * seq,
            )(*rows)
        )

    branches = [functools.partial(branch, me) for me in range(seq)]
    return lax.switch(own_index, branches, query_rows, key_rows, value_rows)


def attend_pieces_kernel(lists_ref, live_ref, me_ref, *refs, block, slots, qblocks, heads, depth):
    sources = len(refs) // 2
    x_refs, o_refs = refs[:sources], refs[sources:]
    tokens = x_refs[0].shape[1]
    total = sources * tokens
    me = me_ref[0]
    scale = depth ** (-0.5)
    per_source = tokens // block
    column = lax.broadcasted_iota(jnp.int32, (1, total), 1)
    for head in range(heads):
        cols = slice(head * depth, (head + 1) * depth)
        keys = jnp.concatenate([ref[1, :, cols] for ref in x_refs], axis=0).T
        values = jnp.concatenate([ref[2, :, cols] for ref in x_refs], axis=0)
        for step in range(sources):
            device = (me - step + sources) % sources
            for sub in range(per_source):
                rows = slice(sub * block, (sub + 1) * block)
                query = x_refs[step][0, rows, cols]
                entry = head * qblocks + device * per_source + sub
                live = live_ref[entry]
                active = column < 0
                for slot in range(slots):
                    chosen = lists_ref[entry * slots + slot]
                    place = (me - chosen // per_source + sources) % sources
                    low = place * tokens + (chosen % per_source) * block
                    active = active | ((column >= low) & (column < low + block) & (slot < live))
                bias = jnp.where(active, 0.0, -jnp.inf).astype(jnp.float32)
                scores = (
                    jnp.dot(query, keys, preferred_element_type=jnp.float32) * scale + bias
                )
                highest = jnp.max(scores, axis=1, keepdims=True)
                weights = jnp.exp(scores - highest)
                totals = jnp.sum(weights, axis=1, keepdims=True)
                mixed = jnp.dot(
                    weights.astype(jnp.bfloat16), values, preferred_element_type=jnp.float32
                )
                o_refs[step][rows, cols] = (mixed / totals).astype(o_refs[step].dtype)


def attend_pieces(pieces, lists, live, me):
    _, tokens, width = pieces[0].shape
    head_total, qblocks = live.shape
    slots = lists.shape[2]
    depth = width // head_total
    block = len(pieces) * tokens // qblocks
    kernel = functools.partial(
        attend_pieces_kernel,
        block=block,
        slots=slots,
        qblocks=qblocks,
        heads=head_total,
        depth=depth,
    )
    smem = pltpu.SMEM
    return pl.pallas_call(
        kernel,
        in_specs=[pl.BlockSpec(memory_space=smem)] * 3
        + [pl.BlockSpec(memory_space=pltpu.VMEM)] * len(pieces),
        out_specs=[pl.BlockSpec(memory_space=pltpu.VMEM)] * len(pieces),
        out_shape=[jax.ShapeDtypeStruct((tokens, width), jnp.bfloat16)] * len(pieces),
    )(lists.reshape(-1), live.reshape(-1), me.reshape(1), *pieces)


def place_kernel(*refs, seq, stride, offsets, me):
    out_ref = refs[-1]
    for c, offset in enumerate(offsets):
        for step in range(seq):
            piece = refs[c * seq + step]
            width = piece.shape[1]
            low = ((me + step) % seq) * stride + offset
            out_ref[0, :, low:low + width] = piece[...]


def placed_back(backs, own_index, seq, stride, offsets):
    tokens = backs[0].shape[0]

    def branch(me, *pieces):
        kernel = functools.partial(
            place_kernel, seq=seq, stride=stride, offsets=tuple(offsets), me=me
        )
        return pl.pallas_call(
            kernel,
            in_specs=[pl.BlockSpec(memory_space=pltpu.VMEM)] * len(pieces),
            out_specs=pl.BlockSpec(memory_space=pltpu.VMEM),
            out_shape=jax.ShapeDtypeStruct((1, tokens, seq * stride), pieces[0].dtype),
        )(*pieces)

    branches = [functools.partial(branch, me) for me in range(seq)]
    return lax.switch(own_index, branches, *backs)


def local(
    query_rows,
    key_rows,
    value_rows,
    hidden_state,
    modulation,
    head_weight,
    latents,
    time_index,
    live_counts,
    block_lists,
):
    seq_count = lax.axis_size("seq")
    own_index = lax.axis_index("seq")
    head_count = live_counts.shape[0]
    per_device = head_count // seq_count
    if per_device % 4 == 0:
        sizes = [per_device * 3 // 4, per_device // 4]
    else:
        sizes = [per_device]
    starts = [sum(sizes[:c]) for c in range(len(sizes))]
    tokens = query_rows.shape[1]
    width = query_rows.shape[2]
    depth = width // head_count
    permuted = seq_count <= 8

    backs = []
    previous = None
    for per_chunk, start in zip(sizes, starts):
        chunk_width = per_chunk * depth
        first = own_index * per_device + start
        lists = lax.dynamic_slice_in_dim(block_lists, first, per_chunk, 0)
        live = lax.dynamic_slice_in_dim(live_counts, first, per_chunk, 0)
        if permuted:
            pieces = pieces_of(
                query_rows,
                key_rows,
                value_rows,
                own_index,
                seq_count,
                per_device * depth,
                start * depth,
                chunk_width,
            )
            if previous is not None:
                pieces, _ = lax.optimization_barrier((pieces, previous))
            received = [pieces[0]]
            for step in range(1, seq_count):
                received.append(passed_along(pieces[step], "seq", step))
            previous = received
            outs = attend_pieces(received, lists, live, own_index.astype(jnp.int32))
            backs.append(outs[0])
            for step in range(1, seq_count):
                backs.append(passed_along(outs[step], "seq", -step))
            continue
        send = packed_chunk(
            query_rows, key_rows, value_rows, seq_count, per_device * depth, start * depth, chunk_width
        )
        if previous is not None:
            send, _ = lax.optimization_barrier((send, previous))
        packed = lax.all_to_all(send, "seq", 0, 0, tiled=True)
        previous = packed
        attended = attend_heads(packed, lists, live, jnp.zeros((), jnp.int32), False)
        backs.append(lax.all_to_all(attended, "seq", 0, 0, tiled=True))
    offsets = [s * depth for s in starts]
    if permuted:
        mixed_back = placed_back(backs, own_index, seq_count, per_device * depth, offsets)
    else:
        mixed_back = unpacked(backs, seq_count, per_device * depth, offsets)

    source = hidden_state[0].astype(jnp.float32)
    mean_row = jnp.mean(source, axis=1, keepdims=True)
    centred = source - mean_row
    spread = jnp.mean(centred * centred, axis=1, keepdims=True)
    normed = centred * lax.rsqrt(spread + epsilon)
    shaped = (normed * (1.0 + modulation[0, 1]) + modulation[0, 0]).astype(jnp.bfloat16)
    velocity = jnp.dot(shaped, head_weight, preferred_element_type=jnp.float32)
    change = noise_level(time_index[0] - 1) - noise_level(time_index[0])
    moved = latents[0] + change * velocity
    queue_next = passed_along(moved[None], "queue", -1)
    return (mixed_back, queue_next)


def solution(mesh):
    placed = (
        P(("groups", "queue"), "seq", None),
        P(("groups", "queue"), "seq", None),
        P(("groups", "queue"), "seq", None),
        P(("groups", "queue"), "seq", None),
        P(("groups", "queue"), None, None),
        P(),
        P(("groups", "queue"), "seq", None),
        P(("groups", "queue")),
        P(),
        P(),
    )
    return jax.shard_map(
        local,
        mesh=mesh,
        in_specs=placed,
        out_specs=(P(("groups", "queue"), "seq", None), P(("groups", "queue"), "seq", None)),
        check_vma=False,
    )
```

```python
import functools

import jax
import jax.numpy as jnp
from jax import lax
from jax.experimental import pallas as pl
from jax.experimental.pallas import tpu as pltpu
from jax.sharding import PartitionSpec as P

STEPS = 8


epsilon = 1e-06
plan_shift = 5.0


def passed_along(value, axis, steps):
    count = lax.axis_size(axis)
    pairs = [(source, (source + steps) % count) for source in range(count)]
    return lax.ppermute(value, axis, pairs)


def noise_level(step_value):
    fraction = step_value.astype(jnp.float32) / STEPS
    return plan_shift * fraction / (1.0 + (plan_shift - 1.0) * fraction)


def attend_kernel(
    lists_ref, live_ref, me_ref, x_ref, o_ref, *, block, slots, qblocks, heads, depth, shifted
):
    sources, _, tokens, _ = x_ref.shape
    me = me_ref[0]

    def slot_of(device):
        if shifted:
            return (me - device + sources) % sources
        return device

    total = sources * tokens
    scale = depth ** (-0.5)
    column = lax.broadcasted_iota(jnp.int32, (1, total), 1)
    per_source = tokens // block
    for head in range(heads):
        cols = slice(head * depth, (head + 1) * depth)
        keys = x_ref[:, 1, :, cols].reshape(total, depth)
        values = x_ref[:, 2, :, cols].reshape(total, depth)

        def body(qblock, carry):
            source = slot_of(qblock // per_source)
            first = pl.multiple_of((qblock % per_source) * block, block)
            query = x_ref[source, 0, pl.ds(first, block), cols]
            scores = (
                lax.dot_general(
                    query, keys, (((1,), (1,)), ((), ())), preferred_element_type=jnp.float32
                )
                * scale
            )
            live = live_ref[head * qblocks + qblock]
            active = column < 0
            for slot in range(slots):
                chosen = lists_ref[(head * qblocks + qblock) * slots + slot]
                place = slot_of(chosen // per_source)
                low = place * tokens + (chosen % per_source) * block
                active = active | ((column >= low) & (column < low + block) & (slot < live))
            scores = jnp.where(active, scores, -jnp.inf)
            highest = jnp.max(scores, axis=1, keepdims=True)
            weights = jnp.exp(scores - highest)
            totals = jnp.sum(weights, axis=1, keepdims=True)
            mixed = jnp.dot(
                weights.astype(jnp.bfloat16), values, preferred_element_type=jnp.float32
            )
            o_ref[source, pl.ds(first, block), cols] = (mixed / totals).astype(o_ref.dtype)
            return carry

        lax.fori_loop(0, qblocks, body, 0)


def attend_heads(packed, lists, live, me, shifted):
    sources, _, tokens, width = packed.shape
    head_total, qblocks = live.shape
    slots = lists.shape[2]
    depth = width // head_total
    block = sources * tokens // qblocks
    kernel = functools.partial(
        attend_kernel,
        block=block,
        slots=slots,
        qblocks=qblocks,
        heads=head_total,
        depth=depth,
        shifted=shifted,
    )
    smem = pltpu.SMEM
    return pl.pallas_call(
        kernel,
        in_specs=[
            pl.BlockSpec(memory_space=smem),
            pl.BlockSpec(memory_space=smem),
            pl.BlockSpec(memory_space=smem),
            pl.BlockSpec(memory_space=pltpu.VMEM),
        ],
        out_specs=pl.BlockSpec(memory_space=pltpu.VMEM),
        out_shape=jax.ShapeDtypeStruct((sources, tokens, width), jnp.bfloat16),
    )(lists.reshape(-1), live.reshape(-1), me.reshape(1), packed)


def pack_kernel(query_ref, key_ref, value_ref, out_ref, *, seq, stride, offset, width):
    for group in range(seq):
        cols = slice(group * stride + offset, group * stride + offset + width)
        for kind, source in enumerate((query_ref, key_ref, value_ref)):
            out_ref[group, kind] = source[0, :, cols]


def packed_chunk(query_rows, key_rows, value_rows, seq, stride, offset, width):
    tokens = query_rows.shape[1]
    kernel = functools.partial(pack_kernel, seq=seq, stride=stride, offset=offset, width=width)
    return pl.pallas_call(
        kernel,
        in_specs=[pl.BlockSpec(memory_space=pltpu.VMEM)] * 3,
        out_specs=pl.BlockSpec(memory_space=pltpu.VMEM),
        out_shape=jax.ShapeDtypeStruct((seq, 3, tokens, width), query_rows.dtype),
    )(query_rows, key_rows, value_rows)


def unpack_kernel(*refs, seq, stride, offsets):
    chunks = len(refs) - 1
    out_ref = refs[chunks]
    for c in range(chunks):
        width = refs[c].shape[2]
        for group in range(seq):
            low = group * stride + offsets[c]
            out_ref[0, :, low:low + width] = refs[c][group]


def unpacked(backs, seq, stride, offsets):
    tokens = backs[0].shape[1]
    kernel = functools.partial(unpack_kernel, seq=seq, stride=stride, offsets=tuple(offsets))
    return pl.pallas_call(
        kernel,
        in_specs=[pl.BlockSpec(memory_space=pltpu.VMEM)] * len(backs),
        out_specs=pl.BlockSpec(memory_space=pltpu.VMEM),
        out_shape=jax.ShapeDtypeStruct((1, tokens, seq * stride), backs[0].dtype),
    )(*backs)


def pieces_kernel(*refs, seq, stride, offset, width, me):
    sources, outs = refs[:3], refs[3:]
    for step in range(seq):
        low = ((me + step) % seq) * stride + offset
        for kind, source in enumerate(sources):
            outs[step][kind] = source[0, :, low:low + width]


def pieces_of(query_rows, key_rows, value_rows, own_index, seq, stride, offset, width):
    tokens = query_rows.shape[1]

    def branch(me, *rows):
        kernel = functools.partial(
            pieces_kernel, seq=seq, stride=stride, offset=offset, width=width, me=me
        )
        return tuple(
            pl.pallas_call(
                kernel,
                in_specs=[pl.BlockSpec(memory_space=pltpu.VMEM)] * 3,
                out_specs=[pl.BlockSpec(memory_space=pltpu.VMEM)] * seq,
                out_shape=[jax.ShapeDtypeStruct((3, tokens, width), query_rows.dtype)] * seq,
            )(*rows)
        )

    branches = [functools.partial(branch, me) for me in range(seq)]
    return lax.switch(own_index, branches, query_rows, key_rows, value_rows)


def attend_pieces_kernel(lists_ref, live_ref, me_ref, *refs, block, slots, qblocks, heads, depth):
    sources = len(refs) // 2
    x_refs, o_refs = refs[:sources], refs[sources:]
    tokens = x_refs[0].shape[1]
    total = sources * tokens
    me = me_ref[0]
    scale = depth ** (-0.5)
    per_source = tokens // block
    column = lax.broadcasted_iota(jnp.int32, (1, total), 1)
    for head in range(heads):
        cols = slice(head * depth, (head + 1) * depth)
        keys = jnp.concatenate([ref[1, :, cols] for ref in x_refs], axis=0)
        values = jnp.concatenate([ref[2, :, cols] for ref in x_refs], axis=0)
        for step in range(sources):
            device = (me - step + sources) % sources
            for sub in range(per_source):
                rows = slice(sub * block, (sub + 1) * block)
                query = x_refs[step][0, rows, cols]
                entry = head * qblocks + device * per_source + sub
                live = live_ref[entry]
                active = column < 0
                for slot in range(slots):
                    chosen = lists_ref[entry * slots + slot]
                    place = (me - chosen // per_source + sources) % sources
                    low = place * tokens + (chosen % per_source) * block
                    active = active | ((column >= low) & (column < low + block) & (slot < live))
                scores = (
                    lax.dot_general(
                        query, keys, (((1,), (1,)), ((), ())), preferred_element_type=jnp.float32
                    )
                    * scale
                )
                scores = jnp.where(active, scores, -jnp.inf)
                highest = jnp.max(scores, axis=1, keepdims=True)
                weights = jnp.exp(scores - highest)
                totals = jnp.sum(weights, axis=1, keepdims=True)
                mixed = jnp.dot(
                    weights.astype(jnp.bfloat16), values, preferred_element_type=jnp.float32
                )
                o_refs[step][rows, cols] = (mixed / totals).astype(o_refs[step].dtype)


def attend_pieces(pieces, lists, live, me):
    _, tokens, width = pieces[0].shape
    head_total, qblocks = live.shape
    slots = lists.shape[2]
    depth = width // head_total
    block = len(pieces) * tokens // qblocks
    kernel = functools.partial(
        attend_pieces_kernel,
        block=block,
        slots=slots,
        qblocks=qblocks,
        heads=head_total,
        depth=depth,
    )
    smem = pltpu.SMEM
    return pl.pallas_call(
        kernel,
        in_specs=[pl.BlockSpec(memory_space=smem)] * 3
        + [pl.BlockSpec(memory_space=pltpu.VMEM)] * len(pieces),
        out_specs=[pl.BlockSpec(memory_space=pltpu.VMEM)] * len(pieces),
        out_shape=[jax.ShapeDtypeStruct((tokens, width), jnp.bfloat16)] * len(pieces),
    )(lists.reshape(-1), live.reshape(-1), me.reshape(1), *pieces)


def place_kernel(*refs, seq, stride, offsets, me):
    out_ref = refs[-1]
    for c, offset in enumerate(offsets):
        for step in range(seq):
            piece = refs[c * seq + step]
            width = piece.shape[1]
            low = ((me + step) % seq) * stride + offset
            out_ref[0, :, low:low + width] = piece[...]


def placed_back(backs, own_index, seq, stride, offsets):
    tokens = backs[0].shape[0]

    def branch(me, *pieces):
        kernel = functools.partial(
            place_kernel, seq=seq, stride=stride, offsets=tuple(offsets), me=me
        )
        return pl.pallas_call(
            kernel,
            in_specs=[pl.BlockSpec(memory_space=pltpu.VMEM)] * len(pieces),
            out_specs=pl.BlockSpec(memory_space=pltpu.VMEM),
            out_shape=jax.ShapeDtypeStruct((1, tokens, seq * stride), pieces[0].dtype),
        )(*pieces)

    branches = [functools.partial(branch, me) for me in range(seq)]
    return lax.switch(own_index, branches, *backs)


def local(
    query_rows,
    key_rows,
    value_rows,
    hidden_state,
    modulation,
    head_weight,
    latents,
    time_index,
    live_counts,
    block_lists,
):
    seq_count = lax.axis_size("seq")
    own_index = lax.axis_index("seq")
    head_count = live_counts.shape[0]
    per_device = head_count // seq_count
    if per_device % 8 == 0:
        sizes = [per_device * 7 // 8, per_device // 8]
    elif per_device % 4 == 0:
        sizes = [per_device * 3 // 4, per_device // 4]
    else:
        sizes = [per_device]
    starts = [sum(sizes[:c]) for c in range(len(sizes))]
    tokens = query_rows.shape[1]
    width = query_rows.shape[2]
    depth = width // head_count
    permuted = seq_count <= 8

    backs = []
    previous = None
    for per_chunk, start in zip(sizes, starts):
        chunk_width = per_chunk * depth
        first = own_index * per_device + start
        lists = lax.dynamic_slice_in_dim(block_lists, first, per_chunk, 0)
        live = lax.dynamic_slice_in_dim(live_counts, first, per_chunk, 0)
        if permuted:
            pieces = pieces_of(
                query_rows,
                key_rows,
                value_rows,
                own_index,
                seq_count,
                per_device * depth,
                start * depth,
                chunk_width,
            )
            if previous is not None:
                pieces, _ = lax.optimization_barrier((pieces, previous))
            received = [pieces[0]]
            for step in range(1, seq_count):
                received.append(passed_along(pieces[step], "seq", step))
            previous = received
            outs = attend_pieces(received, lists, live, own_index.astype(jnp.int32))
            backs.append(outs[0])
            for step in range(1, seq_count):
                backs.append(passed_along(outs[step], "seq", -step))
            continue
        send = packed_chunk(
            query_rows, key_rows, value_rows, seq_count, per_device * depth, start * depth, chunk_width
        )
        if previous is not None:
            send, _ = lax.optimization_barrier((send, previous))
        packed = lax.all_to_all(send, "seq", 0, 0, tiled=True)
        previous = packed
        attended = attend_heads(packed, lists, live, jnp.zeros((), jnp.int32), False)
        backs.append(lax.all_to_all(attended, "seq", 0, 0, tiled=True))
    offsets = [s * depth for s in starts]
    if permuted:
        mixed_back = placed_back(backs, own_index, seq_count, per_device * depth, offsets)
    else:
        mixed_back = unpacked(backs, seq_count, per_device * depth, offsets)

    source = hidden_state[0].astype(jnp.float32)
    mean_row = jnp.mean(source, axis=1, keepdims=True)
    centred = source - mean_row
    spread = jnp.mean(centred * centred, axis=1, keepdims=True)
    normed = centred * lax.rsqrt(spread + epsilon)
    shaped = (normed * (1.0 + modulation[0, 1]) + modulation[0, 0]).astype(jnp.bfloat16)
    velocity = jnp.dot(shaped, head_weight, preferred_element_type=jnp.float32)
    change = noise_level(time_index[0] - 1) - noise_level(time_index[0])
    moved = latents[0] + change * velocity
    queue_next = passed_along(moved[None], "queue", -1)
    return (mixed_back, queue_next)


def solution(mesh):
    placed = (
        P(("groups", "queue"), "seq", None),
        P(("groups", "queue"), "seq", None),
        P(("groups", "queue"), "seq", None),
        P(("groups", "queue"), "seq", None),
        P(("groups", "queue"), None, None),
        P(),
        P(("groups", "queue"), "seq", None),
        P(("groups", "queue")),
        P(),
        P(),
    )
    return jax.shard_map(
        local,
        mesh=mesh,
        in_specs=placed,
        out_specs=(P(("groups", "queue"), "seq", None), P(("groups", "queue"), "seq", None)),
        check_vma=False,
    )
```

```python
import functools

import jax
import jax.numpy as jnp
from jax import lax
from jax.experimental import pallas as pl
from jax.experimental.pallas import tpu as pltpu
from jax.sharding import PartitionSpec as P


STEPS = 8


epsilon = 1e-06
plan_shift = 5.0


def passed_along(value, axis, steps):
    count = lax.axis_size(axis)
    pairs = [(source, (source + steps) % count) for source in range(count)]
    return lax.ppermute(value, axis, pairs)


def noise_level(step_value):
    fraction = step_value.astype(jnp.float32) / STEPS
    return plan_shift * fraction / (1.0 + (plan_shift - 1.0) * fraction)


def attend_kernel(
    lists_ref, live_ref, me_ref, x_ref, o_ref, *, block, slots, qblocks, heads, depth, shifted
):
    sources, _, tokens, _ = x_ref.shape
    me = me_ref[0]

    def slot_of(device):
        if shifted:
            return (me - device + sources) % sources
        return device

    total = sources * tokens
    scale = depth ** (-0.5)
    column = lax.broadcasted_iota(jnp.int32, (1, total), 1)
    per_source = tokens // block
    for head in range(heads):
        cols = slice(head * depth, (head + 1) * depth)
        keys = x_ref[:, 1, :, cols].reshape(total, depth)
        values = x_ref[:, 2, :, cols].reshape(total, depth)

        def body(qblock, carry):
            source = slot_of(qblock // per_source)
            first = pl.multiple_of((qblock % per_source) * block, block)
            query = x_ref[source, 0, pl.ds(first, block), cols]
            scores = (
                lax.dot_general(
                    query, keys, (((1,), (1,)), ((), ())), preferred_element_type=jnp.float32
                )
                * scale
            )
            live = live_ref[head * qblocks + qblock]
            active = column < 0
            for slot in range(slots):
                chosen = lists_ref[(head * qblocks + qblock) * slots + slot]
                place = slot_of(chosen // per_source)
                low = place * tokens + (chosen % per_source) * block
                active = active | ((column >= low) & (column < low + block) & (slot < live))
            scores = jnp.where(active, scores, -jnp.inf)
            highest = jnp.max(scores, axis=1, keepdims=True)
            weights = jnp.exp(scores - highest)
            totals = jnp.sum(weights, axis=1, keepdims=True)
            mixed = jnp.dot(
                weights.astype(jnp.bfloat16), values, preferred_element_type=jnp.float32
            )
            o_ref[source, pl.ds(first, block), cols] = (mixed / totals).astype(o_ref.dtype)
            return carry

        lax.fori_loop(0, qblocks, body, 0)


def attend_heads(packed, lists, live, me, shifted):
    sources, _, tokens, width = packed.shape
    head_total, qblocks = live.shape
    slots = lists.shape[2]
    depth = width // head_total
    block = sources * tokens // qblocks
    kernel = functools.partial(
        attend_kernel,
        block=block,
        slots=slots,
        qblocks=qblocks,
        heads=head_total,
        depth=depth,
        shifted=shifted,
    )
    smem = pltpu.SMEM
    return pl.pallas_call(
        kernel,
        in_specs=[
            pl.BlockSpec(memory_space=smem),
            pl.BlockSpec(memory_space=smem),
            pl.BlockSpec(memory_space=smem),
            pl.BlockSpec(memory_space=pltpu.VMEM),
        ],
        out_specs=pl.BlockSpec(memory_space=pltpu.VMEM),
        out_shape=jax.ShapeDtypeStruct((sources, tokens, width), jnp.bfloat16),
    )(lists.reshape(-1), live.reshape(-1), me.reshape(1), packed)


def pack_kernel(query_ref, key_ref, value_ref, out_ref, *, seq, stride, offset, width):
    for group in range(seq):
        cols = slice(group * stride + offset, group * stride + offset + width)
        for kind, source in enumerate((query_ref, key_ref, value_ref)):
            out_ref[group, kind] = source[0, :, cols]


def packed_chunk(query_rows, key_rows, value_rows, seq, stride, offset, width):
    tokens = query_rows.shape[1]
    kernel = functools.partial(pack_kernel, seq=seq, stride=stride, offset=offset, width=width)
    return pl.pallas_call(
        kernel,
        in_specs=[pl.BlockSpec(memory_space=pltpu.VMEM)] * 3,
        out_specs=pl.BlockSpec(memory_space=pltpu.VMEM),
        out_shape=jax.ShapeDtypeStruct((seq, 3, tokens, width), query_rows.dtype),
    )(query_rows, key_rows, value_rows)


def unpack_kernel(*refs, seq, stride, offsets):
    chunks = len(refs) - 1
    out_ref = refs[chunks]
    for c in range(chunks):
        width = refs[c].shape[2]
        for group in range(seq):
            low = group * stride + offsets[c]
            out_ref[0, :, low:low + width] = refs[c][group]


def unpacked(backs, seq, stride, offsets):
    tokens = backs[0].shape[1]
    kernel = functools.partial(unpack_kernel, seq=seq, stride=stride, offsets=tuple(offsets))
    return pl.pallas_call(
        kernel,
        in_specs=[pl.BlockSpec(memory_space=pltpu.VMEM)] * len(backs),
        out_specs=pl.BlockSpec(memory_space=pltpu.VMEM),
        out_shape=jax.ShapeDtypeStruct((1, tokens, seq * stride), backs[0].dtype),
    )(*backs)


def pieces_kernel(*refs, seq, stride, offset, width, me):
    sources, outs = refs[:3], refs[3:]
    for step in range(seq):
        low = ((me + step) % seq) * stride + offset
        for kind, source in enumerate(sources):
            outs[step][kind] = source[0, :, low:low + width]


def pieces_of(query_rows, key_rows, value_rows, own_index, seq, stride, offset, width):
    tokens = query_rows.shape[1]

    def branch(me, *rows):
        kernel = functools.partial(
            pieces_kernel, seq=seq, stride=stride, offset=offset, width=width, me=me
        )
        return tuple(
            pl.pallas_call(
                kernel,
                in_specs=[pl.BlockSpec(memory_space=pltpu.VMEM)] * 3,
                out_specs=[pl.BlockSpec(memory_space=pltpu.VMEM)] * seq,
                out_shape=[jax.ShapeDtypeStruct((3, tokens, width), query_rows.dtype)] * seq,
            )(*rows)
        )

    branches = [functools.partial(branch, me) for me in range(seq)]
    return lax.switch(own_index, branches, query_rows, key_rows, value_rows)


def attend_pieces_kernel(lists_ref, live_ref, me_ref, *refs, block, slots, qblocks, heads, depth):
    sources = len(refs) // 2
    x_refs, o_refs = refs[:sources], refs[sources:]
    tokens = x_refs[0].shape[1]
    total = sources * tokens
    me = me_ref[0]
    scale = depth ** (-0.5)
    per_source = tokens // block
    column = lax.broadcasted_iota(jnp.int32, (1, total), 1)
    for head in range(heads):
        cols = slice(head * depth, (head + 1) * depth)
        keys = jnp.concatenate([ref[1, :, cols] for ref in x_refs], axis=0)
        values = jnp.concatenate([ref[2, :, cols] for ref in x_refs], axis=0)
        for step in range(sources):
            device = (me - step + sources) % sources
            for sub in range(per_source):
                rows = slice(sub * block, (sub + 1) * block)
                query = x_refs[step][0, rows, cols]
                entry = head * qblocks + device * per_source + sub
                live = live_ref[entry]
                active = column < 0
                for slot in range(slots):
                    chosen = lists_ref[entry * slots + slot]
                    place = (me - chosen // per_source + sources) % sources
                    low = place * tokens + (chosen % per_source) * block
                    active = active | ((column >= low) & (column < low + block) & (slot < live))
                scores = (
                    lax.dot_general(
                        query, keys, (((1,), (1,)), ((), ())), preferred_element_type=jnp.float32
                    )
                    * scale
                )
                scores = jnp.where(active, scores, -jnp.inf)
                highest = jnp.max(scores, axis=1, keepdims=True)
                weights = jnp.exp(scores - highest)
                totals = jnp.sum(weights, axis=1, keepdims=True)
                mixed = jnp.dot(
                    weights.astype(jnp.bfloat16), values, preferred_element_type=jnp.float32
                )
                o_refs[step][rows, cols] = (mixed / totals).astype(o_refs[step].dtype)


def attend_pieces(pieces, lists, live, me):
    _, tokens, width = pieces[0].shape
    head_total, qblocks = live.shape
    slots = lists.shape[2]
    depth = width // head_total
    block = len(pieces) * tokens // qblocks
    kernel = functools.partial(
        attend_pieces_kernel,
        block=block,
        slots=slots,
        qblocks=qblocks,
        heads=head_total,
        depth=depth,
    )
    smem = pltpu.SMEM
    return pl.pallas_call(
        kernel,
        in_specs=[pl.BlockSpec(memory_space=smem)] * 3
        + [pl.BlockSpec(memory_space=pltpu.VMEM)] * len(pieces),
        out_specs=[pl.BlockSpec(memory_space=pltpu.VMEM)] * len(pieces),
        out_shape=[jax.ShapeDtypeStruct((tokens, width), jnp.bfloat16)] * len(pieces),
    )(lists.reshape(-1), live.reshape(-1), me.reshape(1), *pieces)


def place_kernel(*refs, seq, stride, offsets, me):
    out_ref = refs[-1]
    for c, offset in enumerate(offsets):
        for step in range(seq):
            piece = refs[c * seq + step]
            width = piece.shape[1]
            low = ((me + step) % seq) * stride + offset
            out_ref[0, :, low:low + width] = piece[...]


def placed_back(backs, own_index, seq, stride, offsets):
    tokens = backs[0].shape[0]

    def branch(me, *pieces):
        kernel = functools.partial(
            place_kernel, seq=seq, stride=stride, offsets=tuple(offsets), me=me
        )
        return pl.pallas_call(
            kernel,
            in_specs=[pl.BlockSpec(memory_space=pltpu.VMEM)] * len(pieces),
            out_specs=pl.BlockSpec(memory_space=pltpu.VMEM),
            out_shape=jax.ShapeDtypeStruct((1, tokens, seq * stride), pieces[0].dtype),
        )(*pieces)

    branches = [functools.partial(branch, me) for me in range(seq)]
    return lax.switch(own_index, branches, *backs)


def local_body(
    query_rows,
    key_rows,
    value_rows,
    hidden_state,
    modulation,
    head_weight,
    latents,
    time_index,
    live_counts,
    block_lists,
):
    seq_count = lax.axis_size("seq")
    own_index = lax.axis_index("seq")
    head_count = live_counts.shape[0]
    per_device = head_count // seq_count
    if per_device % 4 == 0:
        sizes = [per_device * 3 // 4, per_device // 4]
    else:
        sizes = [per_device]
    starts = [sum(sizes[:c]) for c in range(len(sizes))]
    width = query_rows.shape[2]
    depth = width // head_count
    permuted = seq_count <= 8

    backs = []
    previous = None
    pending = None

    def send_back(outs):
        backs.append(outs[0])
        for step in range(1, seq_count):
            backs.append(passed_along(outs[step], "seq", -step))

    for per_chunk, start in zip(sizes, starts):
        chunk_width = per_chunk * depth
        first = own_index * per_device + start
        lists = lax.dynamic_slice_in_dim(block_lists, first, per_chunk, 0)
        live = lax.dynamic_slice_in_dim(live_counts, first, per_chunk, 0)
        if permuted:
            pieces = pieces_of(
                query_rows,
                key_rows,
                value_rows,
                own_index,
                seq_count,
                per_device * depth,
                start * depth,
                chunk_width,
            )
            if previous is not None:
                pieces, _ = lax.optimization_barrier((pieces, previous))
            received = [pieces[0]]
            for step in range(1, seq_count):
                received.append(passed_along(pieces[step], "seq", step))
            if pending is not None:
                held, _ = lax.optimization_barrier((pending, received))
                send_back(held)
                pending = attend_pieces(received, lists, live, own_index.astype(jnp.int32))
            else:
                pending = attend_pieces(received, lists, live, own_index.astype(jnp.int32))
            previous = received
            continue
        send = packed_chunk(
            query_rows, key_rows, value_rows, seq_count, per_device * depth, start * depth, chunk_width
        )
        if previous is not None:
            send, _ = lax.optimization_barrier((send, previous))
        packed = lax.all_to_all(send, "seq", 0, 0, tiled=True)
        previous = packed
        attended = attend_heads(packed, lists, live, jnp.zeros((), jnp.int32), False)
        backs.append(lax.all_to_all(attended, "seq", 0, 0, tiled=True))
    if pending is not None:
        send_back(pending)
    offsets = [s * depth for s in starts]
    if permuted:
        mixed_back = placed_back(backs, own_index, seq_count, per_device * depth, offsets)
    else:
        mixed_back = unpacked(backs, seq_count, per_device * depth, offsets)

    source = hidden_state[0].astype(jnp.float32)
    mean_row = jnp.mean(source, axis=1, keepdims=True)
    centred = source - mean_row
    spread = jnp.mean(centred * centred, axis=1, keepdims=True)
    normed = centred * lax.rsqrt(spread + epsilon)
    shaped = (normed * (1.0 + modulation[0, 1]) + modulation[0, 0]).astype(jnp.bfloat16)
    velocity = jnp.dot(shaped, head_weight, preferred_element_type=jnp.float32)
    change = noise_level(time_index[0] - 1) - noise_level(time_index[0])
    moved = latents[0] + change * velocity
    queue_next = passed_along(moved[None], "queue", -1)
    return (mixed_back, queue_next)


def solution(mesh):
    placed = (
        P(("groups", "queue"), "seq", None),
        P(("groups", "queue"), "seq", None),
        P(("groups", "queue"), "seq", None),
        P(("groups", "queue"), "seq", None),
        P(("groups", "queue"), None, None),
        P(),
        P(("groups", "queue"), "seq", None),
        P(("groups", "queue")),
        P(),
        P(),
    )
    return jax.shard_map(
        local_body,
        mesh=mesh,
        in_specs=placed,
        out_specs=(P(("groups", "queue"), "seq", None), P(("groups", "queue"), "seq", None)),
        check_vma=False,
    )
```

```python
import functools

import jax
import jax.numpy as jnp
from jax import lax
from jax.experimental import pallas as pl
from jax.experimental.pallas import tpu as pltpu
from jax.sharding import PartitionSpec as P

STEPS = 8


epsilon = 1e-06
plan_shift = 5.0


def passed_along(value, axis, steps):
    count = lax.axis_size(axis)
    pairs = [(source, (source + steps) % count) for source in range(count)]
    return lax.ppermute(value, axis, pairs)


def noise_level(step_value):
    fraction = step_value.astype(jnp.float32) / STEPS
    return plan_shift * fraction / (1.0 + (plan_shift - 1.0) * fraction)


def attend_kernel(
    lists_ref, live_ref, me_ref, x_ref, o_ref, *, block, slots, qblocks, heads, depth, shifted
):
    sources, _, tokens, _ = x_ref.shape
    me = me_ref[0]

    def slot_of(device):
        if shifted:
            return (me - device + sources) % sources
        return device

    total = sources * tokens
    scale = depth ** (-0.5)
    column = lax.broadcasted_iota(jnp.int32, (1, total), 1)
    per_source = tokens // block
    for head in range(heads):
        cols = slice(head * depth, (head + 1) * depth)
        keys = x_ref[:, 1, :, cols].reshape(total, depth)
        values = x_ref[:, 2, :, cols].reshape(total, depth)

        def body(qblock, carry):
            source = slot_of(qblock // per_source)
            first = pl.multiple_of((qblock % per_source) * block, block)
            query = x_ref[source, 0, pl.ds(first, block), cols]
            scores = (
                lax.dot_general(
                    query, keys, (((1,), (1,)), ((), ())), preferred_element_type=jnp.float32
                )
                * scale
            )
            live = live_ref[head * qblocks + qblock]
            active = column < 0
            for slot in range(slots):
                chosen = lists_ref[(head * qblocks + qblock) * slots + slot]
                place = slot_of(chosen // per_source)
                low = place * tokens + (chosen % per_source) * block
                active = active | ((column >= low) & (column < low + block) & (slot < live))
            scores = jnp.where(active, scores, -jnp.inf)
            highest = jnp.max(scores, axis=1, keepdims=True)
            weights = jnp.exp(scores - highest)
            totals = jnp.sum(weights, axis=1, keepdims=True)
            mixed = jnp.dot(
                weights.astype(jnp.bfloat16), values, preferred_element_type=jnp.float32
            )
            o_ref[source, pl.ds(first, block), cols] = (mixed / totals).astype(o_ref.dtype)
            return carry

        lax.fori_loop(0, qblocks, body, 0)


def attend_heads(packed, lists, live, me, shifted):
    sources, _, tokens, width = packed.shape
    head_total, qblocks = live.shape
    slots = lists.shape[2]
    depth = width // head_total
    block = sources * tokens // qblocks
    kernel = functools.partial(
        attend_kernel,
        block=block,
        slots=slots,
        qblocks=qblocks,
        heads=head_total,
        depth=depth,
        shifted=shifted,
    )
    smem = pltpu.SMEM
    return pl.pallas_call(
        kernel,
        in_specs=[
            pl.BlockSpec(memory_space=smem),
            pl.BlockSpec(memory_space=smem),
            pl.BlockSpec(memory_space=smem),
            pl.BlockSpec(memory_space=pltpu.VMEM),
        ],
        out_specs=pl.BlockSpec(memory_space=pltpu.VMEM),
        out_shape=jax.ShapeDtypeStruct((sources, tokens, width), jnp.bfloat16),
    )(lists.reshape(-1), live.reshape(-1), me.reshape(1), packed)


def pack_kernel(query_ref, key_ref, value_ref, out_ref, *, seq, stride, offset, width):
    for group in range(seq):
        cols = slice(group * stride + offset, group * stride + offset + width)
        for kind, source in enumerate((query_ref, key_ref, value_ref)):
            out_ref[group, kind] = source[0, :, cols]


def packed_chunk(query_rows, key_rows, value_rows, seq, stride, offset, width):
    tokens = query_rows.shape[1]
    kernel = functools.partial(pack_kernel, seq=seq, stride=stride, offset=offset, width=width)
    return pl.pallas_call(
        kernel,
        in_specs=[pl.BlockSpec(memory_space=pltpu.VMEM)] * 3,
        out_specs=pl.BlockSpec(memory_space=pltpu.VMEM),
        out_shape=jax.ShapeDtypeStruct((seq, 3, tokens, width), query_rows.dtype),
    )(query_rows, key_rows, value_rows)


def unpack_kernel(*refs, seq, stride, offsets):
    chunks = len(refs) - 1
    out_ref = refs[chunks]
    for c in range(chunks):
        width = refs[c].shape[2]
        for group in range(seq):
            low = group * stride + offsets[c]
            out_ref[0, :, low:low + width] = refs[c][group]


def unpacked(backs, seq, stride, offsets):
    tokens = backs[0].shape[1]
    kernel = functools.partial(unpack_kernel, seq=seq, stride=stride, offsets=tuple(offsets))
    return pl.pallas_call(
        kernel,
        in_specs=[pl.BlockSpec(memory_space=pltpu.VMEM)] * len(backs),
        out_specs=pl.BlockSpec(memory_space=pltpu.VMEM),
        out_shape=jax.ShapeDtypeStruct((1, tokens, seq * stride), backs[0].dtype),
    )(*backs)


def pieces_kernel(*refs, seq, stride, offset, width, me):
    sources, outs = refs[:3], refs[3:]
    for step in range(seq):
        low = ((me + step) % seq) * stride + offset
        for kind, source in enumerate(sources):
            outs[step][kind] = source[0, :, low:low + width]


def pieces_of(query_rows, key_rows, value_rows, own_index, seq, stride, offset, width):
    tokens = query_rows.shape[1]

    def branch(me, *rows):
        kernel = functools.partial(
            pieces_kernel, seq=seq, stride=stride, offset=offset, width=width, me=me
        )
        return tuple(
            pl.pallas_call(
                kernel,
                in_specs=[pl.BlockSpec(memory_space=pltpu.VMEM)] * 3,
                out_specs=[pl.BlockSpec(memory_space=pltpu.VMEM)] * seq,
                out_shape=[jax.ShapeDtypeStruct((3, tokens, width), query_rows.dtype)] * seq,
            )(*rows)
        )

    branches = [functools.partial(branch, me) for me in range(seq)]
    return lax.switch(own_index, branches, query_rows, key_rows, value_rows)


def attend_pieces_kernel(lists_ref, live_ref, me_ref, *refs, block, slots, qblocks, heads, depth):
    sources = len(refs) // 2
    x_refs, o_refs = refs[:sources], refs[sources:]
    tokens = x_refs[0].shape[1]
    total = sources * tokens
    me = me_ref[0]
    scale = depth ** (-0.5)
    per_source = tokens // block
    column = lax.broadcasted_iota(jnp.int32, (1, total), 1)
    for head in range(heads):
        cols = slice(head * depth, (head + 1) * depth)
        keys = jnp.concatenate([ref[1, :, cols] for ref in x_refs], axis=0)
        values = jnp.concatenate([ref[2, :, cols] for ref in x_refs], axis=0)
        for step in range(sources):
            device = (me - step + sources) % sources
            for sub in range(per_source):
                rows = slice(sub * block, (sub + 1) * block)
                query = x_refs[step][0, rows, cols]
                entry = head * qblocks + device * per_source + sub
                live = live_ref[entry]
                active = column < 0
                for slot in range(slots):
                    chosen = lists_ref[entry * slots + slot]
                    place = (me - chosen // per_source + sources) % sources
                    low = place * tokens + (chosen % per_source) * block
                    active = active | ((column >= low) & (column < low + block) & (slot < live))
                scores = (
                    lax.dot_general(
                        query, keys, (((1,), (1,)), ((), ())), preferred_element_type=jnp.float32
                    )
                    * scale
                )
                scores = jnp.where(active, scores, -jnp.inf)
                highest = jnp.max(scores, axis=1, keepdims=True)
                weights = jnp.exp(scores - highest)
                totals = jnp.sum(weights, axis=1, keepdims=True)
                mixed = jnp.dot(
                    weights.astype(jnp.bfloat16), values, preferred_element_type=jnp.float32
                )
                o_refs[step][rows, cols] = (mixed / totals).astype(o_refs[step].dtype)


def attend_pieces(pieces, lists, live, me):
    _, tokens, width = pieces[0].shape
    head_total, qblocks = live.shape
    slots = lists.shape[2]
    depth = width // head_total
    block = len(pieces) * tokens // qblocks
    kernel = functools.partial(
        attend_pieces_kernel,
        block=block,
        slots=slots,
        qblocks=qblocks,
        heads=head_total,
        depth=depth,
    )
    smem = pltpu.SMEM
    return pl.pallas_call(
        kernel,
        in_specs=[pl.BlockSpec(memory_space=smem)] * 3
        + [pl.BlockSpec(memory_space=pltpu.VMEM)] * len(pieces),
        out_specs=[pl.BlockSpec(memory_space=pltpu.VMEM)] * len(pieces),
        out_shape=[jax.ShapeDtypeStruct((tokens, width), jnp.bfloat16)] * len(pieces),
    )(lists.reshape(-1), live.reshape(-1), me.reshape(1), *pieces)


def place_kernel(*refs, seq, stride, offsets, me):
    out_ref = refs[-1]
    for c, offset in enumerate(offsets):
        for step in range(seq):
            piece = refs[c * seq + step]
            width = piece.shape[1]
            low = ((me + step) % seq) * stride + offset
            out_ref[0, :, low:low + width] = piece[...]


def placed_back(backs, own_index, seq, stride, offsets):
    tokens = backs[0].shape[0]

    def branch(me, *pieces):
        kernel = functools.partial(
            place_kernel, seq=seq, stride=stride, offsets=tuple(offsets), me=me
        )
        return pl.pallas_call(
            kernel,
            in_specs=[pl.BlockSpec(memory_space=pltpu.VMEM)] * len(pieces),
            out_specs=pl.BlockSpec(memory_space=pltpu.VMEM),
            out_shape=jax.ShapeDtypeStruct((1, tokens, seq * stride), pieces[0].dtype),
        )(*pieces)

    branches = [functools.partial(branch, me) for me in range(seq)]
    return lax.switch(own_index, branches, *backs)


def local(
    query_rows,
    key_rows,
    value_rows,
    hidden_state,
    modulation,
    head_weight,
    latents,
    time_index,
    live_counts,
    block_lists,
):
    seq_count = lax.axis_size("seq")
    own_index = lax.axis_index("seq")
    head_count = live_counts.shape[0]
    per_device = head_count // seq_count
    if per_device % 8 == 0:
        sizes = [per_device * 5 // 8, per_device * 3 // 8]
    elif per_device % 4 == 0:
        sizes = [per_device * 3 // 4, per_device // 4]
    else:
        sizes = [per_device]
    starts = [sum(sizes[:c]) for c in range(len(sizes))]
    tokens = query_rows.shape[1]
    width = query_rows.shape[2]
    depth = width // head_count
    permuted = seq_count <= 8

    backs = []
    previous = None
    for per_chunk, start in zip(sizes, starts):
        chunk_width = per_chunk * depth
        first = own_index * per_device + start
        lists = lax.dynamic_slice_in_dim(block_lists, first, per_chunk, 0)
        live = lax.dynamic_slice_in_dim(live_counts, first, per_chunk, 0)
        if permuted:
            pieces = pieces_of(
                query_rows,
                key_rows,
                value_rows,
                own_index,
                seq_count,
                per_device * depth,
                start * depth,
                chunk_width,
            )
            if previous is not None:
                pieces, _ = lax.optimization_barrier((pieces, previous))
            received = [pieces[0]]
            for step in range(1, seq_count):
                received.append(passed_along(pieces[step], "seq", step))
            previous = received
            outs = attend_pieces(received, lists, live, own_index.astype(jnp.int32))
            backs.append(outs[0])
            for step in range(1, seq_count):
                backs.append(passed_along(outs[step], "seq", -step))
            continue
        send = packed_chunk(
            query_rows, key_rows, value_rows, seq_count, per_device * depth, start * depth, chunk_width
        )
        if previous is not None:
            send, _ = lax.optimization_barrier((send, previous))
        packed = lax.all_to_all(send, "seq", 0, 0, tiled=True)
        previous = packed
        attended = attend_heads(packed, lists, live, jnp.zeros((), jnp.int32), False)
        backs.append(lax.all_to_all(attended, "seq", 0, 0, tiled=True))
    offsets = [s * depth for s in starts]
    if permuted:
        mixed_back = placed_back(backs, own_index, seq_count, per_device * depth, offsets)
    else:
        mixed_back = unpacked(backs, seq_count, per_device * depth, offsets)

    source = hidden_state[0].astype(jnp.float32)
    mean_row = jnp.mean(source, axis=1, keepdims=True)
    centred = source - mean_row
    spread = jnp.mean(centred * centred, axis=1, keepdims=True)
    normed = centred * lax.rsqrt(spread + epsilon)
    shaped = (normed * (1.0 + modulation[0, 1]) + modulation[0, 0]).astype(jnp.bfloat16)
    velocity = jnp.dot(shaped, head_weight, preferred_element_type=jnp.float32)
    change = noise_level(time_index[0] - 1) - noise_level(time_index[0])
    moved = latents[0] + change * velocity
    queue_next = passed_along(moved[None], "queue", -1)
    return (mixed_back, queue_next)


def solution(mesh):
    placed = (
        P(("groups", "queue"), "seq", None),
        P(("groups", "queue"), "seq", None),
        P(("groups", "queue"), "seq", None),
        P(("groups", "queue"), "seq", None),
        P(("groups", "queue"), None, None),
        P(),
        P(("groups", "queue"), "seq", None),
        P(("groups", "queue")),
        P(),
        P(),
    )
    return jax.shard_map(
        local,
        mesh=mesh,
        in_specs=placed,
        out_specs=(P(("groups", "queue"), "seq", None), P(("groups", "queue"), "seq", None)),
        check_vma=False,
    )
```

```python
import functools

import jax
import jax.numpy as jnp
from jax import lax
from jax.experimental import pallas as pl
from jax.experimental.pallas import tpu as pltpu
from jax.sharding import PartitionSpec as P

STEPS = 8


epsilon = 1e-06
plan_shift = 5.0


def passed_along(value, axis, steps):
    count = lax.axis_size(axis)
    pairs = [(source, (source + steps) % count) for source in range(count)]
    return lax.ppermute(value, axis, pairs)


def noise_level(step_value):
    fraction = step_value.astype(jnp.float32) / STEPS
    return plan_shift * fraction / (1.0 + (plan_shift - 1.0) * fraction)


def attend_kernel(
    lists_ref, live_ref, me_ref, x_ref, o_ref, *, block, slots, qblocks, heads, depth, shifted
):
    sources, _, tokens, _ = x_ref.shape
    me = me_ref[0]

    def slot_of(device):
        if shifted:
            return (me - device + sources) % sources
        return device

    total = sources * tokens
    scale = depth ** (-0.5)
    column = lax.broadcasted_iota(jnp.int32, (1, total), 1)
    per_source = tokens // block
    for head in range(heads):
        cols = slice(head * depth, (head + 1) * depth)
        keys = x_ref[:, 1, :, cols].reshape(total, depth)
        values = x_ref[:, 2, :, cols].reshape(total, depth)

        def body(qblock, carry):
            source = slot_of(qblock // per_source)
            first = pl.multiple_of((qblock % per_source) * block, block)
            query = x_ref[source, 0, pl.ds(first, block), cols]
            scores = (
                lax.dot_general(
                    query, keys, (((1,), (1,)), ((), ())), preferred_element_type=jnp.float32
                )
                * scale
            )
            live = live_ref[head * qblocks + qblock]
            active = column < 0
            for slot in range(slots):
                chosen = lists_ref[(head * qblocks + qblock) * slots + slot]
                place = slot_of(chosen // per_source)
                low = place * tokens + (chosen % per_source) * block
                active = active | ((column >= low) & (column < low + block) & (slot < live))
            scores = jnp.where(active, scores, -jnp.inf)
            highest = jnp.max(scores, axis=1, keepdims=True)
            weights = jnp.exp(scores - highest)
            totals = jnp.sum(weights, axis=1, keepdims=True)
            mixed = jnp.dot(
                weights.astype(jnp.bfloat16), values, preferred_element_type=jnp.float32
            )
            o_ref[source, pl.ds(first, block), cols] = (mixed / totals).astype(o_ref.dtype)
            return carry

        lax.fori_loop(0, qblocks, body, 0)


def attend_heads(packed, lists, live, me, shifted):
    sources, _, tokens, width = packed.shape
    head_total, qblocks = live.shape
    slots = lists.shape[2]
    depth = width // head_total
    block = sources * tokens // qblocks
    kernel = functools.partial(
        attend_kernel,
        block=block,
        slots=slots,
        qblocks=qblocks,
        heads=head_total,
        depth=depth,
        shifted=shifted,
    )
    smem = pltpu.SMEM
    return pl.pallas_call(
        kernel,
        in_specs=[
            pl.BlockSpec(memory_space=smem),
            pl.BlockSpec(memory_space=smem),
            pl.BlockSpec(memory_space=smem),
            pl.BlockSpec(memory_space=pltpu.VMEM),
        ],
        out_specs=pl.BlockSpec(memory_space=pltpu.VMEM),
        out_shape=jax.ShapeDtypeStruct((sources, tokens, width), jnp.bfloat16),
    )(lists.reshape(-1), live.reshape(-1), me.reshape(1), packed)


def pack_kernel(query_ref, key_ref, value_ref, out_ref, *, seq, stride, offset, width):
    for group in range(seq):
        cols = slice(group * stride + offset, group * stride + offset + width)
        for kind, source in enumerate((query_ref, key_ref, value_ref)):
            out_ref[group, kind] = source[0, :, cols]


def packed_chunk(query_rows, key_rows, value_rows, seq, stride, offset, width):
    tokens = query_rows.shape[1]
    kernel = functools.partial(pack_kernel, seq=seq, stride=stride, offset=offset, width=width)
    return pl.pallas_call(
        kernel,
        in_specs=[pl.BlockSpec(memory_space=pltpu.VMEM)] * 3,
        out_specs=pl.BlockSpec(memory_space=pltpu.VMEM),
        out_shape=jax.ShapeDtypeStruct((seq, 3, tokens, width), query_rows.dtype),
    )(query_rows, key_rows, value_rows)


def unpack_kernel(*refs, seq, stride, offsets):
    chunks = len(refs) - 1
    out_ref = refs[chunks]
    for c in range(chunks):
        width = refs[c].shape[2]
        for group in range(seq):
            low = group * stride + offsets[c]
            out_ref[0, :, low:low + width] = refs[c][group]


def unpacked(backs, seq, stride, offsets):
    tokens = backs[0].shape[1]
    kernel = functools.partial(unpack_kernel, seq=seq, stride=stride, offsets=tuple(offsets))
    return pl.pallas_call(
        kernel,
        in_specs=[pl.BlockSpec(memory_space=pltpu.VMEM)] * len(backs),
        out_specs=pl.BlockSpec(memory_space=pltpu.VMEM),
        out_shape=jax.ShapeDtypeStruct((1, tokens, seq * stride), backs[0].dtype),
    )(*backs)


def pieces_kernel(*refs, seq, stride, offset, width, me):
    sources, outs = refs[:3], refs[3:]
    for step in range(seq):
        low = ((me + step) % seq) * stride + offset
        for kind, source in enumerate(sources):
            outs[step][kind] = source[0, :, low:low + width]


def pieces_of(query_rows, key_rows, value_rows, own_index, seq, stride, offset, width):
    tokens = query_rows.shape[1]

    def branch(me, *rows):
        kernel = functools.partial(
            pieces_kernel, seq=seq, stride=stride, offset=offset, width=width, me=me
        )
        return tuple(
            pl.pallas_call(
                kernel,
                in_specs=[pl.BlockSpec(memory_space=pltpu.VMEM)] * 3,
                out_specs=[pl.BlockSpec(memory_space=pltpu.VMEM)] * seq,
                out_shape=[jax.ShapeDtypeStruct((3, tokens, width), query_rows.dtype)] * seq,
            )(*rows)
        )

    branches = [functools.partial(branch, me) for me in range(seq)]
    return lax.switch(own_index, branches, query_rows, key_rows, value_rows)


def attend_pieces_kernel(
    lists_ref, live_ref, me_ref, *refs, block, slots, qblocks, heads, depth, steps
):
    sources = len(refs) - len(steps)
    x_refs, outs = refs[:sources], refs[sources:]
    o_refs = dict(zip(steps, outs))
    tokens = x_refs[0].shape[1]
    total = sources * tokens
    me = me_ref[0]
    scale = depth ** (-0.5)
    per_source = tokens // block
    column = lax.broadcasted_iota(jnp.int32, (1, total), 1)
    for head in range(heads):
        cols = slice(head * depth, (head + 1) * depth)
        keys = jnp.concatenate([ref[1, :, cols] for ref in x_refs], axis=0)
        values = jnp.concatenate([ref[2, :, cols] for ref in x_refs], axis=0)
        for step in steps:
            device = (me - step + sources) % sources
            for sub in range(per_source):
                rows = slice(sub * block, (sub + 1) * block)
                query = x_refs[step][0, rows, cols]
                entry = head * qblocks + device * per_source + sub
                live = live_ref[entry]
                active = column < 0
                for slot in range(slots):
                    chosen = lists_ref[entry * slots + slot]
                    place = (me - chosen // per_source + sources) % sources
                    low = place * tokens + (chosen % per_source) * block
                    active = active | ((column >= low) & (column < low + block) & (slot < live))
                scores = (
                    lax.dot_general(
                        query, keys, (((1,), (1,)), ((), ())), preferred_element_type=jnp.float32
                    )
                    * scale
                )
                scores = jnp.where(active, scores, -jnp.inf)
                highest = jnp.max(scores, axis=1, keepdims=True)
                weights = jnp.exp(scores - highest)
                totals = jnp.sum(weights, axis=1, keepdims=True)
                mixed = jnp.dot(
                    weights.astype(jnp.bfloat16), values, preferred_element_type=jnp.float32
                )
                o_refs[step][rows, cols] = (mixed / totals).astype(o_refs[step].dtype)


def attend_pieces(pieces, lists, live, me, steps=None):
    steps = tuple(range(len(pieces))) if steps is None else tuple(steps)
    _, tokens, width = pieces[0].shape
    head_total, qblocks = live.shape
    slots = lists.shape[2]
    depth = width // head_total
    block = len(pieces) * tokens // qblocks
    kernel = functools.partial(
        attend_pieces_kernel,
        block=block,
        slots=slots,
        qblocks=qblocks,
        heads=head_total,
        depth=depth,
        steps=steps,
    )
    smem = pltpu.SMEM
    return pl.pallas_call(
        kernel,
        in_specs=[pl.BlockSpec(memory_space=smem)] * 3
        + [pl.BlockSpec(memory_space=pltpu.VMEM)] * len(pieces),
        out_specs=[pl.BlockSpec(memory_space=pltpu.VMEM)] * len(steps),
        out_shape=[jax.ShapeDtypeStruct((tokens, width), jnp.bfloat16)] * len(steps),
    )(lists.reshape(-1), live.reshape(-1), me.reshape(1), *pieces)


def place_kernel(*refs, seq, stride, offsets, me):
    out_ref = refs[-1]
    for c, offset in enumerate(offsets):
        for step in range(seq):
            piece = refs[c * seq + step]
            width = piece.shape[1]
            low = ((me + step) % seq) * stride + offset
            out_ref[0, :, low:low + width] = piece[...]


def placed_back(backs, own_index, seq, stride, offsets):
    tokens = backs[0].shape[0]

    def branch(me, *pieces):
        kernel = functools.partial(
            place_kernel, seq=seq, stride=stride, offsets=tuple(offsets), me=me
        )
        return pl.pallas_call(
            kernel,
            in_specs=[pl.BlockSpec(memory_space=pltpu.VMEM)] * len(pieces),
            out_specs=pl.BlockSpec(memory_space=pltpu.VMEM),
            out_shape=jax.ShapeDtypeStruct((1, tokens, seq * stride), pieces[0].dtype),
        )(*pieces)

    branches = [functools.partial(branch, me) for me in range(seq)]
    return lax.switch(own_index, branches, *backs)


def local(
    query_rows,
    key_rows,
    value_rows,
    hidden_state,
    modulation,
    head_weight,
    latents,
    time_index,
    live_counts,
    block_lists,
):
    seq_count = lax.axis_size("seq")
    own_index = lax.axis_index("seq")
    head_count = live_counts.shape[0]
    per_device = head_count // seq_count
    if per_device % 4 == 0:
        sizes = [per_device * 3 // 4, per_device // 4]
    else:
        sizes = [per_device]
    starts = [sum(sizes[:c]) for c in range(len(sizes))]
    tokens = query_rows.shape[1]
    width = query_rows.shape[2]
    depth = width // head_count
    permuted = seq_count <= 8

    backs = []
    previous = None
    for per_chunk, start in zip(sizes, starts):
        chunk_width = per_chunk * depth
        first = own_index * per_device + start
        lists = lax.dynamic_slice_in_dim(block_lists, first, per_chunk, 0)
        live = lax.dynamic_slice_in_dim(live_counts, first, per_chunk, 0)
        if permuted:
            pieces = pieces_of(
                query_rows,
                key_rows,
                value_rows,
                own_index,
                seq_count,
                per_device * depth,
                start * depth,
                chunk_width,
            )
            if previous is not None:
                pieces, _ = lax.optimization_barrier((pieces, previous))
            received = [pieces[0]]
            for step in range(1, seq_count):
                received.append(passed_along(pieces[step], "seq", step))
            previous = received
            if start + per_chunk < per_device:
                outs = attend_pieces(received, lists, live, own_index.astype(jnp.int32))
                backs.append(outs[0])
                for step in range(1, seq_count):
                    backs.append(passed_along(outs[step], "seq", -step))
                continue
            returned = {}
            for step in list(range(1, seq_count)) + [0]:
                (piece,) = attend_pieces(
                    received, lists, live, own_index.astype(jnp.int32), steps=(step,)
                )
                returned[step] = passed_along(piece, "seq", -step) if step else piece
            backs.extend(returned[step] for step in range(seq_count))
            continue
        send = packed_chunk(
            query_rows, key_rows, value_rows, seq_count, per_device * depth, start * depth, chunk_width
        )
        if previous is not None:
            send, _ = lax.optimization_barrier((send, previous))
        packed = lax.all_to_all(send, "seq", 0, 0, tiled=True)
        previous = packed
        attended = attend_heads(packed, lists, live, jnp.zeros((), jnp.int32), False)
        backs.append(lax.all_to_all(attended, "seq", 0, 0, tiled=True))
    offsets = [s * depth for s in starts]
    if permuted:
        mixed_back = placed_back(backs, own_index, seq_count, per_device * depth, offsets)
    else:
        mixed_back = unpacked(backs, seq_count, per_device * depth, offsets)

    source = hidden_state[0].astype(jnp.float32)
    mean_row = jnp.mean(source, axis=1, keepdims=True)
    centred = source - mean_row
    spread = jnp.mean(centred * centred, axis=1, keepdims=True)
    normed = centred * lax.rsqrt(spread + epsilon)
    shaped = (normed * (1.0 + modulation[0, 1]) + modulation[0, 0]).astype(jnp.bfloat16)
    velocity = jnp.dot(shaped, head_weight, preferred_element_type=jnp.float32)
    change = noise_level(time_index[0] - 1) - noise_level(time_index[0])
    moved = latents[0] + change * velocity
    queue_next = passed_along(moved[None], "queue", -1)
    return (mixed_back, queue_next)


def solution(mesh):
    placed = (
        P(("groups", "queue"), "seq", None),
        P(("groups", "queue"), "seq", None),
        P(("groups", "queue"), "seq", None),
        P(("groups", "queue"), "seq", None),
        P(("groups", "queue"), None, None),
        P(),
        P(("groups", "queue"), "seq", None),
        P(("groups", "queue")),
        P(),
        P(),
    )
    return jax.shard_map(
        local,
        mesh=mesh,
        in_specs=placed,
        out_specs=(P(("groups", "queue"), "seq", None), P(("groups", "queue"), "seq", None)),
        check_vma=False,
    )
```

```python
import functools

import jax
import jax.numpy as jnp
from jax import lax
from jax.experimental import pallas as pl
from jax.experimental.pallas import tpu as pltpu
from jax.sharding import PartitionSpec as P

STEPS = 8


epsilon = 1e-06
plan_shift = 5.0


def passed_along(value, axis, steps):
    count = lax.axis_size(axis)
    pairs = [(source, (source + steps) % count) for source in range(count)]
    return lax.ppermute(value, axis, pairs)


def noise_level(step_value):
    fraction = step_value.astype(jnp.float32) / STEPS
    return plan_shift * fraction / (1.0 + (plan_shift - 1.0) * fraction)


def attend_kernel(
    lists_ref, live_ref, me_ref, x_ref, o_ref, *, block, slots, qblocks, heads, depth, shifted
):
    sources, _, tokens, _ = x_ref.shape
    me = me_ref[0]

    def slot_of(device):
        if shifted:
            return (me - device + sources) % sources
        return device

    total = sources * tokens
    scale = depth ** (-0.5)
    column = lax.broadcasted_iota(jnp.int32, (1, total), 1)
    per_source = tokens // block
    for head in range(heads):
        cols = slice(head * depth, (head + 1) * depth)
        keys = x_ref[:, 1, :, cols].reshape(total, depth)
        values = x_ref[:, 2, :, cols].reshape(total, depth)

        def body(qblock, carry):
            source = slot_of(qblock // per_source)
            first = pl.multiple_of((qblock % per_source) * block, block)
            query = x_ref[source, 0, pl.ds(first, block), cols]
            scores = (
                lax.dot_general(
                    query, keys, (((1,), (1,)), ((), ())), preferred_element_type=jnp.float32
                )
                * scale
            )
            live = live_ref[head * qblocks + qblock]
            active = column < 0
            for slot in range(slots):
                chosen = lists_ref[(head * qblocks + qblock) * slots + slot]
                place = slot_of(chosen // per_source)
                low = place * tokens + (chosen % per_source) * block
                active = active | ((column >= low) & (column < low + block) & (slot < live))
            scores = jnp.where(active, scores, -jnp.inf)
            highest = jnp.max(scores, axis=1, keepdims=True)
            weights = jnp.exp(scores - highest)
            totals = jnp.sum(weights, axis=1, keepdims=True)
            mixed = jnp.dot(
                weights.astype(jnp.bfloat16), values, preferred_element_type=jnp.float32
            )
            o_ref[source, pl.ds(first, block), cols] = (mixed / totals).astype(o_ref.dtype)
            return carry

        lax.fori_loop(0, qblocks, body, 0)


def attend_heads(packed, lists, live, me, shifted):
    sources, _, tokens, width = packed.shape
    head_total, qblocks = live.shape
    slots = lists.shape[2]
    depth = width // head_total
    block = sources * tokens // qblocks
    kernel = functools.partial(
        attend_kernel,
        block=block,
        slots=slots,
        qblocks=qblocks,
        heads=head_total,
        depth=depth,
        shifted=shifted,
    )
    smem = pltpu.SMEM
    return pl.pallas_call(
        kernel,
        in_specs=[
            pl.BlockSpec(memory_space=smem),
            pl.BlockSpec(memory_space=smem),
            pl.BlockSpec(memory_space=smem),
            pl.BlockSpec(memory_space=pltpu.VMEM),
        ],
        out_specs=pl.BlockSpec(memory_space=pltpu.VMEM),
        out_shape=jax.ShapeDtypeStruct((sources, tokens, width), jnp.bfloat16),
    )(lists.reshape(-1), live.reshape(-1), me.reshape(1), packed)


def pack_kernel(query_ref, key_ref, value_ref, out_ref, *, seq, stride, offset, width):
    for group in range(seq):
        cols = slice(group * stride + offset, group * stride + offset + width)
        for kind, source in enumerate((query_ref, key_ref, value_ref)):
            out_ref[group, kind] = source[0, :, cols]


def packed_chunk(query_rows, key_rows, value_rows, seq, stride, offset, width):
    tokens = query_rows.shape[1]
    kernel = functools.partial(pack_kernel, seq=seq, stride=stride, offset=offset, width=width)
    return pl.pallas_call(
        kernel,
        in_specs=[pl.BlockSpec(memory_space=pltpu.VMEM)] * 3,
        out_specs=pl.BlockSpec(memory_space=pltpu.VMEM),
        out_shape=jax.ShapeDtypeStruct((seq, 3, tokens, width), query_rows.dtype),
    )(query_rows, key_rows, value_rows)


def unpack_kernel(*refs, seq, stride, offsets):
    chunks = len(refs) - 1
    out_ref = refs[chunks]
    for c in range(chunks):
        width = refs[c].shape[2]
        for group in range(seq):
            low = group * stride + offsets[c]
            out_ref[0, :, low:low + width] = refs[c][group]


def unpacked(backs, seq, stride, offsets):
    tokens = backs[0].shape[1]
    kernel = functools.partial(unpack_kernel, seq=seq, stride=stride, offsets=tuple(offsets))
    return pl.pallas_call(
        kernel,
        in_specs=[pl.BlockSpec(memory_space=pltpu.VMEM)] * len(backs),
        out_specs=pl.BlockSpec(memory_space=pltpu.VMEM),
        out_shape=jax.ShapeDtypeStruct((1, tokens, seq * stride), backs[0].dtype),
    )(*backs)


def pieces_kernel(*refs, seq, stride, offset, width, me):
    sources, outs = refs[:3], refs[3:]
    for step in range(seq):
        low = ((me + step) % seq) * stride + offset
        for kind, source in enumerate(sources):
            outs[step][kind] = source[0, :, low:low + width]


def pieces_of(query_rows, key_rows, value_rows, own_index, seq, stride, offset, width):
    tokens = query_rows.shape[1]

    def branch(me, *rows):
        kernel = functools.partial(
            pieces_kernel, seq=seq, stride=stride, offset=offset, width=width, me=me
        )
        return tuple(
            pl.pallas_call(
                kernel,
                in_specs=[pl.BlockSpec(memory_space=pltpu.VMEM)] * 3,
                out_specs=[pl.BlockSpec(memory_space=pltpu.VMEM)] * seq,
                out_shape=[jax.ShapeDtypeStruct((3, tokens, width), query_rows.dtype)] * seq,
            )(*rows)
        )

    branches = [functools.partial(branch, me) for me in range(seq)]
    return lax.switch(own_index, branches, query_rows, key_rows, value_rows)


def attend_pieces_kernel(lists_ref, live_ref, me_ref, *refs, block, slots, qblocks, heads, depth):
    sources = len(refs) // 2
    x_refs, o_refs = refs[:sources], refs[sources:]
    tokens = x_refs[0].shape[1]
    total = sources * tokens
    me = me_ref[0]
    scale = depth ** (-0.5)
    per_source = tokens // block
    column = lax.broadcasted_iota(jnp.int32, (1, total), 1)
    for head in range(heads):
        cols = slice(head * depth, (head + 1) * depth)
        keys = jnp.concatenate([ref[1, :, cols] for ref in x_refs], axis=0)
        values = jnp.concatenate([ref[2, :, cols] for ref in x_refs], axis=0)
        for step in range(sources):
            device = (me - step + sources) % sources
            for sub in range(per_source):
                rows = slice(sub * block, (sub + 1) * block)
                query = x_refs[step][0, rows, cols]
                entry = head * qblocks + device * per_source + sub
                live = live_ref[entry]
                active = column < 0
                for slot in range(slots):
                    chosen = lists_ref[entry * slots + slot]
                    place = (me - chosen // per_source + sources) % sources
                    low = place * tokens + (chosen % per_source) * block
                    active = active | ((column >= low) & (column < low + block) & (slot < live))
                scores = (
                    lax.dot_general(
                        query, keys, (((1,), (1,)), ((), ())), preferred_element_type=jnp.float32
                    )
                    * scale
                )
                scores = jnp.where(active, scores, -jnp.inf)
                highest = jnp.max(scores, axis=1, keepdims=True)
                weights = jnp.exp(scores - highest)
                totals = jnp.sum(weights, axis=1, keepdims=True)
                mixed = jnp.dot(
                    weights.astype(jnp.bfloat16), values, preferred_element_type=jnp.float32
                )
                o_refs[step][rows, cols] = (mixed / totals).astype(o_refs[step].dtype)


def attend_pieces(pieces, lists, live, me):
    _, tokens, width = pieces[0].shape
    head_total, qblocks = live.shape
    slots = lists.shape[2]
    depth = width // head_total
    block = len(pieces) * tokens // qblocks
    kernel = functools.partial(
        attend_pieces_kernel,
        block=block,
        slots=slots,
        qblocks=qblocks,
        heads=head_total,
        depth=depth,
    )
    smem = pltpu.SMEM
    return pl.pallas_call(
        kernel,
        in_specs=[pl.BlockSpec(memory_space=smem)] * 3
        + [pl.BlockSpec(memory_space=pltpu.VMEM)] * len(pieces),
        out_specs=[pl.BlockSpec(memory_space=pltpu.VMEM)] * len(pieces),
        out_shape=[jax.ShapeDtypeStruct((tokens, width), jnp.bfloat16)] * len(pieces),
    )(lists.reshape(-1), live.reshape(-1), me.reshape(1), *pieces)


def place_kernel(*refs, seq, stride, offsets, me):
    out_ref = refs[-1]
    for c, offset in enumerate(offsets):
        for step in range(seq):
            piece = refs[c * seq + step]
            width = piece.shape[1]
            low = ((me + step) % seq) * stride + offset
            out_ref[0, :, low:low + width] = piece[...]


def placed_back(backs, own_index, seq, stride, offsets):
    tokens = backs[0].shape[0]

    def branch(me, *pieces):
        kernel = functools.partial(
            place_kernel, seq=seq, stride=stride, offsets=tuple(offsets), me=me
        )
        return pl.pallas_call(
            kernel,
            in_specs=[pl.BlockSpec(memory_space=pltpu.VMEM)] * len(pieces),
            out_specs=pl.BlockSpec(memory_space=pltpu.VMEM),
            out_shape=jax.ShapeDtypeStruct((1, tokens, seq * stride), pieces[0].dtype),
        )(*pieces)

    branches = [functools.partial(branch, me) for me in range(seq)]
    return lax.switch(own_index, branches, *backs)


def local(
    query_rows,
    key_rows,
    value_rows,
    hidden_state,
    modulation,
    head_weight,
    latents,
    time_index,
    live_counts,
    block_lists,
):
    seq_count = lax.axis_size("seq")
    own_index = lax.axis_index("seq")
    head_count = live_counts.shape[0]
    per_device = head_count // seq_count
    if per_device % 4 == 0:
        sizes = [per_device * 3 // 4, per_device // 4]
    else:
        sizes = [per_device]
    starts = [sum(sizes[:c]) for c in range(len(sizes))]
    tokens = query_rows.shape[1]
    width = query_rows.shape[2]
    depth = width // head_count
    permuted = seq_count <= 8

    source = hidden_state[0].astype(jnp.float32)
    mean_row = jnp.mean(source, axis=1, keepdims=True)
    centred = source - mean_row
    spread = jnp.mean(centred * centred, axis=1, keepdims=True)
    normed = centred * lax.rsqrt(spread + epsilon)
    shaped = (normed * (1.0 + modulation[0, 1]) + modulation[0, 0]).astype(jnp.bfloat16)
    velocity = jnp.dot(shaped, head_weight, preferred_element_type=jnp.float32)
    change = noise_level(time_index[0] - 1) - noise_level(time_index[0])
    moved = latents[0] + change * velocity
    queue_next = None
    backs = []
    previous = None
    for per_chunk, start in zip(sizes, starts):
        chunk_width = per_chunk * depth
        first = own_index * per_device + start
        lists = lax.dynamic_slice_in_dim(block_lists, first, per_chunk, 0)
        live = lax.dynamic_slice_in_dim(live_counts, first, per_chunk, 0)
        if permuted:
            pieces = pieces_of(
                query_rows,
                key_rows,
                value_rows,
                own_index,
                seq_count,
                per_device * depth,
                start * depth,
                chunk_width,
            )
            if previous is not None:
                pieces, _ = lax.optimization_barrier((pieces, previous))
            received = [pieces[0]]
            for step in range(1, seq_count):
                received.append(passed_along(pieces[step], "seq", step))
            if queue_next is None:
                queue_next = passed_along(moved[None], "queue", -1)
                received, queue_next = lax.optimization_barrier((received, queue_next))
            previous = received
            outs = attend_pieces(received, lists, live, own_index.astype(jnp.int32))
            backs.append(outs[0])
            for step in range(1, seq_count):
                backs.append(passed_along(outs[step], "seq", -step))
            continue
        send = packed_chunk(
            query_rows, key_rows, value_rows, seq_count, per_device * depth, start * depth, chunk_width
        )
        if previous is not None:
            send, _ = lax.optimization_barrier((send, previous))
        packed = lax.all_to_all(send, "seq", 0, 0, tiled=True)
        previous = packed
        attended = attend_heads(packed, lists, live, jnp.zeros((), jnp.int32), False)
        backs.append(lax.all_to_all(attended, "seq", 0, 0, tiled=True))
    offsets = [s * depth for s in starts]
    if permuted:
        mixed_back = placed_back(backs, own_index, seq_count, per_device * depth, offsets)
    else:
        mixed_back = unpacked(backs, seq_count, per_device * depth, offsets)

    if queue_next is None:
        queue_next = passed_along(moved[None], "queue", -1)
    return (mixed_back, queue_next)


def solution(mesh):
    placed = (
        P(("groups", "queue"), "seq", None),
        P(("groups", "queue"), "seq", None),
        P(("groups", "queue"), "seq", None),
        P(("groups", "queue"), "seq", None),
        P(("groups", "queue"), None, None),
        P(),
        P(("groups", "queue"), "seq", None),
        P(("groups", "queue")),
        P(),
        P(),
    )
    return jax.shard_map(
        local,
        mesh=mesh,
        in_specs=placed,
        out_specs=(P(("groups", "queue"), "seq", None), P(("groups", "queue"), "seq", None)),
        check_vma=False,
    )
```

```python
import functools

import jax
import jax.numpy as jnp
from jax import lax
from jax.experimental import pallas as pl
from jax.experimental.pallas import tpu as pltpu
from jax.sharding import PartitionSpec as P

STEPS = 8


epsilon = 1e-06
plan_shift = 5.0


def passed_along(value, axis, steps):
    count = lax.axis_size(axis)
    pairs = [(source, (source + steps) % count) for source in range(count)]
    return lax.ppermute(value, axis, pairs)


def noise_level(step_value):
    fraction = step_value.astype(jnp.float32) / STEPS
    return plan_shift * fraction / (1.0 + (plan_shift - 1.0) * fraction)


def attend_kernel(
    lists_ref, live_ref, me_ref, x_ref, o_ref, *, block, slots, qblocks, heads, depth, shifted
):
    sources, _, tokens, _ = x_ref.shape
    me = me_ref[0]

    def slot_of(device):
        if shifted:
            return (me - device + sources) % sources
        return device

    total = sources * tokens
    scale = depth ** (-0.5)
    column = lax.broadcasted_iota(jnp.int32, (1, total), 1)
    per_source = tokens // block
    for head in range(heads):
        cols = slice(head * depth, (head + 1) * depth)
        keys = x_ref[:, 1, :, cols].reshape(total, depth)
        values = x_ref[:, 2, :, cols].reshape(total, depth)

        def body(qblock, carry):
            source = slot_of(qblock // per_source)
            first = pl.multiple_of((qblock % per_source) * block, block)
            query = x_ref[source, 0, pl.ds(first, block), cols]
            scores = (
                lax.dot_general(
                    query, keys, (((1,), (1,)), ((), ())), preferred_element_type=jnp.float32
                )
                * scale
            )
            live = live_ref[head * qblocks + qblock]
            active = column < 0
            for slot in range(slots):
                chosen = lists_ref[(head * qblocks + qblock) * slots + slot]
                place = slot_of(chosen // per_source)
                low = place * tokens + (chosen % per_source) * block
                active = active | ((column >= low) & (column < low + block) & (slot < live))
            scores = jnp.where(active, scores, -jnp.inf)
            highest = jnp.max(scores, axis=1, keepdims=True)
            weights = jnp.exp(scores - highest)
            totals = jnp.sum(weights, axis=1, keepdims=True)
            mixed = jnp.dot(
                weights.astype(jnp.bfloat16), values, preferred_element_type=jnp.float32
            )
            o_ref[source, pl.ds(first, block), cols] = (mixed / totals).astype(o_ref.dtype)
            return carry

        lax.fori_loop(0, qblocks, body, 0)


def attend_heads(packed, lists, live, me, shifted):
    sources, _, tokens, width = packed.shape
    head_total, qblocks = live.shape
    slots = lists.shape[2]
    depth = width // head_total
    block = sources * tokens // qblocks
    kernel = functools.partial(
        attend_kernel,
        block=block,
        slots=slots,
        qblocks=qblocks,
        heads=head_total,
        depth=depth,
        shifted=shifted,
    )
    smem = pltpu.SMEM
    return pl.pallas_call(
        kernel,
        in_specs=[
            pl.BlockSpec(memory_space=smem),
            pl.BlockSpec(memory_space=smem),
            pl.BlockSpec(memory_space=smem),
            pl.BlockSpec(memory_space=pltpu.VMEM),
        ],
        out_specs=pl.BlockSpec(memory_space=pltpu.VMEM),
        out_shape=jax.ShapeDtypeStruct((sources, tokens, width), jnp.bfloat16),
    )(lists.reshape(-1), live.reshape(-1), me.reshape(1), packed)


def pack_kernel(query_ref, key_ref, value_ref, out_ref, *, seq, stride, offset, width):
    for group in range(seq):
        cols = slice(group * stride + offset, group * stride + offset + width)
        for kind, source in enumerate((query_ref, key_ref, value_ref)):
            out_ref[group, kind] = source[0, :, cols]


def packed_chunk(query_rows, key_rows, value_rows, seq, stride, offset, width):
    tokens = query_rows.shape[1]
    kernel = functools.partial(pack_kernel, seq=seq, stride=stride, offset=offset, width=width)
    return pl.pallas_call(
        kernel,
        in_specs=[pl.BlockSpec(memory_space=pltpu.VMEM)] * 3,
        out_specs=pl.BlockSpec(memory_space=pltpu.VMEM),
        out_shape=jax.ShapeDtypeStruct((seq, 3, tokens, width), query_rows.dtype),
    )(query_rows, key_rows, value_rows)


def unpack_kernel(*refs, seq, stride, offsets):
    chunks = len(refs) - 1
    out_ref = refs[chunks]
    for c in range(chunks):
        width = refs[c].shape[2]
        for group in range(seq):
            low = group * stride + offsets[c]
            out_ref[0, :, low:low + width] = refs[c][group]


def unpacked(backs, seq, stride, offsets):
    tokens = backs[0].shape[1]
    kernel = functools.partial(unpack_kernel, seq=seq, stride=stride, offsets=tuple(offsets))
    return pl.pallas_call(
        kernel,
        in_specs=[pl.BlockSpec(memory_space=pltpu.VMEM)] * len(backs),
        out_specs=pl.BlockSpec(memory_space=pltpu.VMEM),
        out_shape=jax.ShapeDtypeStruct((1, tokens, seq * stride), backs[0].dtype),
    )(*backs)


def pieces_kernel(*refs, seq, stride, offset, width, me):
    sources, outs = refs[:3], refs[3:]
    for step in range(seq):
        low = ((me + step) % seq) * stride + offset
        for kind, source in enumerate(sources):
            outs[step][kind] = source[0, :, low:low + width]


def pieces_of(query_rows, key_rows, value_rows, own_index, seq, stride, offset, width):
    tokens = query_rows.shape[1]

    def branch(me, *rows):
        kernel = functools.partial(
            pieces_kernel, seq=seq, stride=stride, offset=offset, width=width, me=me
        )
        return tuple(
            pl.pallas_call(
                kernel,
                in_specs=[pl.BlockSpec(memory_space=pltpu.VMEM)] * 3,
                out_specs=[pl.BlockSpec(memory_space=pltpu.VMEM)] * seq,
                out_shape=[jax.ShapeDtypeStruct((3, tokens, width), query_rows.dtype)] * seq,
            )(*rows)
        )

    branches = [functools.partial(branch, me) for me in range(seq)]
    return lax.switch(own_index, branches, query_rows, key_rows, value_rows)


def attend_pieces_kernel(lists_ref, live_ref, me_ref, *refs, block, slots, qblocks, heads, depth):
    sources = len(refs) // 2
    x_refs, o_refs = refs[:sources], refs[sources:]
    tokens = x_refs[0].shape[1]
    total = sources * tokens
    me = me_ref[0]
    scale = depth ** (-0.5)
    per_source = tokens // block
    column = lax.broadcasted_iota(jnp.int32, (1, total), 1)
    for head in range(heads):
        cols = slice(head * depth, (head + 1) * depth)
        keys = jnp.concatenate([ref[1, :, cols] for ref in x_refs], axis=0)
        values = jnp.concatenate([ref[2, :, cols] for ref in x_refs], axis=0)
        for step in range(sources):
            device = (me - step + sources) % sources
            for sub in range(per_source):
                rows = slice(sub * block, (sub + 1) * block)
                query = x_refs[step][0, rows, cols]
                entry = head * qblocks + device * per_source + sub
                live = live_ref[entry]
                active = column < 0
                for slot in range(slots):
                    chosen = lists_ref[entry * slots + slot]
                    place = (me - chosen // per_source + sources) % sources
                    low = place * tokens + (chosen % per_source) * block
                    active = active | ((column >= low) & (column < low + block) & (slot < live))
                scores = (
                    lax.dot_general(
                        query, keys, (((1,), (1,)), ((), ())), preferred_element_type=jnp.float32
                    )
                    * scale
                )
                scores = jnp.where(active, scores, -jnp.inf)
                highest = jnp.max(scores, axis=1, keepdims=True)
                weights = jnp.exp(scores - highest)
                totals = jnp.sum(weights, axis=1, keepdims=True)
                mixed = jnp.dot(
                    weights.astype(jnp.bfloat16), values, preferred_element_type=jnp.float32
                )
                o_refs[step][rows, cols] = (mixed / totals).astype(o_refs[step].dtype)


def attend_pieces(pieces, lists, live, me):
    _, tokens, width = pieces[0].shape
    head_total, qblocks = live.shape
    slots = lists.shape[2]
    depth = width // head_total
    block = len(pieces) * tokens // qblocks
    kernel = functools.partial(
        attend_pieces_kernel,
        block=block,
        slots=slots,
        qblocks=qblocks,
        heads=head_total,
        depth=depth,
    )
    smem = pltpu.SMEM
    return pl.pallas_call(
        kernel,
        in_specs=[pl.BlockSpec(memory_space=smem)] * 3
        + [pl.BlockSpec(memory_space=pltpu.VMEM)] * len(pieces),
        out_specs=[pl.BlockSpec(memory_space=pltpu.VMEM)] * len(pieces),
        out_shape=[jax.ShapeDtypeStruct((tokens, width), jnp.bfloat16)] * len(pieces),
    )(lists.reshape(-1), live.reshape(-1), me.reshape(1), *pieces)


def place_kernel(*refs, seq, stride, offsets, me):
    out_ref = refs[-1]
    for c, offset in enumerate(offsets):
        for step in range(seq):
            piece = refs[c * seq + step]
            width = piece.shape[1]
            low = ((me + step) % seq) * stride + offset
            out_ref[0, :, low:low + width] = piece[...]


def placed_back(backs, own_index, seq, stride, offsets):
    tokens = backs[0].shape[0]

    def branch(me, *pieces):
        kernel = functools.partial(
            place_kernel, seq=seq, stride=stride, offsets=tuple(offsets), me=me
        )
        return pl.pallas_call(
            kernel,
            in_specs=[pl.BlockSpec(memory_space=pltpu.VMEM)] * len(pieces),
            out_specs=pl.BlockSpec(memory_space=pltpu.VMEM),
            out_shape=jax.ShapeDtypeStruct((1, tokens, seq * stride), pieces[0].dtype),
        )(*pieces)

    branches = [functools.partial(branch, me) for me in range(seq)]
    return lax.switch(own_index, branches, *backs)


def local(
    query_rows,
    key_rows,
    value_rows,
    hidden_state,
    modulation,
    head_weight,
    latents,
    time_index,
    live_counts,
    block_lists,
):
    seq_count = lax.axis_size("seq")
    own_index = lax.axis_index("seq")
    head_count = live_counts.shape[0]
    per_device = head_count // seq_count
    if per_device % 4 == 0:
        sizes = [per_device * 3 // 4, per_device // 4]
    else:
        sizes = [per_device]
    starts = [sum(sizes[:c]) for c in range(len(sizes))]
    tokens = query_rows.shape[1]
    width = query_rows.shape[2]
    depth = width // head_count
    permuted = seq_count <= 8

    source = hidden_state[0].astype(jnp.float32)
    mean_row = jnp.mean(source, axis=1, keepdims=True)
    centred = source - mean_row
    spread = jnp.mean(centred * centred, axis=1, keepdims=True)
    normed = centred * lax.rsqrt(spread + epsilon)
    shaped = (normed * (1.0 + modulation[0, 1]) + modulation[0, 0]).astype(jnp.bfloat16)
    velocity = jnp.dot(shaped, head_weight, preferred_element_type=jnp.float32)
    change = noise_level(time_index[0] - 1) - noise_level(time_index[0])
    moved = latents[0] + change * velocity
    queue_next = None
    backs = []
    previous = None
    for per_chunk, start in zip(sizes, starts):
        chunk_width = per_chunk * depth
        first = own_index * per_device + start
        lists = lax.dynamic_slice_in_dim(block_lists, first, per_chunk, 0)
        live = lax.dynamic_slice_in_dim(live_counts, first, per_chunk, 0)
        if permuted:
            pieces = pieces_of(
                query_rows,
                key_rows,
                value_rows,
                own_index,
                seq_count,
                per_device * depth,
                start * depth,
                chunk_width,
            )
            if previous is not None:
                pieces, _ = lax.optimization_barrier((pieces, previous))
            received = [pieces[0]]
            for step in range(1, seq_count):
                received.append(passed_along(pieces[step], "seq", step))
            previous = received
            outs = attend_pieces(received, lists, live, own_index.astype(jnp.int32))
            if queue_next is None:
                queue_next = passed_along(moved[None], "queue", -1)
                outs, queue_next = lax.optimization_barrier((tuple(outs), queue_next))
            backs.append(outs[0])
            for step in range(1, seq_count):
                backs.append(passed_along(outs[step], "seq", -step))
            continue
        send = packed_chunk(
            query_rows, key_rows, value_rows, seq_count, per_device * depth, start * depth, chunk_width
        )
        if previous is not None:
            send, _ = lax.optimization_barrier((send, previous))
        packed = lax.all_to_all(send, "seq", 0, 0, tiled=True)
        previous = packed
        attended = attend_heads(packed, lists, live, jnp.zeros((), jnp.int32), False)
        backs.append(lax.all_to_all(attended, "seq", 0, 0, tiled=True))
    offsets = [s * depth for s in starts]
    if permuted:
        mixed_back = placed_back(backs, own_index, seq_count, per_device * depth, offsets)
    else:
        mixed_back = unpacked(backs, seq_count, per_device * depth, offsets)

    if queue_next is None:
        queue_next = passed_along(moved[None], "queue", -1)
    return (mixed_back, queue_next)


def solution(mesh):
    placed = (
        P(("groups", "queue"), "seq", None),
        P(("groups", "queue"), "seq", None),
        P(("groups", "queue"), "seq", None),
        P(("groups", "queue"), "seq", None),
        P(("groups", "queue"), None, None),
        P(),
        P(("groups", "queue"), "seq", None),
        P(("groups", "queue")),
        P(),
        P(),
    )
    return jax.shard_map(
        local,
        mesh=mesh,
        in_specs=placed,
        out_specs=(P(("groups", "queue"), "seq", None), P(("groups", "queue"), "seq", None)),
        check_vma=False,
    )
```
